32 devices in a mesh: dom: 2 (over y), blk: 16 (over z, x, core).
Axes of the slice: x: 2, y: 2, z: 4, core: 2. Of those that a mesh axis runs over, the one named last changes fastest.
Arguments:
- right_side: float32 [2, 4, 2, 8192], P(None, None, 'dom', 'blk')
- near_blocks: bfloat16 [2, 32, 4, 2, 256, 256], P('dom', 'blk'), may hold values from -0.125 to 0.125
- near_cols: int32 [2, 32, 4], P('dom', 'blk'), may hold values from 0 to 5
- partner: int32 [2, 32], P('dom', 'blk'), may hold values from 0 to 3, as said below
- source_basis: bfloat16 [2, 2, 64, 8192], P('dom', None, None, 'blk'), may hold values from -0.25 to 0.25
- target_basis: bfloat16 [2, 2, 64, 8192], P('dom', None, None, 'blk'), may hold values from -0.75 to 0.75
- coupling: float32 [2, 16, 16, 2, 64, 64], P('dom', 'blk'), as said below
- far_ranks: int32 [2, 16, 16], P('dom', 'blk'), may hold values from 32 to 64, as said below
Outputs:
- second_basis: float32 [2, 4, 2, 8192], P(None, None, 'dom', 'blk')
- third_basis: float32 [2, 4, 2, 8192], P(None, None, 'dom', 'blk')
- hessenberg: float32 [4, 9], replicated
The draws below stay inside these ranges and needn't reach their ends.
Inputs may be any that keep to these rules, and one draw needn't show every extreme that they name: partner[d, c * 2 + i] = e * 2 + j names block j of cluster c in subdomain e; the named block names the first one back, and no block names itself. coupling[d, c, s, a, k, l] equals coupling[d, s, c, a, l, k]. far_ranks[d, c, s] equals far_ranks[d, s, c].
All inputs are finite; a program needn't handle non-finite values.
Results may differ from the reference program's by a relative error of at most 0.0065.
Values may be sent and summed in bfloat16 or wider, within the bound.
No kernel may reach another device: no remote copies, remote signals or barrier semaphores. Data moves between devices by JAX's collectives and lax.ppermute only.
A program may use at most 64 MiB of HBM per device.

```python
import math
import jax
import jax.numpy as jnp
from jax import lax

RB = 2
BS = 256
KN = 4
K = 64
RHS = 4
NDOM = 2
NCL = 16
R = 512
NBT = 32
NT = 8192


def draw_right_side(key, part):
    position = (jnp.arange(NDOM * NT, dtype=jnp.float32) / (NDOM * NT)).reshape(NDOM, NT)
    values = jax.random.truncated_normal(key, -4.0, 4.0, (2, RHS, NDOM, NT), jnp.float32)
    ramp = 1.0 + 2.0 * position
    return values * ramp


def draw_partner(key, part):
    slots = NDOM * RB
    keys = jax.random.split(key, NCL)
    orders = jax.vmap(lambda single: jax.random.permutation(single, slots))(keys).astype(jnp.int32)
    mates = orders.reshape(NCL, slots // 2, 2)[:, :, ::-1].reshape(NCL, slots)

    def place(order, mate):
        return jnp.zeros((slots,), jnp.int32).at[order].set(mate)
    table = jax.vmap(place)(orders, mates)
    return table.reshape(NCL, NDOM, RB).transpose(1, 0, 2).reshape(NDOM, NCL * RB).astype(jnp.int32)


def draw_coupling(key, part):
    shape = (NDOM, NCL, NCL, 2, K, K)
    raw = jax.random.normal(key, shape, jnp.float32)
    paired = (raw + raw.transpose(0, 2, 1, 3, 5, 4)) / math.sqrt(2.0)
    return paired / math.sqrt(NCL * K)


def draw_far_ranks(key, part):
    raw = jax.random.randint(key, (NDOM, NCL, NCL), K // 2, K + 1, jnp.int32)
    paired = jnp.minimum(raw, raw.transpose(0, 2, 1))
    diagonal = jnp.arange(NCL)[:, None] == jnp.arange(NCL)[None, :]
    return jnp.where(diagonal[None], K, paired).astype(jnp.int32)


def with_ends(entries, stream_key, smallest, top_value):
    index_at = [jax.random.randint(jax.random.fold_in(stream_key, axis), (), 0, length) for axis, length in enumerate(entries.shape)]
    widest = entries.shape.index(max(entries.shape))
    next_to = index_at[:widest] + [(index_at[widest] + 1) % entries.shape[widest]] + index_at[widest + 1:]
    return entries.at[tuple(index_at)].set(smallest).at[tuple(next_to)].set(top_value)


def block_levels(stream_key, shape, cuts, smallest, high):
    level, own = 1.0, jax.random.fold_in(stream_key, 6)
    for axis_at, shards_of in cuts:
        heights = jnp.exp(jax.random.uniform(jax.random.fold_in(own, axis_at), (shards_of,), jnp.float32, smallest / len(cuts), high / len(cuts)))
        level = level * jnp.repeat(heights, shape[axis_at] // shards_of).reshape([-1 if axis == axis_at else 1 for axis in range(len(shape))])
    return level


def scatter_about(key, extent, width, reach, cuts=(), kind=jnp.bfloat16):
    drawn = width * jax.random.normal(key, extent, jnp.float32)
    if cuts:
        drawn = drawn * block_levels(key, extent, cuts, -0.22, 0.18)
    return jnp.clip(drawn, -reach, reach).astype(kind)


def setup_inputs(seed: int = 0) -> dict:
    arg_keys = jax.random.split(jax.random.key(seed), 9)
    right_side = draw_right_side(jax.random.fold_in(arg_keys[8], 71), 0)
    near_blocks = scatter_about(arg_keys[1], (NDOM, NBT, KN, 2, BS, BS), (2 * KN * BS) ** -0.5, 0.125, ((0, 2), (1, 16)))
    near_cols = with_ends(jax.random.randint(arg_keys[2], (NDOM, NBT, KN), 0, 3 * RB), jax.random.fold_in(arg_keys[2], 1), 0, (3 * RB) - 1).astype(jnp.int32)
    partner = draw_partner(jax.random.fold_in(arg_keys[8], 71), 0)
    source_basis = scatter_about(arg_keys[4], (NDOM, 2, K, NT), R ** -0.5, 0.25, ((0, 2), (3, 16)))
    target_basis = scatter_about(arg_keys[5], (NDOM, 2, K, NT), K ** -0.5, 0.75, ((0, 2), (3, 16)))
    coupling = draw_coupling(jax.random.fold_in(arg_keys[8], 71), 0)
    far_ranks = draw_far_ranks(jax.random.fold_in(arg_keys[8], 71), 0)
    return {"right_side": right_side, "near_blocks": near_blocks, "near_cols": near_cols, "partner": partner, "source_basis": source_basis, "target_basis": target_basis, "coupling": coupling, "far_ranks": far_ranks}


EPSILON = 1e-06

def complex_mix(products):
    return jnp.stack([products[0, 0] - products[1, 1], products[0, 1] + products[1, 0]])

def apply_operator(vector, near_blocks, near_cols, partner, source_basis, target_basis, coupling, far_ranks):
    rounded = lax.optimization_barrier(vector.astype(jnp.bfloat16))
    padded = jnp.pad(rounded, ((0, 0), (0, 0), (0, 0), (R, R)))
    tiles = padded.reshape(2, RHS, NDOM, NBT + 2 * RB, BS)
    offsets = (jnp.arange(NBT, dtype=jnp.int32) // RB * RB)[:, None]

    def near_domain(domain):
        index = (offsets + near_cols[domain]).astype(jnp.int32)
        chosen = jnp.take(tiles[:, :, domain], index, axis=2)
        products = jnp.einsum('ikarc,pqikc->apqir', near_blocks[domain].astype(jnp.float32), chosen.astype(jnp.float32))
        return complex_mix(products)
    near_part = lax.map(near_domain, jnp.arange(NDOM, dtype=jnp.int32))
    near_part = near_part.transpose(1, 2, 0, 3, 4).reshape(2, RHS, NDOM, NT)
    local = rounded.reshape(2, RHS, NDOM, NCL, R).astype(jnp.float32)
    sources = source_basis.reshape(NDOM, 2, K, NCL, R).astype(jnp.float32)
    products = jnp.einsum('dakcr,pqdcr->apqdck', sources, local)
    coeffs = jnp.stack([products[0, 0] + products[1, 1], products[0, 1] - products[1, 0]])
    levels = jnp.arange(K, dtype=jnp.int32)

    def far_domain(domain):
        rank_now = far_ranks[domain][:, :, None, None]
        keep = (levels[:, None] < rank_now) & (levels[None, :] < rank_now)
        masked = coupling[domain] * keep[:, :, None].astype(coupling.dtype)
        inner = jnp.einsum('csakl,pqsl->apqck', masked, coeffs[:, :, domain], precision=lax.Precision.HIGHEST)
        return complex_mix(inner)
    far_coef = lax.map(far_domain, jnp.arange(NDOM, dtype=jnp.int32))
    rounded_coef = lax.optimization_barrier(far_coef.astype(jnp.bfloat16)).astype(jnp.float32)
    targets = target_basis.reshape(NDOM, 2, K, NCL, R).astype(jnp.float32)
    outward = jnp.einsum('dakcr,dpqck->apqdcr', targets, rounded_coef)
    far_part = complex_mix(outward).reshape(2, RHS, NDOM, NT)
    grid = vector.reshape(2, RHS, NDOM, NCL, RB, BS)
    mate = partner.reshape(NDOM, NCL, RB)
    mate_domain = mate // RB
    mate_block = mate % RB
    cluster = jnp.arange(NCL, dtype=jnp.int32)[None, :, None]
    mates = grid[:, :, mate_domain, cluster, mate_block].reshape(2, RHS, NDOM, NT)
    return vector + near_part + far_part - mates

def inner(first, second):
    total = NDOM * NT
    real_part = lax.optimization_barrier(jnp.sum(first[0] * second[0] + first[1] * second[1], axis=(1, 2))) / total
    imag_part = lax.optimization_barrier(jnp.sum(first[0] * second[1] - first[1] * second[0], axis=(1, 2))) / total
    return jnp.stack([real_part, imag_part])

def squares(field):
    return lax.optimization_barrier(jnp.sum(field[0] * field[0] + field[1] * field[1], axis=(1, 2))) / (NDOM * NT)

def scaled(factor, field):
    real_f = factor[0][:, None, None]
    imag_f = factor[1][:, None, None]
    return jnp.stack([real_f * field[0] - imag_f * field[1], real_f * field[1] + imag_f * field[0]])

def reference(right_side, near_blocks, near_cols, partner, source_basis, target_basis, coupling, far_ranks):

    def operator(field):
        return apply_operator(field, near_blocks, near_cols, partner, source_basis, target_basis, coupling, far_ranks)
    beta = jnp.sqrt(squares(right_side) + EPSILON)
    first_vec = right_side / beta[None, :, None, None]
    image_one = operator(first_vec)
    h_one_one = inner(first_vec, image_one)
    rest_one = image_one - scaled(h_one_one, first_vec)
    h_two_one = jnp.sqrt(squares(rest_one) + EPSILON)
    second_basis = rest_one / h_two_one[None, :, None, None]
    image_two = operator(second_basis)
    h_one_two = inner(first_vec, image_two)
    h_two_two = inner(second_basis, image_two)
    rest_two = image_two - scaled(h_one_two, first_vec) - scaled(h_two_two, second_basis)
    h_three_two = jnp.sqrt(squares(rest_two) + EPSILON)
    third_basis = rest_two / h_three_two[None, :, None, None]
    hessenberg = jnp.stack([beta, h_one_one[0], h_one_one[1], h_two_one, h_one_two[0], h_one_two[1], h_two_two[0], h_two_two[1], h_three_two], axis=1)
    return (second_basis, third_basis, hessenberg)
```

```python
import jax
import jax.numpy as jnp
from jax import lax
from jax.sharding import PartitionSpec as P

EPSILON = 1e-06


def _pow2(n):
    return n > 0 and (n & (n - 1)) == 0


def tree_sum(x, axes):
    for axis in axes:
        n = lax.axis_size(axis)
        if not _pow2(n):
            x = lax.psum(x, axis)
            continue
        k = 1
        while k < n:
            x = x + lax.ppermute(x, axis, [(i, i ^ k) for i in range(n)])
            k *= 2
    return x


def tree_gather(x, axis):
    n = lax.axis_size(axis)
    if not _pow2(n):
        return lax.all_gather(x, axis, axis=0)
    idx = lax.axis_index(axis)
    buf = x[None]
    k = 1
    while k < n:
        other = lax.ppermute(buf, axis, [(i, i ^ k) for i in range(n)])
        low = (idx // k) % 2 == 0
        buf = jnp.where(low, jnp.concatenate([buf, other]), jnp.concatenate([other, buf]))
        k *= 2
    return buf


def extended(cells, sides, width):
    for axis, dim in sides:
        count = lax.axis_size(axis)
        ends = count - 1
        head = lax.slice_in_dim(cells, 0, width, axis=dim)
        tail = lax.slice_in_dim(cells, cells.shape[dim] - width, cells.shape[dim], axis=dim)
        cells = jnp.concatenate(
            [
                lax.ppermute(tail, axis, [(i, (i + 1) % count) for i in range(ends)]),
                cells,
                lax.ppermute(head, axis, [((i + 1) % count, i) for i in range(ends)]),
            ],
            axis=dim,
        )
    return cells


def complex_mix(products):
    return jnp.stack([products[0, 0] - products[1, 1], products[0, 1] + products[1, 0]])


def apply_operator(
    vector, near_blocks, near_cols, partner, source_basis, target_basis, coupling, far_ranks
):
    nrhs = vector.shape[1]
    rows = vector.shape[3]
    blocks_dev = near_blocks.shape[1]
    slots = near_blocks.shape[2]
    width = near_blocks.shape[4]
    rank_cap = source_basis.shape[2]
    rounded = vector.astype(jnp.bfloat16)
    window = extended(rounded, (("blk", 3),), rows)
    window = window.reshape(2, nrhs, 3 * blocks_dev, width)
    chosen = jnp.take(window, near_cols[0].reshape(-1), axis=2).reshape(
        2, nrhs, blocks_dev, slots, width
    )
    near_prod = jnp.einsum(
        "ikarc,pqikc->apqir", near_blocks[0], chosen, preferred_element_type=jnp.float32
    )
    near_part = complex_mix(near_prod).reshape(2, nrhs, 1, rows)
    coef_prod = jnp.einsum(
        "akr,pqr->apqk", source_basis[0], rounded[:, :, 0], preferred_element_type=jnp.float32
    )
    coeffs = jnp.stack([coef_prod[0, 0] + coef_prod[1, 1], coef_prod[0, 1] - coef_prod[1, 0]])
    row_coupling = coupling[0, 0]
    row_ranks = far_ranks[0, 0]
    levels = jnp.arange(rank_cap, dtype=jnp.int32)
    limit = row_ranks[:, None, None]
    keep = (levels[None, :, None] < limit) & (levels[None, None, :] < limit)
    weights = row_coupling * keep[:, None].astype(jnp.float32)
    inner = jnp.einsum(
        "sakl,spql->apqk",
        weights,
        tree_gather(coeffs, "blk"),
        precision=lax.Precision.HIGHEST,
    )
    far_coef = complex_mix(inner)
    rounded_coef = far_coef.astype(jnp.bfloat16)
    outward = jnp.einsum(
        "akr,pqk->apqr", target_basis[0], rounded_coef, preferred_element_type=jnp.float32
    )
    far_part = complex_mix(outward).reshape(2, nrhs, 1, rows)
    every = jnp.moveaxis(tree_gather(vector[:, :, 0], "dom"), 0, 2)
    every = every.reshape(2, nrhs, -1, width)
    mates = jnp.take(every, partner[0], axis=2).reshape(2, nrhs, 1, rows)
    return vector + near_part + far_part - mates


def local_products(vectors, image):
    stacked = []
    for basis in vectors:
        real_part = jnp.sum(basis[0] * image[0] + basis[1] * image[1], axis=(1, 2))
        imag_part = jnp.sum(basis[0] * image[1] - basis[1] * image[0], axis=(1, 2))
        stacked.append(jnp.stack([real_part, imag_part]))
    return jnp.stack(stacked)


def local_squares(field):
    return jnp.sum(field[0] * field[0] + field[1] * field[1], axis=(1, 2))


def scaled(factor, field):
    real_f = factor[0][:, None, None]
    imag_f = factor[1][:, None, None]
    return jnp.stack([real_f * field[0] - imag_f * field[1], real_f * field[1] + imag_f * field[0]])


def shards(
    right_side, near_blocks, near_cols, partner, source_basis, target_basis, coupling, far_ranks
):
    rows = right_side.shape[3]
    total = float(rows * lax.axis_size("dom") * lax.axis_size("blk"))
    everyone = ("dom", "blk")

    def operator(field):
        return apply_operator(
            field, near_blocks, near_cols, partner, source_basis, target_basis, coupling, far_ranks
        )

    start_sum = tree_sum(local_squares(right_side), everyone)
    beta = jnp.sqrt(start_sum / total + EPSILON)
    first_vec = right_side / beta[None, :, None, None]
    image_one = operator(first_vec)

    def projections(vectors, image):
        return tree_sum(local_products(vectors, image), everyone) / total

    def lengths(field):
        return tree_sum(local_squares(field), everyone) / total

    h_one_one = projections([first_vec], image_one)[0]
    rest_one = image_one - scaled(h_one_one, first_vec)
    h_two_one = jnp.sqrt(lengths(rest_one) + EPSILON)
    second_basis = rest_one / h_two_one[None, :, None, None]
    image_two = operator(second_basis)
    both = projections([first_vec, second_basis], image_two)
    h_one_two = both[0]
    h_two_two = both[1]
    rest_two = image_two - scaled(h_one_two, first_vec) - scaled(h_two_two, second_basis)
    h_three_two = jnp.sqrt(lengths(rest_two) + EPSILON)
    third_basis = rest_two / h_three_two[None, :, None, None]
    hessenberg = jnp.stack(
        [
            beta,
            h_one_one[0],
            h_one_one[1],
            h_two_one,
            h_one_two[0],
            h_one_two[1],
            h_two_two[0],
            h_two_two[1],
            h_three_two,
        ],
        axis=1,
    )
    return (second_basis, third_basis, hessenberg)


def solution(mesh):
    return jax.shard_map(
        shards,
        mesh=mesh,
        in_specs=(
            P(None, None, "dom", "blk"),
            P("dom", "blk", None, None, None, None),
            P("dom", "blk", None),
            P("dom", "blk"),
            P("dom", None, None, "blk"),
            P("dom", None, None, "blk"),
            P("dom", "blk", None, None, None, None),
            P("dom", "blk", None),
        ),
        out_specs=(P(None, None, "dom", "blk"), P(None, None, "dom", "blk"), P()),
        check_vma=False,
    )
```

```python
import jax
import jax.numpy as jnp
from jax import lax
from jax.sharding import PartitionSpec as P

EPSILON = 1e-06


def _pow2(n):
    return n > 0 and (n & (n - 1)) == 0


def tree_sum(x, axes):
    for axis in axes:
        n = lax.axis_size(axis)
        if not _pow2(n):
            x = lax.psum(x, axis)
            continue
        k = 1
        while k < n:
            x = x + lax.ppermute(x, axis, [(i, i ^ k) for i in range(n)])
            k *= 2
    return x


def tree_gather(x, axis):
    n = lax.axis_size(axis)
    if not _pow2(n):
        return lax.all_gather(x, axis, axis=0)
    idx = lax.axis_index(axis)
    buf = x[None]
    k = 1
    while k < n:
        other = lax.ppermute(buf, axis, [(i, i ^ k) for i in range(n)])
        low = (idx // k) % 2 == 0
        buf = jnp.where(low, jnp.concatenate([buf, other]), jnp.concatenate([other, buf]))
        k *= 2
    return buf


def extended(cells, sides, width):
    for axis, dim in sides:
        count = lax.axis_size(axis)
        ends = count - 1
        head = lax.slice_in_dim(cells, 0, width, axis=dim)
        tail = lax.slice_in_dim(cells, cells.shape[dim] - width, cells.shape[dim], axis=dim)
        cells = jnp.concatenate(
            [
                lax.ppermute(tail, axis, [(i, (i + 1) % count) for i in range(ends)]),
                cells,
                lax.ppermute(head, axis, [((i + 1) % count, i) for i in range(ends)]),
            ],
            axis=dim,
        )
    return cells


def complex_mix(products):
    return jnp.stack([products[0, 0] - products[1, 1], products[0, 1] + products[1, 0]])


def apply_operator(
    vector, near_blocks, near_cols, partner, source_basis, target_basis, coupling, far_ranks
):
    nrhs = vector.shape[1]
    rows = vector.shape[3]
    blocks_dev = near_blocks.shape[1]
    slots = near_blocks.shape[2]
    width = near_blocks.shape[4]
    rank_cap = source_basis.shape[2]
    rounded = vector.astype(jnp.bfloat16)
    window = extended(rounded, (("blk", 3),), rows)
    window = window.reshape(2, nrhs, 3 * blocks_dev, width)
    chosen = jnp.take(window, near_cols[0].reshape(-1), axis=2).reshape(
        2, nrhs, blocks_dev, slots, width
    )
    near_prod = jnp.einsum(
        "ikarc,pqikc->apqir", near_blocks[0], chosen, preferred_element_type=jnp.float32
    )
    near_part = complex_mix(near_prod).reshape(2, nrhs, 1, rows)
    coef_prod = jnp.einsum(
        "akr,pqr->apqk", source_basis[0], rounded[:, :, 0], preferred_element_type=jnp.float32
    )
    coeffs = jnp.stack([coef_prod[0, 0] + coef_prod[1, 1], coef_prod[0, 1] - coef_prod[1, 0]])
    row_coupling = coupling[0, 0]
    row_ranks = far_ranks[0, 0]
    levels = jnp.arange(rank_cap, dtype=jnp.int32)
    limit = row_ranks[:, None, None]
    keep = (levels[None, :, None] < limit) & (levels[None, None, :] < limit)
    weights = row_coupling * keep[:, None].astype(jnp.float32)
    inner = jnp.einsum(
        "sakl,spql->apqk",
        weights,
        tree_gather(coeffs, "blk"),
        precision=lax.Precision.HIGHEST,
    )
    far_coef = complex_mix(inner)
    rounded_coef = far_coef.astype(jnp.bfloat16)
    outward = jnp.einsum(
        "akr,pqk->apqr", target_basis[0], rounded_coef, preferred_element_type=jnp.float32
    )
    far_part = complex_mix(outward).reshape(2, nrhs, 1, rows)
    every = jnp.moveaxis(tree_gather(vector[:, :, 0], "dom"), 0, 2)
    every = every.reshape(2, nrhs, -1, width)
    mates = jnp.take(every, partner[0], axis=2).reshape(2, nrhs, 1, rows)
    return vector + near_part + far_part - mates


def local_products(vectors, image):
    stacked = []
    for basis in vectors:
        real_part = jnp.sum(basis[0] * image[0] + basis[1] * image[1], axis=(1, 2))
        imag_part = jnp.sum(basis[0] * image[1] - basis[1] * image[0], axis=(1, 2))
        stacked.append(jnp.stack([real_part, imag_part]))
    return jnp.stack(stacked)


def local_squares(field):
    return jnp.sum(field[0] * field[0] + field[1] * field[1], axis=(1, 2))


def scaled(factor, field):
    real_f = factor[0][:, None, None]
    imag_f = factor[1][:, None, None]
    return jnp.stack([real_f * field[0] - imag_f * field[1], real_f * field[1] + imag_f * field[0]])


def shards(
    right_side, near_blocks, near_cols, partner, source_basis, target_basis, coupling, far_ranks
):
    rows = right_side.shape[3]
    total = float(rows * lax.axis_size("dom") * lax.axis_size("blk"))
    everyone = ("dom", "blk")

    def operator(field):
        return apply_operator(
            field, near_blocks, near_cols, partner, source_basis, target_basis, coupling, far_ranks
        )

    start_sum = tree_sum(local_squares(right_side), everyone)
    beta = jnp.sqrt(start_sum / total + EPSILON)
    first_vec = right_side / beta[None, :, None, None]
    image_one = operator(first_vec)

    def reduced(parts):
        return tree_sum(jnp.concatenate(parts), everyone) / total

    def self_products(field):
        return local_squares(field)[None]

    one = reduced(
        [
            local_products([first_vec], image_one)[0],
            self_products(image_one),
            self_products(first_vec),
        ]
    )
    h_one_one = one[0:2]
    sq_w1 = one[2]
    sq_v1 = one[3]
    norm_h11 = h_one_one[0] * h_one_one[0] + h_one_one[1] * h_one_one[1]
    sq_u1 = jnp.maximum(sq_w1 - norm_h11 * (2.0 - sq_v1), 0.0)
    rest_one = image_one - scaled(h_one_one, first_vec)
    h_two_one = jnp.sqrt(sq_u1 + EPSILON)
    second_basis = rest_one / h_two_one[None, :, None, None]
    image_two = operator(second_basis)
    two = reduced(
        [
            local_products([first_vec, second_basis], image_two).reshape(4, -1),
            local_products([first_vec], second_basis)[0],
            self_products(image_two),
            self_products(second_basis),
        ]
    )
    h_one_two = two[0:2]
    h_two_two = two[2:4]
    cross = two[4:6]
    sq_w2 = two[6]
    sq_v2 = two[7]
    norm_a = h_one_two[0] * h_one_two[0] + h_one_two[1] * h_one_two[1]
    norm_b = h_two_two[0] * h_two_two[0] + h_two_two[1] * h_two_two[1]
    ab_re = h_one_two[0] * h_two_two[0] + h_one_two[1] * h_two_two[1]
    ab_im = h_one_two[0] * h_two_two[1] - h_one_two[1] * h_two_two[0]
    mixed = ab_re * cross[0] - ab_im * cross[1]
    sq_u2 = sq_w2 - norm_a * (2.0 - sq_v1) - norm_b * (2.0 - sq_v2) + 2.0 * mixed
    sq_u2 = jnp.maximum(sq_u2, 0.0)
    rest_two = image_two - scaled(h_one_two, first_vec) - scaled(h_two_two, second_basis)
    h_three_two = jnp.sqrt(sq_u2 + EPSILON)
    third_basis = rest_two / h_three_two[None, :, None, None]
    hessenberg = jnp.stack(
        [
            beta,
            h_one_one[0],
            h_one_one[1],
            h_two_one,
            h_one_two[0],
            h_one_two[1],
            h_two_two[0],
            h_two_two[1],
            h_three_two,
        ],
        axis=1,
    )
    return (second_basis, third_basis, hessenberg)


def solution(mesh):
    return jax.shard_map(
        shards,
        mesh=mesh,
        in_specs=(
            P(None, None, "dom", "blk"),
            P("dom", "blk", None, None, None, None),
            P("dom", "blk", None),
            P("dom", "blk"),
            P("dom", None, None, "blk"),
            P("dom", None, None, "blk"),
            P("dom", "blk", None, None, None, None),
            P("dom", "blk", None),
        ),
        out_specs=(P(None, None, "dom", "blk"), P(None, None, "dom", "blk"), P()),
        check_vma=False,
    )
```

```python
import jax
import jax.numpy as jnp
from jax import lax
from jax.sharding import PartitionSpec as P

EPSILON = 1e-06


def _pow2(n):
    return n > 0 and (n & (n - 1)) == 0


def tree_sum(x, axes):
    for axis in axes:
        n = lax.axis_size(axis)
        if not _pow2(n):
            x = lax.psum(x, axis)
            continue
        k = 1
        while k < n:
            x = x + lax.ppermute(x, axis, [(i, i ^ k) for i in range(n)])
            k *= 2
    return x


def tree_collect(red, gat_blk, gat_dom):
    for axis, gat in (("blk", gat_blk), ("dom", gat_dom)):
        n = lax.axis_size(axis)
        if not _pow2(n):
            red = lax.psum(red, axis)
            buf = lax.all_gather(gat, axis, axis=0)
        else:
            idx = lax.axis_index(axis)
            buf = gat[None]
            k = 1
            while k < n:
                packed = jnp.concatenate([red.reshape(-1), buf.reshape(-1)])
                got = lax.ppermute(packed, axis, [(i, i ^ k) for i in range(n)])
                red = red + got[: red.size].reshape(red.shape)
                other = got[red.size :].reshape(buf.shape)
                low = (idx // k) % 2 == 0
                buf = jnp.where(low, jnp.concatenate([buf, other]), jnp.concatenate([other, buf]))
                k *= 2
        if axis == "blk":
            gat_blk = buf
        else:
            gat_dom = buf
    return red, gat_blk, gat_dom


def neighbours(field):
    count = lax.axis_size("blk")
    ends = count - 1
    left = lax.ppermute(field, "blk", [(i, i + 1) for i in range(ends)])
    right = lax.ppermute(field, "blk", [(i + 1, i) for i in range(ends)])
    return jnp.concatenate([left, field, right], axis=3)


def complex_mix(products):
    return jnp.stack([products[0, 0] - products[1, 1], products[0, 1] + products[1, 0]])


def coefficients(field, source_basis):
    rounded = field.astype(jnp.bfloat16)
    coef_prod = jnp.einsum(
        "akr,pqr->apqk", source_basis[0], rounded[:, :, 0], preferred_element_type=jnp.float32
    )
    return jnp.stack([coef_prod[0, 0] + coef_prod[1, 1], coef_prod[0, 1] - coef_prod[1, 0]])


def near_field(window, near_blocks, near_cols):
    nrhs = window.shape[1]
    blocks_dev = near_blocks.shape[1]
    slots = near_blocks.shape[2]
    width = near_blocks.shape[4]
    rounded = window.astype(jnp.bfloat16).reshape(2, nrhs, 3 * blocks_dev, width)
    chosen = jnp.take(rounded, near_cols[0].reshape(-1), axis=2).reshape(
        2, nrhs, blocks_dev, slots, width
    )
    near_prod = jnp.einsum(
        "ikarc,pqikc->apqir", near_blocks[0], chosen, preferred_element_type=jnp.float32
    )
    return complex_mix(near_prod).reshape(2, nrhs, 1, blocks_dev * width)


def far_weights(coupling, far_ranks, rank_cap):
    row_coupling = coupling[0, 0]
    row_ranks = far_ranks[0, 0]
    levels = jnp.arange(rank_cap, dtype=jnp.int32)
    limit = row_ranks[:, None, None]
    keep = (levels[None, :, None] < limit) & (levels[None, None, :] < limit)
    return row_coupling * keep[:, None].astype(jnp.float32)


def far_field(gathered, weights, target_basis):
    nrhs = gathered.shape[2]
    rows = target_basis.shape[3]
    inner = jnp.einsum("sakl,spql->apqk", weights, gathered, precision=lax.Precision.HIGHEST)
    rounded_coef = complex_mix(inner).astype(jnp.bfloat16)
    outward = jnp.einsum(
        "akr,pqk->apqr", target_basis[0], rounded_coef, preferred_element_type=jnp.float32
    )
    return complex_mix(outward).reshape(2, nrhs, 1, rows)


def swapped(every, partner, width):
    nrhs = every.shape[1]
    rows = every.shape[3]
    tiles = every.reshape(2, nrhs, -1, width)
    return jnp.take(tiles, partner[0], axis=2).reshape(2, nrhs, 1, rows)


def local_products(vectors, image):
    stacked = []
    for basis in vectors:
        real_part = jnp.sum(basis[0] * image[0] + basis[1] * image[1], axis=(1, 2))
        imag_part = jnp.sum(basis[0] * image[1] - basis[1] * image[0], axis=(1, 2))
        stacked.append(jnp.stack([real_part, imag_part]))
    return jnp.stack(stacked)


def local_squares(field):
    return jnp.sum(field[0] * field[0] + field[1] * field[1], axis=(1, 2))


def scaled(factor, field):
    real_f = factor[0][:, None, None]
    imag_f = factor[1][:, None, None]
    return jnp.stack([real_f * field[0] - imag_f * field[1], real_f * field[1] + imag_f * field[0]])


def coef_scaled(factor, coef):
    real_f = factor[0][None, :, None]
    imag_f = factor[1][None, :, None]
    return jnp.stack(
        [real_f * coef[:, 0] - imag_f * coef[:, 1], real_f * coef[:, 1] + imag_f * coef[:, 0]],
        axis=1,
    )


def shards(
    right_side, near_blocks, near_cols, partner, source_basis, target_basis, coupling, far_ranks
):
    rows = right_side.shape[3]
    width = near_blocks.shape[4]
    total = float(rows * lax.axis_size("dom") * lax.axis_size("blk"))
    everyone = ("dom", "blk")
    weights = far_weights(coupling, far_ranks, source_basis.shape[2])

    def spread(every):
        return jnp.moveaxis(every, 0, 2)

    window_rhs = neighbours(right_side)
    start_sum, coef_rhs, every_rhs = tree_collect(
        local_squares(right_side), coefficients(right_side, source_basis), right_side[:, :, 0]
    )
    beta = jnp.sqrt(start_sum / total + EPSILON)
    inv_scale = beta[None, :, None, None]
    first_vec = right_side / inv_scale
    window_one = window_rhs / inv_scale
    every_one = spread(every_rhs) / inv_scale
    coef_one = coef_rhs / beta[None, None, :, None]
    image_one = (
        first_vec
        + near_field(window_one, near_blocks, near_cols)
        + far_field(coef_one, weights, target_basis)
        - swapped(every_one, partner, width)
    )

    window_img = neighbours(image_one)
    parts = jnp.concatenate(
        [
            local_products([first_vec], image_one)[0],
            local_squares(image_one)[None],
            local_squares(first_vec)[None],
        ]
    )
    one, coef_img, every_img = tree_collect(
        parts, coefficients(image_one, source_basis), image_one[:, :, 0]
    )
    one = one / total
    h_one_one = one[0:2]
    sq_w1 = one[2]
    sq_v1 = one[3]
    norm_h11 = h_one_one[0] * h_one_one[0] + h_one_one[1] * h_one_one[1]
    sq_u1 = jnp.maximum(sq_w1 - norm_h11 * (2.0 - sq_v1), 0.0)
    h_two_one = jnp.sqrt(sq_u1 + EPSILON)
    inv_two = h_two_one[None, :, None, None]
    second_basis = (image_one - scaled(h_one_one, first_vec)) / inv_two
    window_two = (window_img - scaled(h_one_one, window_one)) / inv_two
    every_two = (spread(every_img) - scaled(h_one_one, every_one)) / inv_two
    coef_two = (coef_img - coef_scaled(h_one_one, coef_one)) / h_two_one[None, None, :, None]
    image_two = (
        second_basis
        + near_field(window_two, near_blocks, near_cols)
        + far_field(coef_two, weights, target_basis)
        - swapped(every_two, partner, width)
    )

    two = (
        tree_sum(
            jnp.concatenate(
                [
                    local_products([first_vec, second_basis], image_two).reshape(4, -1),
                    local_products([first_vec], second_basis)[0],
                    local_squares(image_two)[None],
                    local_squares(second_basis)[None],
                ]
            ),
            everyone,
        )
        / total
    )
    h_one_two = two[0:2]
    h_two_two = two[2:4]
    cross = two[4:6]
    sq_w2 = two[6]
    sq_v2 = two[7]
    norm_a = h_one_two[0] * h_one_two[0] + h_one_two[1] * h_one_two[1]
    norm_b = h_two_two[0] * h_two_two[0] + h_two_two[1] * h_two_two[1]
    ab_re = h_one_two[0] * h_two_two[0] + h_one_two[1] * h_two_two[1]
    ab_im = h_one_two[0] * h_two_two[1] - h_one_two[1] * h_two_two[0]
    mixed = ab_re * cross[0] - ab_im * cross[1]
    sq_u2 = sq_w2 - norm_a * (2.0 - sq_v1) - norm_b * (2.0 - sq_v2) + 2.0 * mixed
    sq_u2 = jnp.maximum(sq_u2, 0.0)
    rest_two = image_two - scaled(h_one_two, first_vec) - scaled(h_two_two, second_basis)
    h_three_two = jnp.sqrt(sq_u2 + EPSILON)
    third_basis = rest_two / h_three_two[None, :, None, None]
    hessenberg = jnp.stack(
        [
            beta,
            h_one_one[0],
            h_one_one[1],
            h_two_one,
            h_one_two[0],
            h_one_two[1],
            h_two_two[0],
            h_two_two[1],
            h_three_two,
        ],
        axis=1,
    )
    return (second_basis, third_basis, hessenberg)


def solution(mesh):
    return jax.shard_map(
        shards,
        mesh=mesh,
        in_specs=(
            P(None, None, "dom", "blk"),
            P("dom", "blk", None, None, None, None),
            P("dom", "blk", None),
            P("dom", "blk"),
            P("dom", None, None, "blk"),
            P("dom", None, None, "blk"),
            P("dom", "blk", None, None, None, None),
            P("dom", "blk", None),
        ),
        out_specs=(P(None, None, "dom", "blk"), P(None, None, "dom", "blk"), P()),
        check_vma=False,
    )
```

```python
import jax
import jax.numpy as jnp
from jax import lax
from jax.sharding import PartitionSpec as P

EPSILON = 1e-06


def _pow2(n):
    return n > 0 and (n & (n - 1)) == 0


def tree_sum(x, axes):
    for axis in axes:
        n = lax.axis_size(axis)
        if not _pow2(n):
            x = lax.psum(x, axis)
            continue
        k = 1
        while k < n:
            x = x + lax.ppermute(x, axis, [(i, i ^ k) for i in range(n)])
            k *= 2
    return x


def tree_collect(red, gat_blk, field):
    n = lax.axis_size("dom")
    flat = field[:, :, 0]
    if _pow2(n):
        idx = lax.axis_index("dom")
        every = flat[None]
        k = 1
        while k < n:
            packed = jnp.concatenate([red.reshape(-1), every.reshape(-1)])
            got = lax.ppermute(packed, "dom", [(i, i ^ k) for i in range(n)])
            red = red + got[: red.size].reshape(red.shape)
            other = got[red.size :].reshape(every.shape)
            low = (idx // k) % 2 == 0
            every = jnp.where(low, jnp.concatenate([every, other]), jnp.concatenate([other, every]))
            k *= 2
    else:
        red = lax.psum(red, "dom")
        every = lax.all_gather(flat, "dom", axis=0)
    n = lax.axis_size("blk")
    idx = lax.axis_index("blk")
    if _pow2(n):
        buf = gat_blk[None]
        first = field
        last = field
        left = jnp.zeros_like(field)
        right = jnp.zeros_like(field)
        k = 1
        while k < n:
            sizes = [red.size, buf.size, field.size, field.size]
            cuts = [sum(sizes[:j]) for j in range(5)]
            packed = jnp.concatenate(
                [red.reshape(-1), buf.reshape(-1), first.reshape(-1), last.reshape(-1)]
            )
            got = lax.ppermute(packed, "blk", [(i, i ^ k) for i in range(n)])
            o_red, o_buf, o_first, o_last = (got[cuts[j] : cuts[j + 1]] for j in range(4))
            red = red + o_red.reshape(red.shape)
            o_buf = o_buf.reshape(buf.shape)
            o_first = o_first.reshape(field.shape)
            o_last = o_last.reshape(field.shape)
            low = (idx // k) % 2 == 0
            buf = jnp.where(low, jnp.concatenate([buf, o_buf]), jnp.concatenate([o_buf, buf]))
            right = jnp.where(low & ((idx + 1) % k == 0), o_first, right)
            left = jnp.where((~low) & (idx % k == 0), o_last, left)
            first = jnp.where(low, first, o_first)
            last = jnp.where(low, o_last, last)
            k *= 2
    else:
        red = lax.psum(red, "blk")
        buf = lax.all_gather(gat_blk, "blk", axis=0)
        left = lax.ppermute(field, "blk", [(i, i + 1) for i in range(n - 1)])
        right = lax.ppermute(field, "blk", [(i + 1, i) for i in range(n - 1)])
    window = jnp.concatenate([left, field, right], axis=3)
    return red, buf, every, window


def complex_mix(products):
    return jnp.stack([products[0, 0] - products[1, 1], products[0, 1] + products[1, 0]])


def coefficients(field, source_basis):
    head = field.astype(jnp.bfloat16)
    tail = (field - head.astype(jnp.float32)).astype(jnp.bfloat16)
    split = jnp.concatenate([head[:, :, 0], tail[:, :, 0]], axis=1)
    coef_prod = jnp.einsum(
        "akr,pqr->apqk", source_basis[0], split, preferred_element_type=jnp.float32
    )
    nrhs = field.shape[1]
    coef_prod = coef_prod[:, :, :nrhs] + coef_prod[:, :, nrhs:]
    return jnp.stack([coef_prod[0, 0] + coef_prod[1, 1], coef_prod[0, 1] - coef_prod[1, 0]])


def near_field(window, near_blocks, near_cols):
    nrhs = window.shape[1]
    blocks_dev = near_blocks.shape[1]
    slots = near_blocks.shape[2]
    width = near_blocks.shape[4]
    rounded = window.astype(jnp.bfloat16).reshape(2, nrhs, 3 * blocks_dev, width)
    chosen = jnp.take(rounded, near_cols[0].reshape(-1), axis=2).reshape(
        2, nrhs, blocks_dev, slots, width
    )
    near_prod = jnp.einsum(
        "ikarc,pqikc->apqir", near_blocks[0], chosen, preferred_element_type=jnp.float32
    )
    return complex_mix(near_prod).reshape(2, nrhs, 1, blocks_dev * width)


def far_field(gathered, coupling, far_ranks, target_basis):
    nrhs = gathered.shape[2]
    rows = target_basis.shape[3]
    rank_cap = gathered.shape[3]
    levels = jnp.arange(rank_cap, dtype=jnp.int32)
    keep = (levels[None, :] < far_ranks[0, 0][:, None]).astype(jnp.float32)
    masked = gathered * keep[:, None, None, :]
    inner = jnp.einsum(
        "sakl,spql->apqsk", coupling[0, 0], masked, precision=lax.Precision.HIGHEST
    )
    inner = jnp.sum(inner * keep[None, None, None], axis=3)
    rounded_coef = complex_mix(inner).astype(jnp.bfloat16)
    outward = jnp.einsum(
        "akr,pqk->apqr", target_basis[0], rounded_coef, preferred_element_type=jnp.float32
    )
    return complex_mix(outward).reshape(2, nrhs, 1, rows)


def swapped(every, partner, width):
    nrhs = every.shape[1]
    rows = every.shape[3]
    tiles = every.reshape(2, nrhs, -1, width)
    return jnp.take(tiles, partner[0], axis=2).reshape(2, nrhs, 1, rows)


def local_products(vectors, image):
    stacked = []
    for basis in vectors:
        real_part = jnp.sum(basis[0] * image[0] + basis[1] * image[1], axis=(1, 2))
        imag_part = jnp.sum(basis[0] * image[1] - basis[1] * image[0], axis=(1, 2))
        stacked.append(jnp.stack([real_part, imag_part]))
    return jnp.stack(stacked)


def local_squares(field):
    return jnp.sum(field[0] * field[0] + field[1] * field[1], axis=(1, 2))


def scaled(factor, field):
    real_f = factor[0][:, None, None]
    imag_f = factor[1][:, None, None]
    return jnp.stack([real_f * field[0] - imag_f * field[1], real_f * field[1] + imag_f * field[0]])


def coef_scaled(factor, coef):
    real_f = factor[0][None, :, None]
    imag_f = factor[1][None, :, None]
    return jnp.stack(
        [real_f * coef[:, 0] - imag_f * coef[:, 1], real_f * coef[:, 1] + imag_f * coef[:, 0]],
        axis=1,
    )


def shards(
    right_side, near_blocks, near_cols, partner, source_basis, target_basis, coupling, far_ranks
):
    rows = right_side.shape[3]
    width = near_blocks.shape[4]
    total = float(rows * lax.axis_size("dom") * lax.axis_size("blk"))
    everyone = ("dom", "blk")

    def spread(every):
        return jnp.moveaxis(every, 0, 2)

    start_sum, coef_rhs, every_rhs, window_rhs = tree_collect(
        local_squares(right_side), coefficients(right_side, source_basis), right_side
    )
    beta = jnp.sqrt(start_sum / total + EPSILON)
    inv_scale = beta[None, :, None, None]
    first_vec = right_side / inv_scale
    window_one = window_rhs / inv_scale
    every_one = spread(every_rhs) / inv_scale
    coef_one = coef_rhs / beta[None, None, :, None]
    image_one = (
        first_vec
        + near_field(window_one, near_blocks, near_cols)
        + far_field(coef_one, coupling, far_ranks, target_basis)
        - swapped(every_one, partner, width)
    )

    parts = jnp.concatenate(
        [
            local_products([first_vec], image_one)[0],
            local_squares(image_one)[None],
            local_squares(first_vec)[None],
        ]
    )
    one, coef_img, every_img, window_img = tree_collect(
        parts, coefficients(image_one, source_basis), image_one
    )
    one = one / total
    h_one_one = one[0:2]
    sq_w1 = one[2]
    sq_v1 = one[3]
    norm_h11 = h_one_one[0] * h_one_one[0] + h_one_one[1] * h_one_one[1]
    sq_u1 = jnp.maximum(sq_w1 - norm_h11 * (2.0 - sq_v1), 0.0)
    h_two_one = jnp.sqrt(sq_u1 + EPSILON)
    inv_two = h_two_one[None, :, None, None]
    second_basis = (image_one - scaled(h_one_one, first_vec)) / inv_two
    window_two = (window_img - scaled(h_one_one, window_one)) / inv_two
    every_two = (spread(every_img) - scaled(h_one_one, every_one)) / inv_two
    coef_two = (coef_img - coef_scaled(h_one_one, coef_one)) / h_two_one[None, None, :, None]
    image_two = (
        second_basis
        + near_field(window_two, near_blocks, near_cols)
        + far_field(coef_two, coupling, far_ranks, target_basis)
        - swapped(every_two, partner, width)
    )

    two = (
        tree_sum(
            jnp.concatenate(
                [
                    local_products([first_vec, second_basis], image_two).reshape(4, -1),
                    local_products([first_vec], second_basis)[0],
                    local_squares(image_two)[None],
                    local_squares(second_basis)[None],
                ]
            ),
            everyone,
        )
        / total
    )
    h_one_two = two[0:2]
    h_two_two = two[2:4]
    cross = two[4:6]
    sq_w2 = two[6]
    sq_v2 = two[7]
    norm_a = h_one_two[0] * h_one_two[0] + h_one_two[1] * h_one_two[1]
    norm_b = h_two_two[0] * h_two_two[0] + h_two_two[1] * h_two_two[1]
    ab_re = h_one_two[0] * h_two_two[0] + h_one_two[1] * h_two_two[1]
    ab_im = h_one_two[0] * h_two_two[1] - h_one_two[1] * h_two_two[0]
    mixed = ab_re * cross[0] - ab_im * cross[1]
    sq_u2 = sq_w2 - norm_a * (2.0 - sq_v1) - norm_b * (2.0 - sq_v2) + 2.0 * mixed
    sq_u2 = jnp.maximum(sq_u2, 0.0)
    rest_two = image_two - scaled(h_one_two, first_vec) - scaled(h_two_two, second_basis)
    h_three_two = jnp.sqrt(sq_u2 + EPSILON)
    third_basis = rest_two / h_three_two[None, :, None, None]
    hessenberg = jnp.stack(
        [
            beta,
            h_one_one[0],
            h_one_one[1],
            h_two_one,
            h_one_two[0],
            h_one_two[1],
            h_two_two[0],
            h_two_two[1],
            h_three_two,
        ],
        axis=1,
    )
    return (second_basis, third_basis, hessenberg)


def solution(mesh):
    return jax.shard_map(
        shards,
        mesh=mesh,
        in_specs=(
            P(None, None, "dom", "blk"),
            P("dom", "blk", None, None, None, None),
            P("dom", "blk", None),
            P("dom", "blk"),
            P("dom", None, None, "blk"),
            P("dom", None, None, "blk"),
            P("dom", "blk", None, None, None, None),
            P("dom", "blk", None),
        ),
        out_specs=(P(None, None, "dom", "blk"), P(None, None, "dom", "blk"), P()),
        check_vma=False,
    )
```

```python
import jax
import jax.numpy as jnp
from jax import lax
from jax.sharding import PartitionSpec as P

EPSILON = 1e-06


def _pow2(n):
    return n > 0 and (n & (n - 1)) == 0


def tree_sum(x, axes):
    for axis in axes:
        n = lax.axis_size(axis)
        if not _pow2(n):
            x = lax.psum(x, axis)
            continue
        k = 1
        while k < n:
            x = x + lax.ppermute(x, axis, [(i, i ^ k) for i in range(n)])
            k *= 2
    return x


def tree_collect(red, gat_blk, gat_dom):
    for axis, gat in (("dom", gat_dom), ("blk", gat_blk)):
        n = lax.axis_size(axis)
        if not _pow2(n):
            red = lax.psum(red, axis)
            buf = lax.all_gather(gat, axis, axis=0)
        else:
            idx = lax.axis_index(axis)
            buf = gat[None]
            k = 1
            while k < n:
                packed = jnp.concatenate([red.reshape(-1), buf.reshape(-1)])
                got = lax.ppermute(packed, axis, [(i, i ^ k) for i in range(n)])
                red = red + got[: red.size].reshape(red.shape)
                other = got[red.size :].reshape(buf.shape)
                low = (idx // k) % 2 == 0
                buf = jnp.where(low, jnp.concatenate([buf, other]), jnp.concatenate([other, buf]))
                k *= 2
        if axis == "blk":
            gat_blk = buf
        else:
            gat_dom = buf
    return red, gat_blk, gat_dom


def neighbours(field):
    count = lax.axis_size("blk")
    ends = count - 1
    left = lax.ppermute(field, "blk", [(i, i + 1) for i in range(ends)])
    right = lax.ppermute(field, "blk", [(i + 1, i) for i in range(ends)])
    return jnp.concatenate([left, field, right], axis=3)


def complex_mix(products):
    return jnp.stack([products[0, 0] - products[1, 1], products[0, 1] + products[1, 0]])


def coefficients(field, source_basis):
    rounded = field.astype(jnp.bfloat16)
    coef_prod = jnp.einsum(
        "akr,pqr->apqk", source_basis[0], rounded[:, :, 0], preferred_element_type=jnp.float32
    )
    return jnp.stack([coef_prod[0, 0] + coef_prod[1, 1], coef_prod[0, 1] - coef_prod[1, 0]])


def near_field(window, near_blocks, near_cols):
    nrhs = window.shape[1]
    blocks_dev = near_blocks.shape[1]
    slots = near_blocks.shape[2]
    width = near_blocks.shape[4]
    rounded = window.astype(jnp.bfloat16).reshape(2, nrhs, 3 * blocks_dev, width)
    chosen = jnp.take(rounded, near_cols[0].reshape(-1), axis=2).reshape(
        2, nrhs, blocks_dev, slots, width
    )
    near_prod = jnp.einsum(
        "ikarc,pqikc->apqir", near_blocks[0], chosen, preferred_element_type=jnp.float32
    )
    return complex_mix(near_prod).reshape(2, nrhs, 1, blocks_dev * width)


def far_field(gathered, coupling, far_ranks, target_basis):
    nrhs = gathered.shape[2]
    rows = target_basis.shape[3]
    rank_cap = gathered.shape[3]
    levels = jnp.arange(rank_cap, dtype=jnp.int32)
    keep = (levels[None, :] < far_ranks[0, 0][:, None]).astype(jnp.float32)
    masked = gathered * keep[:, None, None, :]
    inner = jnp.einsum(
        "sakl,spql->apqsk", coupling[0, 0], masked, precision=lax.Precision.HIGHEST
    )
    inner = jnp.sum(inner * keep[None, None, None], axis=3)
    rounded_coef = complex_mix(inner).astype(jnp.bfloat16)
    outward = jnp.einsum(
        "akr,pqk->apqr", target_basis[0], rounded_coef, preferred_element_type=jnp.float32
    )
    return complex_mix(outward).reshape(2, nrhs, 1, rows)


def swapped(every, partner, width):
    nrhs = every.shape[1]
    rows = every.shape[3]
    tiles = every.reshape(2, nrhs, -1, width)
    return jnp.take(tiles, partner[0], axis=2).reshape(2, nrhs, 1, rows)


def local_products(vectors, image):
    stacked = []
    for basis in vectors:
        real_part = jnp.sum(basis[0] * image[0] + basis[1] * image[1], axis=(1, 2))
        imag_part = jnp.sum(basis[0] * image[1] - basis[1] * image[0], axis=(1, 2))
        stacked.append(jnp.stack([real_part, imag_part]))
    return jnp.stack(stacked)


def local_squares(field):
    return jnp.sum(field[0] * field[0] + field[1] * field[1], axis=(1, 2))


def scaled(factor, field):
    real_f = factor[0][:, None, None]
    imag_f = factor[1][:, None, None]
    return jnp.stack([real_f * field[0] - imag_f * field[1], real_f * field[1] + imag_f * field[0]])


def coef_scaled(factor, coef):
    real_f = factor[0][None, :, None]
    imag_f = factor[1][None, :, None]
    return jnp.stack(
        [real_f * coef[:, 0] - imag_f * coef[:, 1], real_f * coef[:, 1] + imag_f * coef[:, 0]],
        axis=1,
    )


def shards(
    right_side, near_blocks, near_cols, partner, source_basis, target_basis, coupling, far_ranks
):
    rows = right_side.shape[3]
    width = near_blocks.shape[4]
    total = float(rows * lax.axis_size("dom") * lax.axis_size("blk"))
    everyone = ("dom", "blk")

    def spread(every):
        return jnp.moveaxis(every, 0, 2)

    window_rhs = neighbours(right_side)
    start_sum, coef_rhs, every_rhs = tree_collect(
        local_squares(right_side), coefficients(right_side, source_basis), right_side[:, :, 0]
    )
    beta = jnp.sqrt(start_sum / total + EPSILON)
    inv_scale = beta[None, :, None, None]
    first_vec = right_side / inv_scale
    window_one = window_rhs / inv_scale
    every_one = spread(every_rhs) / inv_scale
    coef_one = coef_rhs / beta[None, None, :, None]
    image_one = (
        first_vec
        + near_field(window_one, near_blocks, near_cols)
        + far_field(coef_one, coupling, far_ranks, target_basis)
        - swapped(every_one, partner, width)
    )

    window_img = neighbours(image_one)
    parts = jnp.concatenate(
        [
            local_products([first_vec], image_one)[0],
            local_squares(image_one)[None],
            local_squares(first_vec)[None],
        ]
    )
    one, coef_img, every_img = tree_collect(
        parts, coefficients(image_one, source_basis), image_one[:, :, 0]
    )
    one = one / total
    h_one_one = one[0:2]
    sq_w1 = one[2]
    sq_v1 = one[3]
    norm_h11 = h_one_one[0] * h_one_one[0] + h_one_one[1] * h_one_one[1]
    sq_u1 = jnp.maximum(sq_w1 - norm_h11 * (2.0 - sq_v1), 0.0)
    h_two_one = jnp.sqrt(sq_u1 + EPSILON)
    inv_two = h_two_one[None, :, None, None]
    second_basis = (image_one - scaled(h_one_one, first_vec)) / inv_two
    window_two = (window_img - scaled(h_one_one, window_one)) / inv_two
    every_two = (spread(every_img) - scaled(h_one_one, every_one)) / inv_two
    coef_two = (coef_img - coef_scaled(h_one_one, coef_one)) / h_two_one[None, None, :, None]
    image_two = (
        second_basis
        + near_field(window_two, near_blocks, near_cols)
        + far_field(coef_two, coupling, far_ranks, target_basis)
        - swapped(every_two, partner, width)
    )

    two = (
        tree_sum(
            jnp.concatenate(
                [
                    local_products([first_vec, second_basis], image_two).reshape(4, -1),
                    local_products([first_vec], second_basis)[0],
                    local_squares(image_two)[None],
                    local_squares(second_basis)[None],
                ]
            ),
            everyone,
        )
        / total
    )
    h_one_two = two[0:2]
    h_two_two = two[2:4]
    cross = two[4:6]
    sq_w2 = two[6]
    sq_v2 = two[7]
    norm_a = h_one_two[0] * h_one_two[0] + h_one_two[1] * h_one_two[1]
    norm_b = h_two_two[0] * h_two_two[0] + h_two_two[1] * h_two_two[1]
    ab_re = h_one_two[0] * h_two_two[0] + h_one_two[1] * h_two_two[1]
    ab_im = h_one_two[0] * h_two_two[1] - h_one_two[1] * h_two_two[0]
    mixed = ab_re * cross[0] - ab_im * cross[1]
    sq_u2 = sq_w2 - norm_a * (2.0 - sq_v1) - norm_b * (2.0 - sq_v2) + 2.0 * mixed
    sq_u2 = jnp.maximum(sq_u2, 0.0)
    rest_two = image_two - scaled(h_one_two, first_vec) - scaled(h_two_two, second_basis)
    h_three_two = jnp.sqrt(sq_u2 + EPSILON)
    third_basis = rest_two / h_three_two[None, :, None, None]
    hessenberg = jnp.stack(
        [
            beta,
            h_one_one[0],
            h_one_one[1],
            h_two_one,
            h_one_two[0],
            h_one_two[1],
            h_two_two[0],
            h_two_two[1],
            h_three_two,
        ],
        axis=1,
    )
    return (second_basis, third_basis, hessenberg)


def solution(mesh):
    return jax.shard_map(
        shards,
        mesh=mesh,
        in_specs=(
            P(None, None, "dom", "blk"),
            P("dom", "blk", None, None, None, None),
            P("dom", "blk", None),
            P("dom", "blk"),
            P("dom", None, None, "blk"),
            P("dom", None, None, "blk"),
            P("dom", "blk", None, None, None, None),
            P("dom", "blk", None),
        ),
        out_specs=(P(None, None, "dom", "blk"), P(None, None, "dom", "blk"), P()),
        check_vma=False,
    )
```

```python
import jax
import jax.numpy as jnp
from jax import lax
from jax.sharding import PartitionSpec as P

EPSILON = 1e-06


def _pow2(n):
    return n > 0 and (n & (n - 1)) == 0


def tree_sum(x, axes):
    for axis in axes:
        n = lax.axis_size(axis)
        if not _pow2(n):
            x = lax.psum(x, axis)
            continue
        k = 1
        while k < n:
            x = x + lax.ppermute(x, axis, [(i, i ^ k) for i in range(n)])
            k *= 2
    return x


def tree_collect(red, gat_blk, gat_dom):
    for axis, gat in (("blk", gat_blk), ("dom", gat_dom)):
        n = lax.axis_size(axis)
        if not _pow2(n):
            red = lax.psum(red, axis)
            buf = lax.all_gather(gat, axis, axis=0)
        else:
            idx = lax.axis_index(axis)
            buf = gat[None]
            k = 1
            while k < n:
                packed = jnp.concatenate([red.reshape(-1), buf.reshape(-1)])
                got = lax.ppermute(packed, axis, [(i, i ^ k) for i in range(n)])
                red = red + got[: red.size].reshape(red.shape)
                other = got[red.size :].reshape(buf.shape)
                low = (idx // k) % 2 == 0
                buf = jnp.where(low, jnp.concatenate([buf, other]), jnp.concatenate([other, buf]))
                k *= 2
        if axis == "blk":
            gat_blk = buf
        else:
            gat_dom = buf
    return red, gat_blk, gat_dom


def neighbours(field):
    count = lax.axis_size("blk")
    ends = count - 1
    left = lax.ppermute(field, "blk", [(i, i + 1) for i in range(ends)])
    right = lax.ppermute(field, "blk", [(i + 1, i) for i in range(ends)])
    return jnp.concatenate([left, field, right], axis=3)


def complex_mix(products):
    return jnp.stack([products[0, 0] - products[1, 1], products[0, 1] + products[1, 0]])


def coefficients(field, source_basis):
    rounded = field.astype(jnp.bfloat16)
    coef_prod = jnp.einsum(
        "akr,pqr->apqk", source_basis[0], rounded[:, :, 0], preferred_element_type=jnp.float32
    )
    return jnp.stack([coef_prod[0, 0] + coef_prod[1, 1], coef_prod[0, 1] - coef_prod[1, 0]])


def near_field(window, near_blocks, near_cols):
    nrhs = window.shape[1]
    blocks_dev = near_blocks.shape[1]
    slots = near_blocks.shape[2]
    width = near_blocks.shape[4]
    rounded = window.astype(jnp.bfloat16).reshape(2, nrhs, 3 * blocks_dev, width)
    chosen = jnp.take(rounded, near_cols[0].reshape(-1), axis=2).reshape(
        2, nrhs, blocks_dev, slots, width
    )
    near_prod = jnp.einsum(
        "ikarc,pqikc->apqir", near_blocks[0], chosen, preferred_element_type=jnp.float32
    )
    return complex_mix(near_prod).reshape(2, nrhs, 1, blocks_dev * width)


def far_weights(coupling, far_ranks, rank_cap):
    row_coupling = coupling[0, 0]
    row_ranks = far_ranks[0, 0]
    levels = jnp.arange(rank_cap, dtype=jnp.int32)
    limit = row_ranks[:, None, None]
    keep = (levels[None, :, None] < limit) & (levels[None, None, :] < limit)
    return row_coupling * keep[:, None].astype(jnp.float32)


def far_field(gathered, weights, target_basis):
    nrhs = gathered.shape[2]
    rows = target_basis.shape[3]
    inner = jnp.sum(
        weights[:, :, None, None, :, :] * gathered[:, None, :, :, None, :], axis=(0, 5)
    )
    rounded_coef = complex_mix(inner).astype(jnp.bfloat16)
    outward = jnp.einsum(
        "akr,pqk->apqr", target_basis[0], rounded_coef, preferred_element_type=jnp.float32
    )
    return complex_mix(outward).reshape(2, nrhs, 1, rows)


def swapped(every, partner, width):
    nrhs = every.shape[1]
    rows = every.shape[3]
    tiles = every.reshape(2, nrhs, -1, width)
    return jnp.take(tiles, partner[0], axis=2).reshape(2, nrhs, 1, rows)


def local_products(vectors, image):
    stacked = []
    for basis in vectors:
        real_part = jnp.sum(basis[0] * image[0] + basis[1] * image[1], axis=(1, 2))
        imag_part = jnp.sum(basis[0] * image[1] - basis[1] * image[0], axis=(1, 2))
        stacked.append(jnp.stack([real_part, imag_part]))
    return jnp.stack(stacked)


def local_squares(field):
    return jnp.sum(field[0] * field[0] + field[1] * field[1], axis=(1, 2))


def scaled(factor, field):
    real_f = factor[0][:, None, None]
    imag_f = factor[1][:, None, None]
    return jnp.stack([real_f * field[0] - imag_f * field[1], real_f * field[1] + imag_f * field[0]])


def coef_scaled(factor, coef):
    real_f = factor[0][None, :, None]
    imag_f = factor[1][None, :, None]
    return jnp.stack(
        [real_f * coef[:, 0] - imag_f * coef[:, 1], real_f * coef[:, 1] + imag_f * coef[:, 0]],
        axis=1,
    )


def shards(
    right_side, near_blocks, near_cols, partner, source_basis, target_basis, coupling, far_ranks
):
    rows = right_side.shape[3]
    width = near_blocks.shape[4]
    total = float(rows * lax.axis_size("dom") * lax.axis_size("blk"))
    everyone = ("dom", "blk")
    weights = far_weights(coupling, far_ranks, source_basis.shape[2])

    def spread(every):
        return jnp.moveaxis(every, 0, 2)

    window_rhs = neighbours(right_side)
    start_sum, coef_rhs, every_rhs = tree_collect(
        local_squares(right_side), coefficients(right_side, source_basis), right_side[:, :, 0]
    )
    beta = jnp.sqrt(start_sum / total + EPSILON)
    inv_scale = beta[None, :, None, None]
    first_vec = right_side / inv_scale
    window_one = window_rhs / inv_scale
    every_one = spread(every_rhs) / inv_scale
    coef_one = coef_rhs / beta[None, None, :, None]
    image_one = (
        first_vec
        + near_field(window_one, near_blocks, near_cols)
        + far_field(coef_one, weights, target_basis)
        - swapped(every_one, partner, width)
    )

    window_img = neighbours(image_one)
    parts = jnp.concatenate(
        [
            local_products([first_vec], image_one)[0],
            local_squares(image_one)[None],
            local_squares(first_vec)[None],
        ]
    )
    one, coef_img, every_img = tree_collect(
        parts, coefficients(image_one, source_basis), image_one[:, :, 0]
    )
    one = one / total
    h_one_one = one[0:2]
    sq_w1 = one[2]
    sq_v1 = one[3]
    norm_h11 = h_one_one[0] * h_one_one[0] + h_one_one[1] * h_one_one[1]
    sq_u1 = jnp.maximum(sq_w1 - norm_h11 * (2.0 - sq_v1), 0.0)
    h_two_one = jnp.sqrt(sq_u1 + EPSILON)
    inv_two = h_two_one[None, :, None, None]
    second_basis = (image_one - scaled(h_one_one, first_vec)) / inv_two
    window_two = (window_img - scaled(h_one_one, window_one)) / inv_two
    every_two = (spread(every_img) - scaled(h_one_one, every_one)) / inv_two
    coef_two = (coef_img - coef_scaled(h_one_one, coef_one)) / h_two_one[None, None, :, None]
    image_two = (
        second_basis
        + near_field(window_two, near_blocks, near_cols)
        + far_field(coef_two, weights, target_basis)
        - swapped(every_two, partner, width)
    )

    two = (
        tree_sum(
            jnp.concatenate(
                [
                    local_products([first_vec, second_basis], image_two).reshape(4, -1),
                    local_products([first_vec], second_basis)[0],
                    local_squares(image_two)[None],
                    local_squares(second_basis)[None],
                ]
            ),
            everyone,
        )
        / total
    )
    h_one_two = two[0:2]
    h_two_two = two[2:4]
    cross = two[4:6]
    sq_w2 = two[6]
    sq_v2 = two[7]
    norm_a = h_one_two[0] * h_one_two[0] + h_one_two[1] * h_one_two[1]
    norm_b = h_two_two[0] * h_two_two[0] + h_two_two[1] * h_two_two[1]
    ab_re = h_one_two[0] * h_two_two[0] + h_one_two[1] * h_two_two[1]
    ab_im = h_one_two[0] * h_two_two[1] - h_one_two[1] * h_two_two[0]
    mixed = ab_re * cross[0] - ab_im * cross[1]
    sq_u2 = sq_w2 - norm_a * (2.0 - sq_v1) - norm_b * (2.0 - sq_v2) + 2.0 * mixed
    sq_u2 = jnp.maximum(sq_u2, 0.0)
    rest_two = image_two - scaled(h_one_two, first_vec) - scaled(h_two_two, second_basis)
    h_three_two = jnp.sqrt(sq_u2 + EPSILON)
    third_basis = rest_two / h_three_two[None, :, None, None]
    hessenberg = jnp.stack(
        [
            beta,
            h_one_one[0],
            h_one_one[1],
            h_two_one,
            h_one_two[0],
            h_one_two[1],
            h_two_two[0],
            h_two_two[1],
            h_three_two,
        ],
        axis=1,
    )
    return (second_basis, third_basis, hessenberg)


def solution(mesh):
    return jax.shard_map(
        shards,
        mesh=mesh,
        in_specs=(
            P(None, None, "dom", "blk"),
            P("dom", "blk", None, None, None, None),
            P("dom", "blk", None),
            P("dom", "blk"),
            P("dom", None, None, "blk"),
            P("dom", None, None, "blk"),
            P("dom", "blk", None, None, None, None),
            P("dom", "blk", None),
        ),
        out_specs=(P(None, None, "dom", "blk"), P(None, None, "dom", "blk"), P()),
        check_vma=False,
    )
```

```python
import jax
import jax.numpy as jnp
from jax import lax
from jax.sharding import PartitionSpec as P

EPSILON = 1e-06


def _pow2(n):
    return n > 0 and (n & (n - 1)) == 0


def tree_sum(x, axes):
    for axis in axes:
        n = lax.axis_size(axis)
        if not _pow2(n):
            x = lax.psum(x, axis)
            continue
        k = 1
        while k < n:
            x = x + lax.ppermute(x, axis, [(i, i ^ k) for i in range(n)])
            k *= 2
    return x


def tree_collect(red, gat_blk, gat_dom):
    for axis, gat in (("blk", gat_blk), ("dom", gat_dom)):
        n = lax.axis_size(axis)
        if not _pow2(n):
            red = lax.psum(red, axis)
            buf = lax.all_gather(gat, axis, axis=0)
        else:
            idx = lax.axis_index(axis)
            buf = gat[None]
            k = 1
            while k < n:
                packed = jnp.concatenate([red.reshape(-1), buf.reshape(-1)])
                got = lax.ppermute(packed, axis, [(i, i ^ k) for i in range(n)])
                red = red + got[: red.size].reshape(red.shape)
                other = got[red.size :].reshape(buf.shape)
                low = (idx // k) % 2 == 0
                buf = jnp.where(low, jnp.concatenate([buf, other]), jnp.concatenate([other, buf]))
                k *= 2
        if axis == "blk":
            gat_blk = buf
        else:
            gat_dom = buf
    return red, gat_blk, gat_dom


def neighbours(field):
    count = lax.axis_size("blk")
    ends = count - 1
    left = lax.ppermute(field, "blk", [(i, i + 1) for i in range(ends)])
    right = lax.ppermute(field, "blk", [(i + 1, i) for i in range(ends)])
    return jnp.concatenate([left, field, right], axis=3)


def complex_mix(products):
    return jnp.stack([products[0, 0] - products[1, 1], products[0, 1] + products[1, 0]])


def coefficients(field, source_basis):
    rounded = field.astype(jnp.bfloat16)
    coef_prod = jnp.einsum(
        "akr,pqr->apqk", source_basis[0], rounded[:, :, 0], preferred_element_type=jnp.float32
    )
    return jnp.stack([coef_prod[0, 0] + coef_prod[1, 1], coef_prod[0, 1] - coef_prod[1, 0]])


def near_field(window, near_blocks, near_cols):
    nrhs = window.shape[1]
    blocks_dev = near_blocks.shape[1]
    slots = near_blocks.shape[2]
    width = near_blocks.shape[4]
    rounded = window.astype(jnp.bfloat16).reshape(2, nrhs, 3 * blocks_dev, width)
    chosen = jnp.take(rounded, near_cols[0].reshape(-1), axis=2).reshape(
        2, nrhs, blocks_dev, slots, width
    )
    near_prod = jnp.einsum(
        "ikarc,pqikc->apqir", near_blocks[0], chosen, preferred_element_type=jnp.float32
    )
    return complex_mix(near_prod).reshape(2, nrhs, 1, blocks_dev * width)


def far_weights(coupling, far_ranks, rank_cap):
    levels = jnp.arange(rank_cap, dtype=jnp.int32)
    limit = far_ranks[0, 0][:, None, None, None]
    keep = (levels[None, None, :, None] < limit) & (levels[None, None, None, :] < limit)
    return jnp.where(keep, coupling[0, 0], 0.0)


def far_field(gathered, weights, target_basis):
    nrhs = gathered.shape[2]
    rows = target_basis.shape[3]
    inner = jnp.einsum("sakl,spql->apqk", weights, gathered, precision=lax.Precision.HIGHEST)
    rounded_coef = complex_mix(inner).astype(jnp.bfloat16)
    outward = jnp.einsum(
        "akr,pqk->apqr", target_basis[0], rounded_coef, preferred_element_type=jnp.float32
    )
    return complex_mix(outward).reshape(2, nrhs, 1, rows)


def swapped(every, partner, width):
    nrhs = every.shape[1]
    rows = every.shape[3]
    tiles = every.reshape(2, nrhs, -1, width)
    return jnp.take(tiles, partner[0], axis=2).reshape(2, nrhs, 1, rows)


def local_products(vectors, image):
    stacked = []
    for basis in vectors:
        real_part = jnp.sum(basis[0] * image[0] + basis[1] * image[1], axis=(1, 2))
        imag_part = jnp.sum(basis[0] * image[1] - basis[1] * image[0], axis=(1, 2))
        stacked.append(jnp.stack([real_part, imag_part]))
    return jnp.stack(stacked)


def local_squares(field):
    return jnp.sum(field[0] * field[0] + field[1] * field[1], axis=(1, 2))


def scaled(factor, field):
    real_f = factor[0][:, None, None]
    imag_f = factor[1][:, None, None]
    return jnp.stack([real_f * field[0] - imag_f * field[1], real_f * field[1] + imag_f * field[0]])


def coef_scaled(factor, coef):
    real_f = factor[0][None, :, None]
    imag_f = factor[1][None, :, None]
    return jnp.stack(
        [real_f * coef[:, 0] - imag_f * coef[:, 1], real_f * coef[:, 1] + imag_f * coef[:, 0]],
        axis=1,
    )


def shards(
    right_side, near_blocks, near_cols, partner, source_basis, target_basis, coupling, far_ranks
):
    rows = right_side.shape[3]
    width = near_blocks.shape[4]
    total = float(rows * lax.axis_size("dom") * lax.axis_size("blk"))
    everyone = ("dom", "blk")
    weights = far_weights(coupling, far_ranks, source_basis.shape[2])

    def spread(every):
        return jnp.moveaxis(every, 0, 2)

    window_rhs = neighbours(right_side)
    start_sum, coef_rhs, every_rhs = tree_collect(
        local_squares(right_side), coefficients(right_side, source_basis), right_side[:, :, 0]
    )
    beta = jnp.sqrt(start_sum / total + EPSILON)
    inv_scale = beta[None, :, None, None]
    first_vec = right_side / inv_scale
    window_one = window_rhs / inv_scale
    every_one = spread(every_rhs) / inv_scale
    coef_one = coef_rhs / beta[None, None, :, None]
    image_one = (
        first_vec
        + near_field(window_one, near_blocks, near_cols)
        + far_field(coef_one, weights, target_basis)
        - swapped(every_one, partner, width)
    )

    window_img = neighbours(image_one)
    parts = jnp.concatenate(
        [
            local_products([first_vec], image_one)[0],
            local_squares(image_one)[None],
            local_squares(first_vec)[None],
        ]
    )
    one, coef_img, every_img = tree_collect(
        parts, coefficients(image_one, source_basis), image_one[:, :, 0]
    )
    one = one / total
    h_one_one = one[0:2]
    sq_w1 = one[2]
    sq_v1 = one[3]
    norm_h11 = h_one_one[0] * h_one_one[0] + h_one_one[1] * h_one_one[1]
    sq_u1 = jnp.maximum(sq_w1 - norm_h11 * (2.0 - sq_v1), 0.0)
    h_two_one = jnp.sqrt(sq_u1 + EPSILON)
    inv_two = h_two_one[None, :, None, None]
    second_basis = (image_one - scaled(h_one_one, first_vec)) / inv_two
    window_two = (window_img - scaled(h_one_one, window_one)) / inv_two
    every_two = (spread(every_img) - scaled(h_one_one, every_one)) / inv_two
    coef_two = (coef_img - coef_scaled(h_one_one, coef_one)) / h_two_one[None, None, :, None]
    image_two = (
        second_basis
        + near_field(window_two, near_blocks, near_cols)
        + far_field(coef_two, weights, target_basis)
        - swapped(every_two, partner, width)
    )

    two = (
        tree_sum(
            jnp.concatenate(
                [
                    local_products([first_vec, second_basis], image_two).reshape(4, -1),
                    local_products([first_vec], second_basis)[0],
                    local_squares(image_two)[None],
                    local_squares(second_basis)[None],
                ]
            ),
            everyone,
        )
        / total
    )
    h_one_two = two[0:2]
    h_two_two = two[2:4]
    cross = two[4:6]
    sq_w2 = two[6]
    sq_v2 = two[7]
    norm_a = h_one_two[0] * h_one_two[0] + h_one_two[1] * h_one_two[1]
    norm_b = h_two_two[0] * h_two_two[0] + h_two_two[1] * h_two_two[1]
    ab_re = h_one_two[0] * h_two_two[0] + h_one_two[1] * h_two_two[1]
    ab_im = h_one_two[0] * h_two_two[1] - h_one_two[1] * h_two_two[0]
    mixed = ab_re * cross[0] - ab_im * cross[1]
    sq_u2 = sq_w2 - norm_a * (2.0 - sq_v1) - norm_b * (2.0 - sq_v2) + 2.0 * mixed
    sq_u2 = jnp.maximum(sq_u2, 0.0)
    rest_two = image_two - scaled(h_one_two, first_vec) - scaled(h_two_two, second_basis)
    h_three_two = jnp.sqrt(sq_u2 + EPSILON)
    third_basis = rest_two / h_three_two[None, :, None, None]
    hessenberg = jnp.stack(
        [
            beta,
            h_one_one[0],
            h_one_one[1],
            h_two_one,
            h_one_two[0],
            h_one_two[1],
            h_two_two[0],
            h_two_two[1],
            h_three_two,
        ],
        axis=1,
    )
    return (second_basis, third_basis, hessenberg)


def solution(mesh):
    return jax.shard_map(
        shards,
        mesh=mesh,
        in_specs=(
            P(None, None, "dom", "blk"),
            P("dom", "blk", None, None, None, None),
            P("dom", "blk", None),
            P("dom", "blk"),
            P("dom", None, None, "blk"),
            P("dom", None, None, "blk"),
            P("dom", "blk", None, None, None, None),
            P("dom", "blk", None),
        ),
        out_specs=(P(None, None, "dom", "blk"), P(None, None, "dom", "blk"), P()),
        check_vma=False,
    )
```

```python
import jax
import jax.numpy as jnp
from jax import lax
from jax.sharding import PartitionSpec as P

EPSILON = 1e-06


def _pow2(n):
    return n > 0 and (n & (n - 1)) == 0


def tree_sum(x, axes):
    for axis in axes:
        n = lax.axis_size(axis)
        if not _pow2(n):
            x = lax.psum(x, axis)
            continue
        k = 1
        while k < n:
            x = x + lax.ppermute(x, axis, [(i, i ^ k) for i in range(n)])
            k *= 2
    return x


def tree_collect(red, gat_blk, gat_dom):
    for axis, gat in (("blk", gat_blk), ("dom", gat_dom)):
        n = lax.axis_size(axis)
        if not _pow2(n):
            red = lax.psum(red, axis)
            buf = lax.all_gather(gat, axis, axis=0)
        else:
            idx = lax.axis_index(axis)
            buf = gat[None]
            k = 1
            while k < n:
                packed = jnp.concatenate([red.reshape(-1), buf.reshape(-1)])
                got = lax.ppermute(packed, axis, [(i, i ^ k) for i in range(n)])
                red = red + got[: red.size].reshape(red.shape)
                other = got[red.size :].reshape(buf.shape)
                low = (idx // k) % 2 == 0
                buf = jnp.where(low, jnp.concatenate([buf, other]), jnp.concatenate([other, buf]))
                k *= 2
        if axis == "blk":
            gat_blk = buf
        else:
            gat_dom = buf
    return red, gat_blk, gat_dom


def neighbours(field):
    count = lax.axis_size("blk")
    ends = count - 1
    left = lax.ppermute(field, "blk", [(i, i + 1) for i in range(ends)])
    right = lax.ppermute(field, "blk", [(i + 1, i) for i in range(ends)])
    return jnp.concatenate([left, field, right], axis=3)


def complex_mix(products):
    return jnp.stack([products[0, 0] - products[1, 1], products[0, 1] + products[1, 0]])


def coefficients(field, source_basis):
    rounded = field.astype(jnp.bfloat16)
    coef_prod = jnp.einsum(
        "akr,pqr->apqk", source_basis[0], rounded[:, :, 0], preferred_element_type=jnp.float32
    )
    return jnp.stack([coef_prod[0, 0] + coef_prod[1, 1], coef_prod[0, 1] - coef_prod[1, 0]])


def near_field(window, near_blocks, near_cols):
    nrhs = window.shape[1]
    blocks_dev = near_blocks.shape[1]
    slots = near_blocks.shape[2]
    width = near_blocks.shape[4]
    rounded = window.astype(jnp.bfloat16).reshape(2, nrhs, 3 * blocks_dev, width)
    chosen = jnp.take(rounded, near_cols[0].reshape(-1), axis=2).reshape(
        2, nrhs, blocks_dev, slots, width
    )
    near_prod = jnp.einsum(
        "ikarc,pqikc->apqir", near_blocks[0], chosen, preferred_element_type=jnp.float32
    )
    return complex_mix(near_prod).reshape(2, nrhs, 1, blocks_dev * width)


def far_weights(coupling, far_ranks, rank_cap):
    row_coupling = coupling[0, 0]
    row_ranks = far_ranks[0, 0]
    levels = jnp.arange(rank_cap, dtype=jnp.int32)
    limit = row_ranks[:, None, None]
    keep = (levels[None, :, None] < limit) & (levels[None, None, :] < limit)
    return row_coupling * keep[:, None].astype(jnp.float32)


def far_field(gathered, weights, target_basis):
    nrhs = gathered.shape[2]
    rows = target_basis.shape[3]
    inner = jnp.einsum("sakl,spql->apqk", weights, gathered, precision=lax.Precision.HIGH)
    rounded_coef = complex_mix(inner).astype(jnp.bfloat16)
    outward = jnp.einsum(
        "akr,pqk->apqr", target_basis[0], rounded_coef, preferred_element_type=jnp.float32
    )
    return complex_mix(outward).reshape(2, nrhs, 1, rows)


def swapped(every, partner, width):
    nrhs = every.shape[1]
    rows = every.shape[3]
    tiles = every.reshape(2, nrhs, -1, width)
    return jnp.take(tiles, partner[0], axis=2).reshape(2, nrhs, 1, rows)


def local_products(vectors, image):
    stacked = []
    for basis in vectors:
        real_part = jnp.sum(basis[0] * image[0] + basis[1] * image[1], axis=(1, 2))
        imag_part = jnp.sum(basis[0] * image[1] - basis[1] * image[0], axis=(1, 2))
        stacked.append(jnp.stack([real_part, imag_part]))
    return jnp.stack(stacked)


def local_squares(field):
    return jnp.sum(field[0] * field[0] + field[1] * field[1], axis=(1, 2))


def scaled(factor, field):
    real_f = factor[0][:, None, None]
    imag_f = factor[1][:, None, None]
    return jnp.stack([real_f * field[0] - imag_f * field[1], real_f * field[1] + imag_f * field[0]])


def coef_scaled(factor, coef):
    real_f = factor[0][None, :, None]
    imag_f = factor[1][None, :, None]
    return jnp.stack(
        [real_f * coef[:, 0] - imag_f * coef[:, 1], real_f * coef[:, 1] + imag_f * coef[:, 0]],
        axis=1,
    )


def shards(
    right_side, near_blocks, near_cols, partner, source_basis, target_basis, coupling, far_ranks
):
    rows = right_side.shape[3]
    width = near_blocks.shape[4]
    total = float(rows * lax.axis_size("dom") * lax.axis_size("blk"))
    everyone = ("dom", "blk")
    weights = far_weights(coupling, far_ranks, source_basis.shape[2])

    def spread(every):
        return jnp.moveaxis(every, 0, 2)

    window_rhs = neighbours(right_side)
    start_sum, coef_rhs, every_rhs = tree_collect(
        local_squares(right_side), coefficients(right_side, source_basis), right_side[:, :, 0]
    )
    beta = jnp.sqrt(start_sum / total + EPSILON)
    inv_scale = beta[None, :, None, None]
    first_vec = right_side / inv_scale
    window_one = window_rhs / inv_scale
    every_one = spread(every_rhs) / inv_scale
    coef_one = coef_rhs / beta[None, None, :, None]
    image_one = (
        first_vec
        + near_field(window_one, near_blocks, near_cols)
        + far_field(coef_one, weights, target_basis)
        - swapped(every_one, partner, width)
    )

    window_img = neighbours(image_one)
    parts = jnp.concatenate(
        [
            local_products([first_vec], image_one)[0],
            local_squares(image_one)[None],
            local_squares(first_vec)[None],
        ]
    )
    one, coef_img, every_img = tree_collect(
        parts, coefficients(image_one, source_basis), image_one[:, :, 0]
    )
    one = one / total
    h_one_one = one[0:2]
    sq_w1 = one[2]
    sq_v1 = one[3]
    norm_h11 = h_one_one[0] * h_one_one[0] + h_one_one[1] * h_one_one[1]
    sq_u1 = jnp.maximum(sq_w1 - norm_h11 * (2.0 - sq_v1), 0.0)
    h_two_one = jnp.sqrt(sq_u1 + EPSILON)
    inv_two = h_two_one[None, :, None, None]
    second_basis = (image_one - scaled(h_one_one, first_vec)) / inv_two
    window_two = (window_img - scaled(h_one_one, window_one)) / inv_two
    every_two = (spread(every_img) - scaled(h_one_one, every_one)) / inv_two
    coef_two = (coef_img - coef_scaled(h_one_one, coef_one)) / h_two_one[None, None, :, None]
    image_two = (
        second_basis
        + near_field(window_two, near_blocks, near_cols)
        + far_field(coef_two, weights, target_basis)
        - swapped(every_two, partner, width)
    )

    two = (
        tree_sum(
            jnp.concatenate(
                [
                    local_products([first_vec, second_basis], image_two).reshape(4, -1),
                    local_products([first_vec], second_basis)[0],
                    local_squares(image_two)[None],
                    local_squares(second_basis)[None],
                ]
            ),
            everyone,
        )
        / total
    )
    h_one_two = two[0:2]
    h_two_two = two[2:4]
    cross = two[4:6]
    sq_w2 = two[6]
    sq_v2 = two[7]
    norm_a = h_one_two[0] * h_one_two[0] + h_one_two[1] * h_one_two[1]
    norm_b = h_two_two[0] * h_two_two[0] + h_two_two[1] * h_two_two[1]
    ab_re = h_one_two[0] * h_two_two[0] + h_one_two[1] * h_two_two[1]
    ab_im = h_one_two[0] * h_two_two[1] - h_one_two[1] * h_two_two[0]
    mixed = ab_re * cross[0] - ab_im * cross[1]
    sq_u2 = sq_w2 - norm_a * (2.0 - sq_v1) - norm_b * (2.0 - sq_v2) + 2.0 * mixed
    sq_u2 = jnp.maximum(sq_u2, 0.0)
    rest_two = image_two - scaled(h_one_two, first_vec) - scaled(h_two_two, second_basis)
    h_three_two = jnp.sqrt(sq_u2 + EPSILON)
    third_basis = rest_two / h_three_two[None, :, None, None]
    hessenberg = jnp.stack(
        [
            beta,
            h_one_one[0],
            h_one_one[1],
            h_two_one,
            h_one_two[0],
            h_one_two[1],
            h_two_two[0],
            h_two_two[1],
            h_three_two,
        ],
        axis=1,
    )
    return (second_basis, third_basis, hessenberg)


def solution(mesh):
    return jax.shard_map(
        shards,
        mesh=mesh,
        in_specs=(
            P(None, None, "dom", "blk"),
            P("dom", "blk", None, None, None, None),
            P("dom", "blk", None),
            P("dom", "blk"),
            P("dom", None, None, "blk"),
            P("dom", None, None, "blk"),
            P("dom", "blk", None, None, None, None),
            P("dom", "blk", None),
        ),
        out_specs=(P(None, None, "dom", "blk"), P(None, None, "dom", "blk"), P()),
        check_vma=False,
    )
```

```python
import jax
import jax.numpy as jnp
from jax import lax
from jax.sharding import PartitionSpec as P

EPSILON = 1e-06


def _pow2(n):
    return n > 0 and (n & (n - 1)) == 0


def tree_sum(x, axes):
    for axis in axes:
        n = lax.axis_size(axis)
        if not _pow2(n):
            x = lax.psum(x, axis)
            continue
        k = 1
        while k < n:
            x = x + lax.ppermute(x, axis, [(i, i ^ k) for i in range(n)])
            k *= 2
    return x


def tree_collect(red, gat_blk, gat_dom):
    for axis, gat in (("blk", gat_blk), ("dom", gat_dom)):
        n = lax.axis_size(axis)
        if not _pow2(n):
            red = lax.psum(red, axis)
            buf = lax.all_gather(gat, axis, axis=0)
        else:
            idx = lax.axis_index(axis)
            buf = gat[None]
            k = 1
            while k < n:
                packed = jnp.concatenate([red.reshape(-1), buf.reshape(-1)])
                got = lax.ppermute(packed, axis, [(i, i ^ k) for i in range(n)])
                red = red + got[: red.size].reshape(red.shape)
                other = got[red.size :].reshape(buf.shape)
                low = (idx // k) % 2 == 0
                buf = jnp.where(low, jnp.concatenate([buf, other]), jnp.concatenate([other, buf]))
                k *= 2
        if axis == "blk":
            gat_blk = buf
        else:
            gat_dom = buf
    return red, gat_blk, gat_dom


def neighbours(field):
    count = lax.axis_size("blk")
    ends = count - 1
    left = lax.ppermute(field, "blk", [(i, i + 1) for i in range(ends)])
    right = lax.ppermute(field, "blk", [(i + 1, i) for i in range(ends)])
    return jnp.concatenate([left, field, right], axis=3)


def complex_mix(products):
    return jnp.stack([products[0, 0] - products[1, 1], products[0, 1] + products[1, 0]])


def coefficients(field, source_basis):
    rounded = field.astype(jnp.bfloat16)
    coef_prod = jnp.einsum(
        "akr,pqr->apqk", source_basis[0], rounded[:, :, 0], preferred_element_type=jnp.float32
    )
    return jnp.stack([coef_prod[0, 0] + coef_prod[1, 1], coef_prod[0, 1] - coef_prod[1, 0]])


def near_field(window, near_blocks, near_cols):
    nrhs = window.shape[1]
    blocks_dev = near_blocks.shape[1]
    slots = near_blocks.shape[2]
    width = near_blocks.shape[4]
    rounded = window.astype(jnp.bfloat16).reshape(2, nrhs, 3 * blocks_dev, width)
    chosen = rounded.at[:, :, near_cols[0].reshape(-1)].get(mode="promise_in_bounds").reshape(
        2, nrhs, blocks_dev, slots, width
    )
    near_prod = jnp.einsum(
        "ikarc,pqikc->apqir", near_blocks[0], chosen, preferred_element_type=jnp.float32
    )
    return complex_mix(near_prod).reshape(2, nrhs, 1, blocks_dev * width)


def far_weights(coupling, far_ranks, rank_cap):
    row_coupling = coupling[0, 0]
    row_ranks = far_ranks[0, 0]
    levels = jnp.arange(rank_cap, dtype=jnp.int32)
    limit = row_ranks[:, None, None]
    keep = (levels[None, :, None] < limit) & (levels[None, None, :] < limit)
    return row_coupling * keep[:, None].astype(jnp.float32)


def far_field(gathered, weights, target_basis):
    nrhs = gathered.shape[2]
    rows = target_basis.shape[3]
    inner = jnp.einsum("sakl,spql->apqk", weights, gathered, precision=lax.Precision.HIGH)
    rounded_coef = complex_mix(inner).astype(jnp.bfloat16)
    outward = jnp.einsum(
        "akr,pqk->apqr", target_basis[0], rounded_coef, preferred_element_type=jnp.float32
    )
    return complex_mix(outward).reshape(2, nrhs, 1, rows)


def swapped(every, partner, width):
    nrhs = every.shape[1]
    rows = every.shape[3]
    tiles = every.reshape(2, nrhs, -1, width)
    return tiles.at[:, :, partner[0]].get(mode="promise_in_bounds").reshape(2, nrhs, 1, rows)


def local_products(vectors, image):
    stacked = []
    for basis in vectors:
        real_part = jnp.sum(basis[0] * image[0] + basis[1] * image[1], axis=(1, 2))
        imag_part = jnp.sum(basis[0] * image[1] - basis[1] * image[0], axis=(1, 2))
        stacked.append(jnp.stack([real_part, imag_part]))
    return jnp.stack(stacked)


def local_squares(field):
    return jnp.sum(field[0] * field[0] + field[1] * field[1], axis=(1, 2))


def scaled(factor, field):
    real_f = factor[0][:, None, None]
    imag_f = factor[1][:, None, None]
    return jnp.stack([real_f * field[0] - imag_f * field[1], real_f * field[1] + imag_f * field[0]])


def coef_scaled(factor, coef):
    real_f = factor[0][None, :, None]
    imag_f = factor[1][None, :, None]
    return jnp.stack(
        [real_f * coef[:, 0] - imag_f * coef[:, 1], real_f * coef[:, 1] + imag_f * coef[:, 0]],
        axis=1,
    )


def shards(
    right_side, near_blocks, near_cols, partner, source_basis, target_basis, coupling, far_ranks
):
    rows = right_side.shape[3]
    width = near_blocks.shape[4]
    total = float(rows * lax.axis_size("dom") * lax.axis_size("blk"))
    everyone = ("dom", "blk")
    weights = far_weights(coupling, far_ranks, source_basis.shape[2])

    def spread(every):
        return jnp.moveaxis(every, 0, 2)

    window_rhs = neighbours(right_side)
    start_sum, coef_rhs, every_rhs = tree_collect(
        local_squares(right_side), coefficients(right_side, source_basis), right_side[:, :, 0]
    )
    beta = jnp.sqrt(start_sum / total + EPSILON)
    inv_scale = beta[None, :, None, None]
    first_vec = right_side / inv_scale
    window_one = window_rhs / inv_scale
    every_one = spread(every_rhs) / inv_scale
    coef_one = coef_rhs / beta[None, None, :, None]
    image_one = (
        first_vec
        + near_field(window_one, near_blocks, near_cols)
        + far_field(coef_one, weights, target_basis)
        - swapped(every_one, partner, width)
    )

    window_img = neighbours(image_one)
    parts = jnp.concatenate(
        [
            local_products([first_vec], image_one)[0],
            local_squares(image_one)[None],
            local_squares(first_vec)[None],
        ]
    )
    one, coef_img, every_img = tree_collect(
        parts, coefficients(image_one, source_basis), image_one[:, :, 0]
    )
    one = one / total
    h_one_one = one[0:2]
    sq_w1 = one[2]
    sq_v1 = one[3]
    norm_h11 = h_one_one[0] * h_one_one[0] + h_one_one[1] * h_one_one[1]
    sq_u1 = jnp.maximum(sq_w1 - norm_h11 * (2.0 - sq_v1), 0.0)
    h_two_one = jnp.sqrt(sq_u1 + EPSILON)
    inv_two = h_two_one[None, :, None, None]
    second_basis = (image_one - scaled(h_one_one, first_vec)) / inv_two
    window_two = (window_img - scaled(h_one_one, window_one)) / inv_two
    every_two = (spread(every_img) - scaled(h_one_one, every_one)) / inv_two
    coef_two = (coef_img - coef_scaled(h_one_one, coef_one)) / h_two_one[None, None, :, None]
    image_two = (
        second_basis
        + near_field(window_two, near_blocks, near_cols)
        + far_field(coef_two, weights, target_basis)
        - swapped(every_two, partner, width)
    )

    two = (
        tree_sum(
            jnp.concatenate(
                [
                    local_products([first_vec, second_basis], image_two).reshape(4, -1),
                    local_products([first_vec], second_basis)[0],
                    local_squares(image_two)[None],
                    local_squares(second_basis)[None],
                ]
            ),
            everyone,
        )
        / total
    )
    h_one_two = two[0:2]
    h_two_two = two[2:4]
    cross = two[4:6]
    sq_w2 = two[6]
    sq_v2 = two[7]
    norm_a = h_one_two[0] * h_one_two[0] + h_one_two[1] * h_one_two[1]
    norm_b = h_two_two[0] * h_two_two[0] + h_two_two[1] * h_two_two[1]
    ab_re = h_one_two[0] * h_two_two[0] + h_one_two[1] * h_two_two[1]
    ab_im = h_one_two[0] * h_two_two[1] - h_one_two[1] * h_two_two[0]
    mixed = ab_re * cross[0] - ab_im * cross[1]
    sq_u2 = sq_w2 - norm_a * (2.0 - sq_v1) - norm_b * (2.0 - sq_v2) + 2.0 * mixed
    sq_u2 = jnp.maximum(sq_u2, 0.0)
    rest_two = image_two - scaled(h_one_two, first_vec) - scaled(h_two_two, second_basis)
    h_three_two = jnp.sqrt(sq_u2 + EPSILON)
    third_basis = rest_two / h_three_two[None, :, None, None]
    hessenberg = jnp.stack(
        [
            beta,
            h_one_one[0],
            h_one_one[1],
            h_two_one,
            h_one_two[0],
            h_one_two[1],
            h_two_two[0],
            h_two_two[1],
            h_three_two,
        ],
        axis=1,
    )
    return (second_basis, third_basis, hessenberg)


def solution(mesh):
    return jax.shard_map(
        shards,
        mesh=mesh,
        in_specs=(
            P(None, None, "dom", "blk"),
            P("dom", "blk", None, None, None, None),
            P("dom", "blk", None),
            P("dom", "blk"),
            P("dom", None, None, "blk"),
            P("dom", None, None, "blk"),
            P("dom", "blk", None, None, None, None),
            P("dom", "blk", None),
        ),
        out_specs=(P(None, None, "dom", "blk"), P(None, None, "dom", "blk"), P()),
        check_vma=False,
    )
```

```python
import jax
import jax.numpy as jnp
from jax import lax
from jax.sharding import PartitionSpec as P

EPSILON = 1e-06


def _pow2(n):
    return n > 0 and (n & (n - 1)) == 0


def tree_sum(x, axes):
    for axis in axes:
        n = lax.axis_size(axis)
        if not _pow2(n):
            x = lax.psum(x, axis)
            continue
        k = 1
        while k < n:
            x = x + lax.ppermute(x, axis, [(i, i ^ k) for i in range(n)])
            k *= 2
    return x


def tree_collect(red, gat_blk, gat_dom, dom_first=False):
    rounds = (("blk", gat_blk), ("dom", gat_dom))
    if dom_first:
        rounds = rounds[::-1]
    for axis, gat in rounds:
        n = lax.axis_size(axis)
        if not _pow2(n):
            red = lax.psum(red, axis)
            buf = lax.all_gather(gat, axis, axis=0)
        else:
            idx = lax.axis_index(axis)
            buf = gat[None]
            k = 1
            while k < n:
                packed = jnp.concatenate([red.reshape(-1), buf.reshape(-1)])
                got = lax.ppermute(packed, axis, [(i, i ^ k) for i in range(n)])
                red = red + got[: red.size].reshape(red.shape)
                other = got[red.size :].reshape(buf.shape)
                low = (idx // k) % 2 == 0
                buf = jnp.where(low, jnp.concatenate([buf, other]), jnp.concatenate([other, buf]))
                k *= 2
        if axis == "blk":
            gat_blk = buf
        else:
            gat_dom = buf
    return red, gat_blk, gat_dom


def neighbours(field):
    count = lax.axis_size("blk")
    ends = count - 1
    left = lax.ppermute(field, "blk", [(i, i + 1) for i in range(ends)])
    right = lax.ppermute(field, "blk", [(i + 1, i) for i in range(ends)])
    return jnp.concatenate([left, field, right], axis=3)


def complex_mix(products):
    return jnp.stack([products[0, 0] - products[1, 1], products[0, 1] + products[1, 0]])


def coefficients(field, source_basis):
    rounded = field.astype(jnp.bfloat16)
    coef_prod = jnp.einsum(
        "akr,pqr->apqk", source_basis[0], rounded[:, :, 0], preferred_element_type=jnp.float32
    )
    return jnp.stack([coef_prod[0, 0] + coef_prod[1, 1], coef_prod[0, 1] - coef_prod[1, 0]])


def near_field(window, near_blocks, near_cols):
    nrhs = window.shape[1]
    blocks_dev = near_blocks.shape[1]
    slots = near_blocks.shape[2]
    width = near_blocks.shape[4]
    rounded = window.astype(jnp.bfloat16).reshape(2, nrhs, 3 * blocks_dev, width)
    chosen = rounded.at[:, :, near_cols[0].reshape(-1)].get(mode="promise_in_bounds").reshape(
        2, nrhs, blocks_dev, slots, width
    )
    near_prod = jnp.einsum(
        "ikarc,pqikc->apqir", near_blocks[0], chosen, preferred_element_type=jnp.float32
    )
    return complex_mix(near_prod).reshape(2, nrhs, 1, blocks_dev * width)


def far_weights(coupling, far_ranks, rank_cap):
    row_coupling = coupling[0, 0]
    row_ranks = far_ranks[0, 0]
    levels = jnp.arange(rank_cap, dtype=jnp.int32)
    limit = row_ranks[:, None, None]
    keep = (levels[None, :, None] < limit) & (levels[None, None, :] < limit)
    return row_coupling * keep[:, None].astype(jnp.float32)


def far_field(gathered, weights, target_basis):
    nrhs = gathered.shape[2]
    rows = target_basis.shape[3]
    inner = jnp.einsum("sakl,spql->apqk", weights, gathered, precision=lax.Precision.HIGH)
    rounded_coef = complex_mix(inner).astype(jnp.bfloat16)
    outward = jnp.einsum(
        "akr,pqk->apqr", target_basis[0], rounded_coef, preferred_element_type=jnp.float32
    )
    return complex_mix(outward).reshape(2, nrhs, 1, rows)


def swapped(every, partner, width):
    nrhs = every.shape[1]
    rows = every.shape[3]
    tiles = every.reshape(2, nrhs, -1, width)
    return tiles.at[:, :, partner[0]].get(mode="promise_in_bounds").reshape(2, nrhs, 1, rows)


def local_products(vectors, image):
    stacked = []
    for basis in vectors:
        real_part = jnp.sum(basis[0] * image[0] + basis[1] * image[1], axis=(1, 2))
        imag_part = jnp.sum(basis[0] * image[1] - basis[1] * image[0], axis=(1, 2))
        stacked.append(jnp.stack([real_part, imag_part]))
    return jnp.stack(stacked)


def local_squares(field):
    return jnp.sum(field[0] * field[0] + field[1] * field[1], axis=(1, 2))


def scaled(factor, field):
    real_f = factor[0][:, None, None]
    imag_f = factor[1][:, None, None]
    return jnp.stack([real_f * field[0] - imag_f * field[1], real_f * field[1] + imag_f * field[0]])


def coef_scaled(factor, coef):
    real_f = factor[0][None, :, None]
    imag_f = factor[1][None, :, None]
    return jnp.stack(
        [real_f * coef[:, 0] - imag_f * coef[:, 1], real_f * coef[:, 1] + imag_f * coef[:, 0]],
        axis=1,
    )


def shards(
    right_side, near_blocks, near_cols, partner, source_basis, target_basis, coupling, far_ranks
):
    rows = right_side.shape[3]
    width = near_blocks.shape[4]
    total = float(rows * lax.axis_size("dom") * lax.axis_size("blk"))
    everyone = ("dom", "blk")
    weights = far_weights(coupling, far_ranks, source_basis.shape[2])

    def spread(every):
        return jnp.moveaxis(every, 0, 2)

    window_rhs = neighbours(right_side)
    start_sum, coef_rhs, every_rhs = tree_collect(
        local_squares(right_side),
        coefficients(right_side, source_basis),
        right_side[:, :, 0],
        dom_first=True,
    )
    beta = jnp.sqrt(start_sum / total + EPSILON)
    inv_scale = beta[None, :, None, None]
    first_vec = right_side / inv_scale
    window_one = window_rhs / inv_scale
    every_one = spread(every_rhs) / inv_scale
    coef_one = coef_rhs / beta[None, None, :, None]
    image_one = (
        first_vec
        + near_field(window_one, near_blocks, near_cols)
        + far_field(coef_one, weights, target_basis)
        - swapped(every_one, partner, width)
    )

    window_img = neighbours(image_one)
    parts = jnp.concatenate(
        [
            local_products([first_vec], image_one)[0],
            local_squares(image_one)[None],
            local_squares(first_vec)[None],
        ]
    )
    one, coef_img, every_img = tree_collect(
        parts, coefficients(image_one, source_basis), image_one[:, :, 0]
    )
    one = one / total
    h_one_one = one[0:2]
    sq_w1 = one[2]
    sq_v1 = one[3]
    norm_h11 = h_one_one[0] * h_one_one[0] + h_one_one[1] * h_one_one[1]
    sq_u1 = jnp.maximum(sq_w1 - norm_h11 * (2.0 - sq_v1), 0.0)
    h_two_one = jnp.sqrt(sq_u1 + EPSILON)
    inv_two = h_two_one[None, :, None, None]
    second_basis = (image_one - scaled(h_one_one, first_vec)) / inv_two
    window_two = (window_img - scaled(h_one_one, window_one)) / inv_two
    every_two = (spread(every_img) - scaled(h_one_one, every_one)) / inv_two
    coef_two = (coef_img - coef_scaled(h_one_one, coef_one)) / h_two_one[None, None, :, None]
    image_two = (
        second_basis
        + near_field(window_two, near_blocks, near_cols)
        + far_field(coef_two, weights, target_basis)
        - swapped(every_two, partner, width)
    )

    two = (
        tree_sum(
            jnp.concatenate(
                [
                    local_products([first_vec, second_basis], image_two).reshape(4, -1),
                    local_products([first_vec], second_basis)[0],
                    local_squares(image_two)[None],
                    local_squares(second_basis)[None],
                ]
            ),
            everyone,
        )
        / total
    )
    h_one_two = two[0:2]
    h_two_two = two[2:4]
    cross = two[4:6]
    sq_w2 = two[6]
    sq_v2 = two[7]
    norm_a = h_one_two[0] * h_one_two[0] + h_one_two[1] * h_one_two[1]
    norm_b = h_two_two[0] * h_two_two[0] + h_two_two[1] * h_two_two[1]
    ab_re = h_one_two[0] * h_two_two[0] + h_one_two[1] * h_two_two[1]
    ab_im = h_one_two[0] * h_two_two[1] - h_one_two[1] * h_two_two[0]
    mixed = ab_re * cross[0] - ab_im * cross[1]
    sq_u2 = sq_w2 - norm_a * (2.0 - sq_v1) - norm_b * (2.0 - sq_v2) + 2.0 * mixed
    sq_u2 = jnp.maximum(sq_u2, 0.0)
    rest_two = image_two - scaled(h_one_two, first_vec) - scaled(h_two_two, second_basis)
    h_three_two = jnp.sqrt(sq_u2 + EPSILON)
    third_basis = rest_two / h_three_two[None, :, None, None]
    hessenberg = jnp.stack(
        [
            beta,
            h_one_one[0],
            h_one_one[1],
            h_two_one,
            h_one_two[0],
            h_one_two[1],
            h_two_two[0],
            h_two_two[1],
            h_three_two,
        ],
        axis=1,
    )
    return (second_basis, third_basis, hessenberg)


def solution(mesh):
    return jax.shard_map(
        shards,
        mesh=mesh,
        in_specs=(
            P(None, None, "dom", "blk"),
            P("dom", "blk", None, None, None, None),
            P("dom", "blk", None),
            P("dom", "blk"),
            P("dom", None, None, "blk"),
            P("dom", None, None, "blk"),
            P("dom", "blk", None, None, None, None),
            P("dom", "blk", None),
        ),
        out_specs=(P(None, None, "dom", "blk"), P(None, None, "dom", "blk"), P()),
        check_vma=False,
    )
```

```python
import jax
import jax.numpy as jnp
from jax import lax
from jax.sharding import PartitionSpec as P

EPSILON = 1e-06


def _pow2(n):
    return n > 0 and (n & (n - 1)) == 0


def tree_sum(x, axes):
    for axis in axes:
        n = lax.axis_size(axis)
        if not _pow2(n):
            x = lax.psum(x, axis)
            continue
        k = 1
        while k < n:
            x = x + lax.ppermute(x, axis, [(i, i ^ k) for i in range(n)])
            k *= 2
    return x


def tree_collect(red, gat_blk, gat_dom, dom_first=False, halo=None):
    rounds = (("blk", gat_blk), ("dom", gat_dom))
    if dom_first:
        rounds = rounds[::-1]
    for axis, gat in rounds:
        n = lax.axis_size(axis)
        if not _pow2(n):
            red = lax.psum(red, axis)
            buf = lax.all_gather(gat, axis, axis=0)
        else:
            idx = lax.axis_index(axis)
            buf = gat[None]
            k = 1
            while k < n:
                packed = jnp.concatenate([red.reshape(-1), buf.reshape(-1)])
                if halo is not None and axis == "blk" and k == 2:
                    packed, halo = lax.optimization_barrier((packed, halo))
                    halo = neighbours(halo)
                got = lax.ppermute(packed, axis, [(i, i ^ k) for i in range(n)])
                red = red + got[: red.size].reshape(red.shape)
                other = got[red.size :].reshape(buf.shape)
                low = (idx // k) % 2 == 0
                buf = jnp.where(low, jnp.concatenate([buf, other]), jnp.concatenate([other, buf]))
                k *= 2
        if axis == "blk":
            gat_blk = buf
        else:
            gat_dom = buf
    if halo is not None:
        return red, gat_blk, gat_dom, halo
    return red, gat_blk, gat_dom


def neighbours(field):
    count = lax.axis_size("blk")
    ends = count - 1
    left = lax.ppermute(field, "blk", [(i, i + 1) for i in range(ends)])
    right = lax.ppermute(field, "blk", [(i + 1, i) for i in range(ends)])
    return jnp.concatenate([left, field, right], axis=3)


def complex_mix(products):
    return jnp.stack([products[0, 0] - products[1, 1], products[0, 1] + products[1, 0]])


def coefficients(field, source_basis):
    rounded = field.astype(jnp.bfloat16)
    coef_prod = jnp.einsum(
        "akr,pqr->apqk", source_basis[0], rounded[:, :, 0], preferred_element_type=jnp.float32
    )
    return jnp.stack([coef_prod[0, 0] + coef_prod[1, 1], coef_prod[0, 1] - coef_prod[1, 0]])


def near_field(window, near_blocks, near_cols):
    nrhs = window.shape[1]
    blocks_dev = near_blocks.shape[1]
    slots = near_blocks.shape[2]
    width = near_blocks.shape[4]
    rounded = window.astype(jnp.bfloat16).reshape(2, nrhs, 3 * blocks_dev, width)
    chosen = rounded.at[:, :, near_cols[0].reshape(-1)].get(mode="promise_in_bounds").reshape(
        2, nrhs, blocks_dev, slots, width
    )
    near_prod = jnp.einsum(
        "ikarc,pqikc->apqir", near_blocks[0], chosen, preferred_element_type=jnp.float32
    )
    return complex_mix(near_prod).reshape(2, nrhs, 1, blocks_dev * width)


def far_weights(coupling, far_ranks, rank_cap):
    row_coupling = coupling[0, 0]
    row_ranks = far_ranks[0, 0]
    levels = jnp.arange(rank_cap, dtype=jnp.int32)
    limit = row_ranks[:, None, None]
    keep = (levels[None, :, None] < limit) & (levels[None, None, :] < limit)
    return row_coupling * keep[:, None].astype(jnp.float32)


def far_field(gathered, weights, target_basis):
    nrhs = gathered.shape[2]
    rows = target_basis.shape[3]
    inner = jnp.einsum("sakl,spql->apqk", weights, gathered, precision=lax.Precision.HIGH)
    rounded_coef = complex_mix(inner).astype(jnp.bfloat16)
    outward = jnp.einsum(
        "akr,pqk->apqr", target_basis[0], rounded_coef, preferred_element_type=jnp.float32
    )
    return complex_mix(outward).reshape(2, nrhs, 1, rows)


def swapped(every, partner, width):
    nrhs = every.shape[1]
    rows = every.shape[3]
    tiles = every.reshape(2, nrhs, -1, width)
    return tiles.at[:, :, partner[0]].get(mode="promise_in_bounds").reshape(2, nrhs, 1, rows)


def local_products(vectors, image):
    stacked = []
    for basis in vectors:
        real_part = jnp.sum(basis[0] * image[0] + basis[1] * image[1], axis=(1, 2))
        imag_part = jnp.sum(basis[0] * image[1] - basis[1] * image[0], axis=(1, 2))
        stacked.append(jnp.stack([real_part, imag_part]))
    return jnp.stack(stacked)


def local_squares(field):
    return jnp.sum(field[0] * field[0] + field[1] * field[1], axis=(1, 2))


def scaled(factor, field):
    real_f = factor[0][:, None, None]
    imag_f = factor[1][:, None, None]
    return jnp.stack([real_f * field[0] - imag_f * field[1], real_f * field[1] + imag_f * field[0]])


def coef_scaled(factor, coef):
    real_f = factor[0][None, :, None]
    imag_f = factor[1][None, :, None]
    return jnp.stack(
        [real_f * coef[:, 0] - imag_f * coef[:, 1], real_f * coef[:, 1] + imag_f * coef[:, 0]],
        axis=1,
    )


def shards(
    right_side, near_blocks, near_cols, partner, source_basis, target_basis, coupling, far_ranks
):
    rows = right_side.shape[3]
    width = near_blocks.shape[4]
    total = float(rows * lax.axis_size("dom") * lax.axis_size("blk"))
    everyone = ("dom", "blk")
    weights = far_weights(coupling, far_ranks, source_basis.shape[2])

    def spread(every):
        return jnp.moveaxis(every, 0, 2)

    start_sum, coef_rhs, every_rhs, window_rhs = tree_collect(
        local_squares(right_side),
        coefficients(right_side, source_basis),
        right_side[:, :, 0],
        dom_first=True,
        halo=right_side,
    )
    beta = jnp.sqrt(start_sum / total + EPSILON)
    inv_scale = beta[None, :, None, None]
    first_vec = right_side / inv_scale
    window_one = window_rhs / inv_scale
    every_one = spread(every_rhs) / inv_scale
    coef_one = coef_rhs / beta[None, None, :, None]
    image_one = (
        first_vec
        + near_field(window_one, near_blocks, near_cols)
        + far_field(coef_one, weights, target_basis)
        - swapped(every_one, partner, width)
    )

    window_img = neighbours(image_one)
    parts = jnp.concatenate(
        [
            local_products([first_vec], image_one)[0],
            local_squares(image_one)[None],
            local_squares(first_vec)[None],
        ]
    )
    one, coef_img, every_img = tree_collect(
        parts, coefficients(image_one, source_basis), image_one[:, :, 0]
    )
    one = one / total
    h_one_one = one[0:2]
    sq_w1 = one[2]
    sq_v1 = one[3]
    norm_h11 = h_one_one[0] * h_one_one[0] + h_one_one[1] * h_one_one[1]
    sq_u1 = jnp.maximum(sq_w1 - norm_h11 * (2.0 - sq_v1), 0.0)
    h_two_one = jnp.sqrt(sq_u1 + EPSILON)
    inv_two = h_two_one[None, :, None, None]
    second_basis = (image_one - scaled(h_one_one, first_vec)) / inv_two
    window_two = (window_img - scaled(h_one_one, window_one)) / inv_two
    every_two = (spread(every_img) - scaled(h_one_one, every_one)) / inv_two
    coef_two = (coef_img - coef_scaled(h_one_one, coef_one)) / h_two_one[None, None, :, None]
    image_two = (
        second_basis
        + near_field(window_two, near_blocks, near_cols)
        + far_field(coef_two, weights, target_basis)
        - swapped(every_two, partner, width)
    )

    two = (
        tree_sum(
            jnp.concatenate(
                [
                    local_products([first_vec, second_basis], image_two).reshape(4, -1),
                    local_products([first_vec], second_basis)[0],
                    local_squares(image_two)[None],
                    local_squares(second_basis)[None],
                ]
            ),
            everyone,
        )
        / total
    )
    h_one_two = two[0:2]
    h_two_two = two[2:4]
    cross = two[4:6]
    sq_w2 = two[6]
    sq_v2 = two[7]
    norm_a = h_one_two[0] * h_one_two[0] + h_one_two[1] * h_one_two[1]
    norm_b = h_two_two[0] * h_two_two[0] + h_two_two[1] * h_two_two[1]
    ab_re = h_one_two[0] * h_two_two[0] + h_one_two[1] * h_two_two[1]
    ab_im = h_one_two[0] * h_two_two[1] - h_one_two[1] * h_two_two[0]
    mixed = ab_re * cross[0] - ab_im * cross[1]
    sq_u2 = sq_w2 - norm_a * (2.0 - sq_v1) - norm_b * (2.0 - sq_v2) + 2.0 * mixed
    sq_u2 = jnp.maximum(sq_u2, 0.0)
    rest_two = image_two - scaled(h_one_two, first_vec) - scaled(h_two_two, second_basis)
    h_three_two = jnp.sqrt(sq_u2 + EPSILON)
    third_basis = rest_two / h_three_two[None, :, None, None]
    hessenberg = jnp.stack(
        [
            beta,
            h_one_one[0],
            h_one_one[1],
            h_two_one,
            h_one_two[0],
            h_one_two[1],
            h_two_two[0],
            h_two_two[1],
            h_three_two,
        ],
        axis=1,
    )
    return (second_basis, third_basis, hessenberg)


def solution(mesh):
    return jax.shard_map(
        shards,
        mesh=mesh,
        in_specs=(
            P(None, None, "dom", "blk"),
            P("dom", "blk", None, None, None, None),
            P("dom", "blk", None),
            P("dom", "blk"),
            P("dom", None, None, "blk"),
            P("dom", None, None, "blk"),
            P("dom", "blk", None, None, None, None),
            P("dom", "blk", None),
        ),
        out_specs=(P(None, None, "dom", "blk"), P(None, None, "dom", "blk"), P()),
        check_vma=False,
    )
```

```python
import jax
import jax.numpy as jnp
from jax import lax
from jax.sharding import PartitionSpec as P

EPSILON = 1e-06


def _pow2(n):
    return n > 0 and (n & (n - 1)) == 0


def tree_sum(x, axes):
    for axis in axes:
        n = lax.axis_size(axis)
        if not _pow2(n):
            x = lax.psum(x, axis)
            continue
        k = 1
        while k < n:
            x = x + lax.ppermute(x, axis, [(i, i ^ k) for i in range(n)])
            k *= 2
    return x


def tree_collect(red, gat_blk, gat_dom, dom_first=False, halo=None):
    left = None
    right = None
    rounds = (("blk", gat_blk), ("dom", gat_dom))
    if dom_first:
        rounds = rounds[::-1]
    for axis, gat in rounds:
        n = lax.axis_size(axis)
        if not _pow2(n):
            red = lax.psum(red, axis)
            buf = lax.all_gather(gat, axis, axis=0)
        else:
            idx = lax.axis_index(axis)
            buf = gat[None]
            k = 1
            while k < n:
                packed = jnp.concatenate([red.reshape(-1), buf.reshape(-1)])
                if halo is not None and axis == "blk":
                    if left is not None and k == min(4, n // 2) and k > 2:
                        packed, left = lax.optimization_barrier((packed, left))
                    if right is not None and k == min(8, n // 2) and k > 4:
                        packed, right = lax.optimization_barrier((packed, right))
                    if k == min(2, n // 2) and left is None:
                        packed, tied = lax.optimization_barrier((packed, halo))
                        left = lax.ppermute(tied, "blk", [(i, i + 1) for i in range(n - 1)])
                    if k == min(4, n // 2) and right is None:
                        packed, tied = lax.optimization_barrier((packed, halo))
                        right = lax.ppermute(tied, "blk", [(i + 1, i) for i in range(n - 1)])
                got = lax.ppermute(packed, axis, [(i, i ^ k) for i in range(n)])
                red = red + got[: red.size].reshape(red.shape)
                other = got[red.size :].reshape(buf.shape)
                low = (idx // k) % 2 == 0
                buf = jnp.where(low, jnp.concatenate([buf, other]), jnp.concatenate([other, buf]))
                k *= 2
        if axis == "blk":
            gat_blk = buf
        else:
            gat_dom = buf
    if halo is not None:
        if left is None or right is None:
            return red, gat_blk, gat_dom, neighbours(halo)
        return red, gat_blk, gat_dom, jnp.concatenate([left, halo, right], axis=3)
    return red, gat_blk, gat_dom


def neighbours(field):
    count = lax.axis_size("blk")
    ends = count - 1
    left = lax.ppermute(field, "blk", [(i, i + 1) for i in range(ends)])
    right = lax.ppermute(field, "blk", [(i + 1, i) for i in range(ends)])
    return jnp.concatenate([left, field, right], axis=3)


def complex_mix(products):
    return jnp.stack([products[0, 0] - products[1, 1], products[0, 1] + products[1, 0]])


def coefficients(field, source_basis):
    rounded = field.astype(jnp.bfloat16)
    coef_prod = jnp.einsum(
        "akr,pqr->apqk", source_basis[0], rounded[:, :, 0], preferred_element_type=jnp.float32
    )
    return jnp.stack([coef_prod[0, 0] + coef_prod[1, 1], coef_prod[0, 1] - coef_prod[1, 0]])


def near_field(window, near_blocks, near_cols):
    nrhs = window.shape[1]
    blocks_dev = near_blocks.shape[1]
    slots = near_blocks.shape[2]
    width = near_blocks.shape[4]
    rounded = window.astype(jnp.bfloat16).reshape(2, nrhs, 3 * blocks_dev, width)
    chosen = rounded.at[:, :, near_cols[0].reshape(-1)].get(mode="promise_in_bounds").reshape(
        2, nrhs, blocks_dev, slots, width
    )
    near_prod = jnp.einsum(
        "ikarc,pqikc->apqir", near_blocks[0], chosen, preferred_element_type=jnp.float32
    )
    return complex_mix(near_prod).reshape(2, nrhs, 1, blocks_dev * width)


def far_weights(coupling, far_ranks, rank_cap):
    row_coupling = coupling[0, 0]
    row_ranks = far_ranks[0, 0]
    levels = jnp.arange(rank_cap, dtype=jnp.int32)
    limit = row_ranks[:, None, None]
    keep = (levels[None, :, None] < limit) & (levels[None, None, :] < limit)
    return row_coupling * keep[:, None].astype(jnp.float32)


def far_field(gathered, weights, target_basis):
    nrhs = gathered.shape[2]
    rows = target_basis.shape[3]
    inner = jnp.einsum("sakl,spql->apqk", weights, gathered, precision=lax.Precision.HIGH)
    rounded_coef = complex_mix(inner).astype(jnp.bfloat16)
    outward = jnp.einsum(
        "akr,pqk->apqr", target_basis[0], rounded_coef, preferred_element_type=jnp.float32
    )
    return complex_mix(outward).reshape(2, nrhs, 1, rows)


def swapped(every, partner, width):
    nrhs = every.shape[1]
    rows = every.shape[3]
    tiles = every.reshape(2, nrhs, -1, width)
    return tiles.at[:, :, partner[0]].get(mode="promise_in_bounds").reshape(2, nrhs, 1, rows)


def local_products(vectors, image):
    stacked = []
    for basis in vectors:
        real_part = jnp.sum(basis[0] * image[0] + basis[1] * image[1], axis=(1, 2))
        imag_part = jnp.sum(basis[0] * image[1] - basis[1] * image[0], axis=(1, 2))
        stacked.append(jnp.stack([real_part, imag_part]))
    return jnp.stack(stacked)


def local_squares(field):
    return jnp.sum(field[0] * field[0] + field[1] * field[1], axis=(1, 2))


def scaled(factor, field):
    real_f = factor[0][:, None, None]
    imag_f = factor[1][:, None, None]
    return jnp.stack([real_f * field[0] - imag_f * field[1], real_f * field[1] + imag_f * field[0]])


def coef_scaled(factor, coef):
    real_f = factor[0][None, :, None]
    imag_f = factor[1][None, :, None]
    return jnp.stack(
        [real_f * coef[:, 0] - imag_f * coef[:, 1], real_f * coef[:, 1] + imag_f * coef[:, 0]],
        axis=1,
    )


def shards(
    right_side, near_blocks, near_cols, partner, source_basis, target_basis, coupling, far_ranks
):
    rows = right_side.shape[3]
    width = near_blocks.shape[4]
    total = float(rows * lax.axis_size("dom") * lax.axis_size("blk"))
    everyone = ("dom", "blk")
    weights = far_weights(coupling, far_ranks, source_basis.shape[2])

    def spread(every):
        return jnp.moveaxis(every, 0, 2)

    start_sum, coef_rhs, every_rhs, window_rhs = tree_collect(
        local_squares(right_side),
        coefficients(right_side, source_basis),
        right_side[:, :, 0],
        dom_first=True,
        halo=right_side,
    )
    beta = jnp.sqrt(start_sum / total + EPSILON)
    inv_scale = beta[None, :, None, None]
    first_vec = right_side / inv_scale
    window_one = window_rhs / inv_scale
    every_one = spread(every_rhs) / inv_scale
    coef_one = coef_rhs / beta[None, None, :, None]
    image_one = (
        first_vec
        + near_field(window_one, near_blocks, near_cols)
        + far_field(coef_one, weights, target_basis)
        - swapped(every_one, partner, width)
    )

    parts = jnp.concatenate(
        [
            local_products([first_vec], image_one)[0],
            local_squares(image_one)[None],
            local_squares(first_vec)[None],
        ]
    )
    one, coef_img, every_img, window_img = tree_collect(
        parts, coefficients(image_one, source_basis), image_one[:, :, 0], halo=image_one
    )
    one = one / total
    h_one_one = one[0:2]
    sq_w1 = one[2]
    sq_v1 = one[3]
    norm_h11 = h_one_one[0] * h_one_one[0] + h_one_one[1] * h_one_one[1]
    sq_u1 = jnp.maximum(sq_w1 - norm_h11 * (2.0 - sq_v1), 0.0)
    h_two_one = jnp.sqrt(sq_u1 + EPSILON)
    inv_two = h_two_one[None, :, None, None]
    second_basis = (image_one - scaled(h_one_one, first_vec)) / inv_two
    window_two = (window_img - scaled(h_one_one, window_one)) / inv_two
    every_two = (spread(every_img) - scaled(h_one_one, every_one)) / inv_two
    coef_two = (coef_img - coef_scaled(h_one_one, coef_one)) / h_two_one[None, None, :, None]
    image_two = (
        second_basis
        + near_field(window_two, near_blocks, near_cols)
        + far_field(coef_two, weights, target_basis)
        - swapped(every_two, partner, width)
    )

    two = (
        tree_sum(
            jnp.concatenate(
                [
                    local_products([first_vec, second_basis], image_two).reshape(4, -1),
                    local_products([first_vec], second_basis)[0],
                    local_squares(image_two)[None],
                    local_squares(second_basis)[None],
                ]
            ),
            everyone,
        )
        / total
    )
    h_one_two = two[0:2]
    h_two_two = two[2:4]
    cross = two[4:6]
    sq_w2 = two[6]
    sq_v2 = two[7]
    norm_a = h_one_two[0] * h_one_two[0] + h_one_two[1] * h_one_two[1]
    norm_b = h_two_two[0] * h_two_two[0] + h_two_two[1] * h_two_two[1]
    ab_re = h_one_two[0] * h_two_two[0] + h_one_two[1] * h_two_two[1]
    ab_im = h_one_two[0] * h_two_two[1] - h_one_two[1] * h_two_two[0]
    mixed = ab_re * cross[0] - ab_im * cross[1]
    sq_u2 = sq_w2 - norm_a * (2.0 - sq_v1) - norm_b * (2.0 - sq_v2) + 2.0 * mixed
    sq_u2 = jnp.maximum(sq_u2, 0.0)
    rest_two = image_two - scaled(h_one_two, first_vec) - scaled(h_two_two, second_basis)
    h_three_two = jnp.sqrt(sq_u2 + EPSILON)
    third_basis = rest_two / h_three_two[None, :, None, None]
    hessenberg = jnp.stack(
        [
            beta,
            h_one_one[0],
            h_one_one[1],
            h_two_one,
            h_one_two[0],
            h_one_two[1],
            h_two_two[0],
            h_two_two[1],
            h_three_two,
        ],
        axis=1,
    )
    return (second_basis, third_basis, hessenberg)


def solution(mesh):
    return jax.shard_map(
        shards,
        mesh=mesh,
        in_specs=(
            P(None, None, "dom", "blk"),
            P("dom", "blk", None, None, None, None),
            P("dom", "blk", None),
            P("dom", "blk"),
            P("dom", None, None, "blk"),
            P("dom", None, None, "blk"),
            P("dom", "blk", None, None, None, None),
            P("dom", "blk", None),
        ),
        out_specs=(P(None, None, "dom", "blk"), P(None, None, "dom", "blk"), P()),
        check_vma=False,
    )
```

```python
import jax
import jax.numpy as jnp
from jax import lax
from jax.sharding import PartitionSpec as P

EPSILON = 1e-06


def _pow2(n):
    return n > 0 and (n & (n - 1)) == 0


def tree_sum(x, axes):
    for axis in axes:
        n = lax.axis_size(axis)
        if not _pow2(n):
            x = lax.psum(x, axis)
            continue
        k = 1
        while k < n:
            x = x + lax.ppermute(x, axis, [(i, i ^ k) for i in range(n)])
            k *= 2
    return x


def tree_collect(red, gat_blk, gat_dom, dom_first=False, halo=None):
    rounds = (("blk", gat_blk), ("dom", gat_dom))
    if dom_first:
        rounds = rounds[::-1]
    for axis, gat in rounds:
        n = lax.axis_size(axis)
        if not _pow2(n):
            red = lax.psum(red, axis)
            buf = lax.all_gather(gat, axis, axis=0)
        else:
            idx = lax.axis_index(axis)
            buf = gat[None]
            k = 1
            while k < n:
                packed = jnp.concatenate([red.reshape(-1), buf.reshape(-1)])
                if halo is not None and axis == "blk" and k == 2:
                    packed, halo = lax.optimization_barrier((packed, halo))
                    halo = neighbours(halo)
                got = lax.ppermute(packed, axis, [(i, i ^ k) for i in range(n)])
                red = red + got[: red.size].reshape(red.shape)
                other = got[red.size :].reshape(buf.shape)
                low = (idx // k) % 2 == 0
                buf = jnp.where(low, jnp.concatenate([buf, other]), jnp.concatenate([other, buf]))
                k *= 2
        if axis == "blk":
            gat_blk = buf
        else:
            gat_dom = buf
    if halo is not None:
        return red, gat_blk, gat_dom, halo
    return red, gat_blk, gat_dom


def neighbours(field):
    count = lax.axis_size("blk")
    ends = count - 1
    left = lax.ppermute(field, "blk", [(i, i + 1) for i in range(ends)])
    right = lax.ppermute(field, "blk", [(i + 1, i) for i in range(ends)])
    return jnp.concatenate([left, field, right], axis=3)


def complex_mix(products):
    return jnp.stack([products[0, 0] - products[1, 1], products[0, 1] + products[1, 0]])


def coefficients(field, source_basis):
    rounded = field.astype(jnp.bfloat16)
    coef_prod = jnp.einsum(
        "akr,pqr->apqk", source_basis[0], rounded[:, :, 0], preferred_element_type=jnp.float32
    )
    return jnp.stack([coef_prod[0, 0] + coef_prod[1, 1], coef_prod[0, 1] - coef_prod[1, 0]])


def near_field(window, near_blocks, near_cols):
    nrhs = window.shape[1]
    blocks_dev = near_blocks.shape[1]
    slots = near_blocks.shape[2]
    width = near_blocks.shape[4]
    rounded = window.astype(jnp.bfloat16).reshape(2, nrhs, 3 * blocks_dev, width)
    chosen = rounded.at[:, :, near_cols[0].reshape(-1)].get(mode="promise_in_bounds").reshape(
        2, nrhs, blocks_dev, slots, width
    )
    near_prod = jnp.einsum(
        "ikarc,pqikc->apqir", near_blocks[0], chosen, preferred_element_type=jnp.float32
    )
    return complex_mix(near_prod).reshape(2, nrhs, 1, blocks_dev * width)


def far_weights(coupling, far_ranks, rank_cap):
    row_coupling = coupling[0, 0]
    row_ranks = far_ranks[0, 0]
    levels = jnp.arange(rank_cap, dtype=jnp.int32)
    limit = row_ranks[:, None, None]
    keep = (levels[None, :, None] < limit) & (levels[None, None, :] < limit)
    return row_coupling * keep[:, None].astype(jnp.float32)


def far_field(gathered, weights, target_basis):
    nrhs = gathered.shape[2]
    rows = target_basis.shape[3]
    inner = jnp.einsum("sakl,spql->apqk", weights, gathered, precision=lax.Precision.HIGH)
    rounded_coef = complex_mix(inner).astype(jnp.bfloat16)
    outward = jnp.einsum(
        "akr,pqk->apqr", target_basis[0], rounded_coef, preferred_element_type=jnp.float32
    )
    return complex_mix(outward).reshape(2, nrhs, 1, rows)


def swapped(every, partner, width):
    nrhs = every.shape[1]
    rows = every.shape[3]
    tiles = every.reshape(2, nrhs, -1, width)
    return tiles.at[:, :, partner[0]].get(mode="promise_in_bounds").reshape(2, nrhs, 1, rows)


def local_products(vectors, image):
    stacked = []
    for basis in vectors:
        real_part = jnp.sum(basis[0] * image[0] + basis[1] * image[1], axis=(1, 2))
        imag_part = jnp.sum(basis[0] * image[1] - basis[1] * image[0], axis=(1, 2))
        stacked.append(jnp.stack([real_part, imag_part]))
    return jnp.stack(stacked)


def local_squares(field):
    return jnp.sum(field[0] * field[0] + field[1] * field[1], axis=(1, 2))


def scaled(factor, field):
    real_f = factor[0][:, None, None]
    imag_f = factor[1][:, None, None]
    return jnp.stack([real_f * field[0] - imag_f * field[1], real_f * field[1] + imag_f * field[0]])


def coef_scaled(factor, coef):
    real_f = factor[0][None, :, None]
    imag_f = factor[1][None, :, None]
    return jnp.stack(
        [real_f * coef[:, 0] - imag_f * coef[:, 1], real_f * coef[:, 1] + imag_f * coef[:, 0]],
        axis=1,
    )


def shards(
    right_side, near_blocks, near_cols, partner, source_basis, target_basis, coupling, far_ranks
):
    rows = right_side.shape[3]
    width = near_blocks.shape[4]
    total = float(rows * lax.axis_size("dom") * lax.axis_size("blk"))
    everyone = ("dom", "blk")
    weights = far_weights(coupling, far_ranks, source_basis.shape[2])

    def spread(every):
        return jnp.moveaxis(every, 0, 2)

    start_sum, coef_rhs, every_rhs, window_rhs = tree_collect(
        local_squares(right_side),
        coefficients(right_side, source_basis),
        right_side[:, :, 0],
        dom_first=True,
        halo=right_side,
    )
    beta = jnp.sqrt(start_sum / total + EPSILON)
    inv_scale = beta[None, :, None, None]
    first_vec = right_side / inv_scale
    window_one = window_rhs / inv_scale
    every_one = spread(every_rhs) / inv_scale
    coef_one = coef_rhs / beta[None, None, :, None]
    image_one = (
        first_vec
        + near_field(window_one, near_blocks, near_cols)
        + far_field(coef_one, weights, target_basis)
        - swapped(every_one, partner, width)
    )

    window_img = neighbours(image_one)
    parts = jnp.concatenate(
        [
            local_products([first_vec], image_one)[0],
            local_squares(image_one)[None],
            local_squares(first_vec)[None],
        ]
    )
    one, coef_img, every_img = tree_collect(
        parts, coefficients(image_one, source_basis), image_one[:, :, 0]
    )
    one = one / total
    h_one_one = one[0:2]
    sq_w1 = one[2]
    sq_v1 = one[3]
    norm_h11 = h_one_one[0] * h_one_one[0] + h_one_one[1] * h_one_one[1]
    sq_u1 = jnp.maximum(sq_w1 - norm_h11 * (2.0 - sq_v1), 0.0)
    h_two_one = jnp.sqrt(sq_u1 + EPSILON)
    inv_two = h_two_one[None, :, None, None]
    second_basis = (image_one - scaled(h_one_one, first_vec)) / inv_two
    window_two = (window_img - scaled(h_one_one, window_one)) / inv_two
    every_two = (spread(every_img) - scaled(h_one_one, every_one)) / inv_two
    coef_two = (coef_img - coef_scaled(h_one_one, coef_one)) / h_two_one[None, None, :, None]
    early_columns = jnp.stack([beta, h_one_one[0], h_one_one[1], h_two_one], axis=1)
    image_two = (
        second_basis
        + near_field(window_two, near_blocks, near_cols)
        + far_field(coef_two, weights, target_basis)
        - swapped(every_two, partner, width)
    )

    two = (
        tree_sum(
            jnp.concatenate(
                [
                    local_products([first_vec, second_basis], image_two).reshape(4, -1),
                    local_products([first_vec], second_basis)[0],
                    local_squares(image_two)[None],
                    local_squares(second_basis)[None],
                ]
            ),
            everyone,
        )
        / total
    )
    h_one_two = two[0:2]
    h_two_two = two[2:4]
    cross = two[4:6]
    sq_w2 = two[6]
    sq_v2 = two[7]
    norm_a = h_one_two[0] * h_one_two[0] + h_one_two[1] * h_one_two[1]
    norm_b = h_two_two[0] * h_two_two[0] + h_two_two[1] * h_two_two[1]
    ab_re = h_one_two[0] * h_two_two[0] + h_one_two[1] * h_two_two[1]
    ab_im = h_one_two[0] * h_two_two[1] - h_one_two[1] * h_two_two[0]
    mixed = ab_re * cross[0] - ab_im * cross[1]
    sq_u2 = sq_w2 - norm_a * (2.0 - sq_v1) - norm_b * (2.0 - sq_v2) + 2.0 * mixed
    sq_u2 = jnp.maximum(sq_u2, 0.0)
    rest_two = image_two - scaled(h_one_two, first_vec) - scaled(h_two_two, second_basis)
    h_three_two = jnp.sqrt(sq_u2 + EPSILON)
    third_basis = rest_two / h_three_two[None, :, None, None]
    hessenberg = jnp.concatenate(
        [early_columns, two[0:4].T, h_three_two[:, None]], axis=1
    )
    return (second_basis, third_basis, hessenberg)


def solution(mesh):
    return jax.shard_map(
        shards,
        mesh=mesh,
        in_specs=(
            P(None, None, "dom", "blk"),
            P("dom", "blk", None, None, None, None),
            P("dom", "blk", None),
            P("dom", "blk"),
            P("dom", None, None, "blk"),
            P("dom", None, None, "blk"),
            P("dom", "blk", None, None, None, None),
            P("dom", "blk", None),
        ),
        out_specs=(P(None, None, "dom", "blk"), P(None, None, "dom", "blk"), P()),
        check_vma=False,
    )
```

```python
import jax
import jax.numpy as jnp
from jax import lax
from jax.sharding import PartitionSpec as P

EPSILON = 1e-06


def _pow2(n):
    return n > 0 and (n & (n - 1)) == 0


def tree_sum(x, axes):
    for axis in axes:
        n = lax.axis_size(axis)
        if not _pow2(n):
            x = lax.psum(x, axis)
            continue
        k = 1
        while k < n:
            x = x + lax.ppermute(x, axis, [(i, i ^ k) for i in range(n)])
            k *= 2
    return x


def tree_collect(red, gat_blk, gat_dom, dom_first=False, halo=None):
    rounds = (("blk", gat_blk), ("dom", gat_dom))
    if dom_first:
        rounds = rounds[::-1]
    for axis, gat in rounds:
        n = lax.axis_size(axis)
        if not _pow2(n):
            red = lax.psum(red, axis)
            buf = lax.all_gather(gat, axis, axis=0)
        else:
            idx = lax.axis_index(axis)
            buf = gat[None]
            k = 1
            while k < n:
                packed = jnp.concatenate([red.reshape(-1), buf.reshape(-1)])
                if halo is not None and axis == "blk" and k == 2:
                    packed, halo = lax.optimization_barrier((packed, halo))
                    halo = neighbours(halo)
                got = lax.ppermute(packed, axis, [(i, i ^ k) for i in range(n)])
                red = red + got[: red.size].reshape(red.shape)
                other = got[red.size :].reshape(buf.shape)
                low = (idx // k) % 2 == 0
                buf = jnp.where(low, jnp.concatenate([buf, other]), jnp.concatenate([other, buf]))
                k *= 2
        if axis == "blk":
            gat_blk = buf
        else:
            gat_dom = buf
    if halo is not None:
        return red, gat_blk, gat_dom, halo
    return red, gat_blk, gat_dom


def neighbours(field):
    count = lax.axis_size("blk")
    ends = count - 1
    left = lax.ppermute(field, "blk", [(i, i + 1) for i in range(ends)])
    right = lax.ppermute(field, "blk", [(i + 1, i) for i in range(ends)])
    return jnp.concatenate([left, field, right], axis=3)


def complex_mix(products):
    return jnp.stack([products[0, 0] - products[1, 1], products[0, 1] + products[1, 0]])


def coefficients(field, source_basis):
    rounded = field.astype(jnp.bfloat16)
    coef_prod = jnp.einsum(
        "akr,pqr->apqk", source_basis[0], rounded[:, :, 0], preferred_element_type=jnp.float32
    )
    return jnp.stack([coef_prod[0, 0] + coef_prod[1, 1], coef_prod[0, 1] - coef_prod[1, 0]])


def near_tiles(window, near_blocks, near_cols):
    nrhs = window.shape[1]
    blocks_dev = near_blocks.shape[1]
    width = near_blocks.shape[4]
    tiles = window.reshape(2, nrhs, 3 * blocks_dev, width)
    return tiles.at[:, :, near_cols[0].reshape(-1)].get(mode="promise_in_bounds")


def near_field(chosen, near_blocks):
    nrhs = chosen.shape[1]
    blocks_dev = near_blocks.shape[1]
    slots = near_blocks.shape[2]
    width = near_blocks.shape[4]
    rounded = chosen.astype(jnp.bfloat16).reshape(2, nrhs, blocks_dev, slots, width)
    near_prod = jnp.einsum(
        "ikarc,pqikc->apqir", near_blocks[0], rounded, preferred_element_type=jnp.float32
    )
    return complex_mix(near_prod).reshape(2, nrhs, 1, blocks_dev * width)


def far_weights(coupling, far_ranks, rank_cap):
    row_coupling = coupling[0, 0]
    row_ranks = far_ranks[0, 0]
    levels = jnp.arange(rank_cap, dtype=jnp.int32)
    limit = row_ranks[:, None, None]
    keep = (levels[None, :, None] < limit) & (levels[None, None, :] < limit)
    return row_coupling * keep[:, None].astype(jnp.float32)


def far_field(gathered, weights, target_basis):
    nrhs = gathered.shape[2]
    rows = target_basis.shape[3]
    inner = jnp.einsum("sakl,spql->apqk", weights, gathered, precision=lax.Precision.HIGH)
    rounded_coef = complex_mix(inner).astype(jnp.bfloat16)
    outward = jnp.einsum(
        "akr,pqk->apqr", target_basis[0], rounded_coef, preferred_element_type=jnp.float32
    )
    return complex_mix(outward).reshape(2, nrhs, 1, rows)


def swapped(every, partner, width):
    nrhs = every.shape[1]
    tiles = every.reshape(2, nrhs, -1, width)
    return tiles.at[:, :, partner[0]].get(mode="promise_in_bounds")


def local_products(vectors, image):
    stacked = []
    for basis in vectors:
        real_part = jnp.sum(basis[0] * image[0] + basis[1] * image[1], axis=(1, 2))
        imag_part = jnp.sum(basis[0] * image[1] - basis[1] * image[0], axis=(1, 2))
        stacked.append(jnp.stack([real_part, imag_part]))
    return jnp.stack(stacked)


def local_squares(field):
    return jnp.sum(field[0] * field[0] + field[1] * field[1], axis=(1, 2))


def scaled(factor, field):
    real_f = factor[0][:, None, None]
    imag_f = factor[1][:, None, None]
    return jnp.stack([real_f * field[0] - imag_f * field[1], real_f * field[1] + imag_f * field[0]])


def coef_scaled(factor, coef):
    real_f = factor[0][None, :, None]
    imag_f = factor[1][None, :, None]
    return jnp.stack(
        [real_f * coef[:, 0] - imag_f * coef[:, 1], real_f * coef[:, 1] + imag_f * coef[:, 0]],
        axis=1,
    )


def shards(
    right_side, near_blocks, near_cols, partner, source_basis, target_basis, coupling, far_ranks
):
    rows = right_side.shape[3]
    width = near_blocks.shape[4]
    total = float(rows * lax.axis_size("dom") * lax.axis_size("blk"))
    everyone = ("dom", "blk")
    weights = far_weights(coupling, far_ranks, source_basis.shape[2])

    def spread(every):
        return jnp.moveaxis(every, 0, 2)

    start_sum, coef_rhs, every_rhs, window_rhs = tree_collect(
        local_squares(right_side),
        coefficients(right_side, source_basis),
        right_side[:, :, 0],
        dom_first=True,
        halo=right_side,
    )
    beta = jnp.sqrt(start_sum / total + EPSILON)
    inv_scale = beta[None, :, None, None]
    first_vec = right_side / inv_scale
    chosen_one = near_tiles(window_rhs, near_blocks, near_cols) / inv_scale
    mates_one = swapped(spread(every_rhs), partner, width) / inv_scale
    coef_one = coef_rhs / beta[None, None, :, None]
    image_one = (
        first_vec
        + near_field(chosen_one, near_blocks)
        + far_field(coef_one, weights, target_basis)
        - mates_one.reshape(first_vec.shape)
    )

    window_img = neighbours(image_one)
    parts = jnp.concatenate(
        [
            local_products([first_vec], image_one)[0],
            local_squares(image_one)[None],
            local_squares(first_vec)[None],
        ]
    )
    one, coef_img, every_img = tree_collect(
        parts, coefficients(image_one, source_basis), image_one[:, :, 0]
    )
    one = one / total
    h_one_one = one[0:2]
    sq_w1 = one[2]
    sq_v1 = one[3]
    norm_h11 = h_one_one[0] * h_one_one[0] + h_one_one[1] * h_one_one[1]
    sq_u1 = jnp.maximum(sq_w1 - norm_h11 * (2.0 - sq_v1), 0.0)
    h_two_one = jnp.sqrt(sq_u1 + EPSILON)
    inv_two = h_two_one[None, :, None, None]
    second_basis = (image_one - scaled(h_one_one, first_vec)) / inv_two
    chosen_img = near_tiles(window_img, near_blocks, near_cols)
    chosen_two = (chosen_img - scaled(h_one_one, chosen_one)) / inv_two
    mates_img = swapped(spread(every_img), partner, width)
    mates_two = (mates_img - scaled(h_one_one, mates_one)) / inv_two
    coef_two = (coef_img - coef_scaled(h_one_one, coef_one)) / h_two_one[None, None, :, None]
    early_columns = jnp.stack([beta, h_one_one[0], h_one_one[1], h_two_one], axis=1)
    image_two = (
        second_basis
        + near_field(chosen_two, near_blocks)
        + far_field(coef_two, weights, target_basis)
        - mates_two.reshape(second_basis.shape)
    )

    two = (
        tree_sum(
            jnp.concatenate(
                [
                    local_products([first_vec, second_basis], image_two).reshape(4, -1),
                    local_products([first_vec], second_basis)[0],
                    local_squares(image_two)[None],
                    local_squares(second_basis)[None],
                ]
            ),
            everyone,
        )
        / total
    )
    h_one_two = two[0:2]
    h_two_two = two[2:4]
    cross = two[4:6]
    sq_w2 = two[6]
    sq_v2 = two[7]
    norm_a = h_one_two[0] * h_one_two[0] + h_one_two[1] * h_one_two[1]
    norm_b = h_two_two[0] * h_two_two[0] + h_two_two[1] * h_two_two[1]
    ab_re = h_one_two[0] * h_two_two[0] + h_one_two[1] * h_two_two[1]
    ab_im = h_one_two[0] * h_two_two[1] - h_one_two[1] * h_two_two[0]
    mixed = ab_re * cross[0] - ab_im * cross[1]
    sq_u2 = sq_w2 - norm_a * (2.0 - sq_v1) - norm_b * (2.0 - sq_v2) + 2.0 * mixed
    sq_u2 = jnp.maximum(sq_u2, 0.0)
    rest_two = image_two - scaled(h_one_two, first_vec) - scaled(h_two_two, second_basis)
    h_three_two = jnp.sqrt(sq_u2 + EPSILON)
    third_basis = rest_two / h_three_two[None, :, None, None]
    hessenberg = jnp.concatenate(
        [early_columns, two[0:4].T, h_three_two[:, None]], axis=1
    )
    return (second_basis, third_basis, hessenberg)


def solution(mesh):
    return jax.shard_map(
        shards,
        mesh=mesh,
        in_specs=(
            P(None, None, "dom", "blk"),
            P("dom", "blk", None, None, None, None),
            P("dom", "blk", None),
            P("dom", "blk"),
            P("dom", None, None, "blk"),
            P("dom", None, None, "blk"),
            P("dom", "blk", None, None, None, None),
            P("dom", "blk", None),
        ),
        out_specs=(P(None, None, "dom", "blk"), P(None, None, "dom", "blk"), P()),
        check_vma=False,
    )
```

```python
import jax
import jax.numpy as jnp
from jax import lax
from jax.sharding import PartitionSpec as P

EPSILON = 1e-06


def _pow2(n):
    return n > 0 and (n & (n - 1)) == 0


def tree_sum(x, axes):
    for axis in axes:
        n = lax.axis_size(axis)
        if not _pow2(n):
            x = lax.psum(x, axis)
            continue
        k = 1
        while k < n:
            x = x + lax.ppermute(x, axis, [(i, i ^ k) for i in range(n)])
            k *= 2
    return x


def tree_collect(red, gat_blk, gat_dom, dom_first=False, halo=None):
    rounds = (("blk", gat_blk), ("dom", gat_dom))
    if dom_first:
        rounds = rounds[::-1]
    for axis, gat in rounds:
        n = lax.axis_size(axis)
        if not _pow2(n):
            red = lax.psum(red, axis)
            buf = lax.all_gather(gat, axis, axis=0)
        else:
            idx = lax.axis_index(axis)
            buf = gat[None]
            k = 1
            while k < n:
                packed = jnp.concatenate([red.reshape(-1), buf.reshape(-1)])
                if halo is not None and axis == "blk" and k == 2:
                    packed, halo = lax.optimization_barrier((packed, halo))
                    halo = neighbours(halo)
                got = lax.ppermute(packed, axis, [(i, i ^ k) for i in range(n)])
                red = red + got[: red.size].reshape(red.shape)
                other = got[red.size :].reshape(buf.shape)
                low = (idx // k) % 2 == 0
                buf = jnp.where(low, jnp.concatenate([buf, other]), jnp.concatenate([other, buf]))
                k *= 2
        if axis == "blk":
            gat_blk = buf
        else:
            gat_dom = buf
    if halo is not None:
        return red, gat_blk, gat_dom, halo
    return red, gat_blk, gat_dom


def neighbours(field):
    count = lax.axis_size("blk")
    ends = count - 1
    left = lax.ppermute(field, "blk", [(i, i + 1) for i in range(ends)])
    right = lax.ppermute(field, "blk", [(i + 1, i) for i in range(ends)])
    return jnp.concatenate([left, field, right], axis=3)


def complex_mix(products):
    return jnp.stack([products[0, 0] - products[1, 1], products[0, 1] + products[1, 0]])


def coefficients(field, source_basis):
    rounded = field.astype(jnp.bfloat16)
    coef_prod = jnp.einsum(
        "akr,pqr->apqk", source_basis[0], rounded[:, :, 0], preferred_element_type=jnp.float32
    )
    return jnp.stack([coef_prod[0, 0] + coef_prod[1, 1], coef_prod[0, 1] - coef_prod[1, 0]])


def near_tiles(window, near_blocks, near_cols):
    nrhs = window.shape[1]
    blocks_dev = near_blocks.shape[1]
    width = near_blocks.shape[4]
    tiles = window.reshape(2, nrhs, 3 * blocks_dev, width)
    return tiles.at[:, :, near_cols[0].reshape(-1)].get(mode="promise_in_bounds")


def near_field(chosen, near_blocks):
    nrhs = chosen.shape[1]
    blocks_dev = near_blocks.shape[1]
    slots = near_blocks.shape[2]
    width = near_blocks.shape[4]
    rounded = chosen.astype(jnp.bfloat16).reshape(2, nrhs, blocks_dev, slots, width)
    near_prod = jnp.einsum(
        "ikarc,pqikc->apqir", near_blocks[0], rounded, preferred_element_type=jnp.float32
    )
    return complex_mix(near_prod).reshape(2, nrhs, 1, blocks_dev * width)


def far_weights(coupling, far_ranks, rank_cap):
    row_coupling = coupling[0, 0]
    row_ranks = far_ranks[0, 0]
    levels = jnp.arange(rank_cap, dtype=jnp.int32)
    limit = row_ranks[:, None, None]
    keep = (levels[None, :, None] < limit) & (levels[None, None, :] < limit)
    return row_coupling * keep[:, None].astype(jnp.float32)


def far_inner(gathered, weights):
    inner = jnp.einsum("sakl,spql->apqk", weights, gathered, precision=lax.Precision.HIGH)
    return complex_mix(inner)


def far_field(far_coef, target_basis):
    nrhs = far_coef.shape[1]
    rows = target_basis.shape[3]
    rounded_coef = far_coef.astype(jnp.bfloat16)
    outward = jnp.einsum(
        "akr,pqk->apqr", target_basis[0], rounded_coef, preferred_element_type=jnp.float32
    )
    return complex_mix(outward).reshape(2, nrhs, 1, rows)


def swapped(every, partner, width):
    nrhs = every.shape[1]
    tiles = every.reshape(2, nrhs, -1, width)
    return tiles.at[:, :, partner[0]].get(mode="promise_in_bounds")


def local_products(vectors, image):
    stacked = []
    for basis in vectors:
        real_part = jnp.sum(basis[0] * image[0] + basis[1] * image[1], axis=(1, 2))
        imag_part = jnp.sum(basis[0] * image[1] - basis[1] * image[0], axis=(1, 2))
        stacked.append(jnp.stack([real_part, imag_part]))
    return jnp.stack(stacked)


def local_squares(field):
    return jnp.sum(field[0] * field[0] + field[1] * field[1], axis=(1, 2))


def scaled(factor, field):
    real_f = factor[0][:, None, None]
    imag_f = factor[1][:, None, None]
    return jnp.stack([real_f * field[0] - imag_f * field[1], real_f * field[1] + imag_f * field[0]])


def coef_scaled(factor, coef):
    real_f = factor[0][None, :, None]
    imag_f = factor[1][None, :, None]
    return jnp.stack(
        [real_f * coef[:, 0] - imag_f * coef[:, 1], real_f * coef[:, 1] + imag_f * coef[:, 0]],
        axis=1,
    )


def shards(
    right_side, near_blocks, near_cols, partner, source_basis, target_basis, coupling, far_ranks
):
    rows = right_side.shape[3]
    width = near_blocks.shape[4]
    total = float(rows * lax.axis_size("dom") * lax.axis_size("blk"))
    everyone = ("dom", "blk")
    weights = far_weights(coupling, far_ranks, source_basis.shape[2])

    def spread(every):
        return jnp.moveaxis(every, 0, 2)

    start_sum, coef_rhs, every_rhs, window_rhs = tree_collect(
        local_squares(right_side),
        coefficients(right_side, source_basis),
        right_side[:, :, 0],
        dom_first=True,
        halo=right_side,
    )
    beta = jnp.sqrt(start_sum / total + EPSILON)
    inv_scale = beta[None, :, None, None]
    first_vec = right_side / inv_scale
    chosen_one = near_tiles(window_rhs, near_blocks, near_cols) / inv_scale
    mates_one = swapped(spread(every_rhs), partner, width) / inv_scale
    coef_one = coef_rhs / beta[None, None, :, None]
    far_one = far_inner(coef_one, weights)
    image_one = (
        first_vec
        + near_field(chosen_one, near_blocks)
        + far_field(far_one, target_basis)
        - mates_one.reshape(first_vec.shape)
    )

    window_img = neighbours(image_one)
    parts = jnp.concatenate(
        [
            local_products([first_vec], image_one)[0],
            local_squares(image_one)[None],
            local_squares(first_vec)[None],
        ]
    )
    one, coef_img, every_img = tree_collect(
        parts, coefficients(image_one, source_basis), image_one[:, :, 0]
    )
    one = one / total
    h_one_one = one[0:2]
    sq_w1 = one[2]
    sq_v1 = one[3]
    norm_h11 = h_one_one[0] * h_one_one[0] + h_one_one[1] * h_one_one[1]
    sq_u1 = jnp.maximum(sq_w1 - norm_h11 * (2.0 - sq_v1), 0.0)
    h_two_one = jnp.sqrt(sq_u1 + EPSILON)
    inv_two = h_two_one[None, :, None, None]
    second_basis = (image_one - scaled(h_one_one, first_vec)) / inv_two
    chosen_img = near_tiles(window_img, near_blocks, near_cols)
    chosen_two = (chosen_img - scaled(h_one_one, chosen_one)) / inv_two
    mates_img = swapped(spread(every_img), partner, width)
    mates_two = (mates_img - scaled(h_one_one, mates_one)) / inv_two
    far_img = far_inner(coef_img, weights)
    far_two = (far_img - scaled(h_one_one, far_one[:, :, None])[:, :, 0]) / h_two_one[None, :, None]
    early_columns = jnp.stack([beta, h_one_one[0], h_one_one[1], h_two_one], axis=1)
    image_two = (
        second_basis
        + near_field(chosen_two, near_blocks)
        + far_field(far_two, target_basis)
        - mates_two.reshape(second_basis.shape)
    )

    two = (
        tree_sum(
            jnp.concatenate(
                [
                    local_products([first_vec, second_basis], image_two).reshape(4, -1),
                    local_products([first_vec], second_basis)[0],
                    local_squares(image_two)[None],
                    local_squares(second_basis)[None],
                ]
            ),
            everyone,
        )
        / total
    )
    h_one_two = two[0:2]
    h_two_two = two[2:4]
    cross = two[4:6]
    sq_w2 = two[6]
    sq_v2 = two[7]
    norm_a = h_one_two[0] * h_one_two[0] + h_one_two[1] * h_one_two[1]
    norm_b = h_two_two[0] * h_two_two[0] + h_two_two[1] * h_two_two[1]
    ab_re = h_one_two[0] * h_two_two[0] + h_one_two[1] * h_two_two[1]
    ab_im = h_one_two[0] * h_two_two[1] - h_one_two[1] * h_two_two[0]
    mixed = ab_re * cross[0] - ab_im * cross[1]
    sq_u2 = sq_w2 - norm_a * (2.0 - sq_v1) - norm_b * (2.0 - sq_v2) + 2.0 * mixed
    sq_u2 = jnp.maximum(sq_u2, 0.0)
    rest_two = image_two - scaled(h_one_two, first_vec) - scaled(h_two_two, second_basis)
    h_three_two = jnp.sqrt(sq_u2 + EPSILON)
    third_basis = rest_two / h_three_two[None, :, None, None]
    hessenberg = jnp.concatenate(
        [early_columns, two[0:4].T, h_three_two[:, None]], axis=1
    )
    return (second_basis, third_basis, hessenberg)


def solution(mesh):
    return jax.shard_map(
        shards,
        mesh=mesh,
        in_specs=(
            P(None, None, "dom", "blk"),
            P("dom", "blk", None, None, None, None),
            P("dom", "blk", None),
            P("dom", "blk"),
            P("dom", None, None, "blk"),
            P("dom", None, None, "blk"),
            P("dom", "blk", None, None, None, None),
            P("dom", "blk", None),
        ),
        out_specs=(P(None, None, "dom", "blk"), P(None, None, "dom", "blk"), P()),
        check_vma=False,
    )
```

```python
import jax
import jax.numpy as jnp
from jax import lax
from jax.sharding import PartitionSpec as P

EPSILON = 1e-06


def _pow2(n):
    return n > 0 and (n & (n - 1)) == 0


def tree_sum(x, axes):
    for axis in axes:
        n = lax.axis_size(axis)
        if not _pow2(n):
            x = lax.psum(x, axis)
            continue
        k = 1
        while k < n:
            x = x + lax.ppermute(x, axis, [(i, i ^ k) for i in range(n)])
            k *= 2
    return x


def tree_collect(red, gat_blk, gat_dom, dom_first=False, halo=None, weights=None):
    rounds = (("blk", gat_blk), ("dom", gat_dom))
    if dom_first:
        rounds = rounds[::-1]
    for axis, gat in rounds:
        n = lax.axis_size(axis)
        if not _pow2(n):
            red = lax.psum(red, axis)
            buf = lax.all_gather(gat, axis, axis=0)
        else:
            idx = lax.axis_index(axis)
            buf = gat[None]
            k = 1
            while k < n:
                packed = jnp.concatenate([red.reshape(-1), buf.reshape(-1)])
                if halo is not None and axis == "blk" and k == 2:
                    packed, halo = lax.optimization_barrier((packed, halo))
                    halo = neighbours(halo)
                got = lax.ppermute(packed, axis, [(i, i ^ k) for i in range(n)])
                red = red + got[: red.size].reshape(red.shape)
                other = got[red.size :].reshape(buf.shape)
                if weights is not None and axis == "blk" and 2 * k == n:
                    base = idx - idx % k
                    mine = lax.dynamic_slice_in_dim(weights, base, k, axis=0)
                    theirs = lax.dynamic_slice_in_dim(weights, base ^ k, k, axis=0)
                    weights = far_inner(buf, mine) + far_inner(other, theirs)
                low = (idx // k) % 2 == 0
                buf = jnp.where(low, jnp.concatenate([buf, other]), jnp.concatenate([other, buf]))
                k *= 2
        if axis == "blk":
            gat_blk = buf
        else:
            gat_dom = buf
    if weights is not None:
        return red, gat_blk, gat_dom, halo, weights
    if halo is not None:
        return red, gat_blk, gat_dom, halo
    return red, gat_blk, gat_dom


def neighbours(field):
    count = lax.axis_size("blk")
    ends = count - 1
    left = lax.ppermute(field, "blk", [(i, i + 1) for i in range(ends)])
    right = lax.ppermute(field, "blk", [(i + 1, i) for i in range(ends)])
    return jnp.concatenate([left, field, right], axis=3)


def complex_mix(products):
    return jnp.stack([products[0, 0] - products[1, 1], products[0, 1] + products[1, 0]])


def coefficients(field, source_basis):
    rounded = field.astype(jnp.bfloat16)
    coef_prod = jnp.einsum(
        "akr,pqr->apqk", source_basis[0], rounded[:, :, 0], preferred_element_type=jnp.float32
    )
    return jnp.stack([coef_prod[0, 0] + coef_prod[1, 1], coef_prod[0, 1] - coef_prod[1, 0]])


def near_tiles(window, near_blocks, near_cols):
    nrhs = window.shape[1]
    blocks_dev = near_blocks.shape[1]
    width = near_blocks.shape[4]
    tiles = window.reshape(2, nrhs, 3 * blocks_dev, width)
    return tiles.at[:, :, near_cols[0].reshape(-1)].get(mode="promise_in_bounds")


def near_field(chosen, near_blocks):
    nrhs = chosen.shape[1]
    blocks_dev = near_blocks.shape[1]
    slots = near_blocks.shape[2]
    width = near_blocks.shape[4]
    rounded = chosen.astype(jnp.bfloat16).reshape(2, nrhs, blocks_dev, slots, width)
    near_prod = jnp.einsum(
        "ikarc,pqikc->apqir", near_blocks[0], rounded, preferred_element_type=jnp.float32
    )
    return complex_mix(near_prod).reshape(2, nrhs, 1, blocks_dev * width)


def far_weights(coupling, far_ranks, rank_cap):
    row_coupling = coupling[0, 0]
    row_ranks = far_ranks[0, 0]
    levels = jnp.arange(rank_cap, dtype=jnp.int32)
    limit = row_ranks[:, None, None]
    keep = (levels[None, :, None] < limit) & (levels[None, None, :] < limit)
    return row_coupling * keep[:, None].astype(jnp.float32)


def far_inner(gathered, weights):
    inner = jnp.einsum("sakl,spql->apqk", weights, gathered, precision=lax.Precision.HIGH)
    return complex_mix(inner)


def far_field(far_coef, target_basis):
    nrhs = far_coef.shape[1]
    rows = target_basis.shape[3]
    rounded_coef = far_coef.astype(jnp.bfloat16)
    outward = jnp.einsum(
        "akr,pqk->apqr", target_basis[0], rounded_coef, preferred_element_type=jnp.float32
    )
    return complex_mix(outward).reshape(2, nrhs, 1, rows)


def swapped(every, partner, width):
    nrhs = every.shape[1]
    tiles = every.reshape(2, nrhs, -1, width)
    return tiles.at[:, :, partner[0]].get(mode="promise_in_bounds")


def local_products(vectors, image):
    stacked = []
    for basis in vectors:
        real_part = jnp.sum(basis[0] * image[0] + basis[1] * image[1], axis=(1, 2))
        imag_part = jnp.sum(basis[0] * image[1] - basis[1] * image[0], axis=(1, 2))
        stacked.append(jnp.stack([real_part, imag_part]))
    return jnp.stack(stacked)


def local_squares(field):
    return jnp.sum(field[0] * field[0] + field[1] * field[1], axis=(1, 2))


def scaled(factor, field):
    real_f = factor[0][:, None, None]
    imag_f = factor[1][:, None, None]
    return jnp.stack([real_f * field[0] - imag_f * field[1], real_f * field[1] + imag_f * field[0]])


def coef_scaled(factor, coef):
    real_f = factor[0][None, :, None]
    imag_f = factor[1][None, :, None]
    return jnp.stack(
        [real_f * coef[:, 0] - imag_f * coef[:, 1], real_f * coef[:, 1] + imag_f * coef[:, 0]],
        axis=1,
    )


def shards(
    right_side, near_blocks, near_cols, partner, source_basis, target_basis, coupling, far_ranks
):
    rows = right_side.shape[3]
    width = near_blocks.shape[4]
    total = float(rows * lax.axis_size("dom") * lax.axis_size("blk"))
    everyone = ("dom", "blk")
    weights = far_weights(coupling, far_ranks, source_basis.shape[2])

    def spread(every):
        return jnp.moveaxis(every, 0, 2)

    start_sum, coef_rhs, every_rhs, window_rhs, far_rhs = tree_collect(
        local_squares(right_side),
        coefficients(right_side, source_basis),
        right_side[:, :, 0],
        dom_first=True,
        halo=right_side,
        weights=weights,
    )
    beta = jnp.sqrt(start_sum / total + EPSILON)
    inv_scale = beta[None, :, None, None]
    first_vec = right_side / inv_scale
    chosen_one = near_tiles(window_rhs, near_blocks, near_cols) / inv_scale
    mates_one = swapped(spread(every_rhs), partner, width) / inv_scale
    coef_one = coef_rhs / beta[None, None, :, None]
    far_one = far_rhs / beta[None, :, None]
    image_one = (
        first_vec
        + near_field(chosen_one, near_blocks)
        + far_field(far_one, target_basis)
        - mates_one.reshape(first_vec.shape)
    )

    window_img = neighbours(image_one)
    parts = jnp.concatenate(
        [
            local_products([first_vec], image_one)[0],
            local_squares(image_one)[None],
            local_squares(first_vec)[None],
        ]
    )
    one, coef_img, every_img = tree_collect(
        parts, coefficients(image_one, source_basis), image_one[:, :, 0]
    )
    one = one / total
    h_one_one = one[0:2]
    sq_w1 = one[2]
    sq_v1 = one[3]
    norm_h11 = h_one_one[0] * h_one_one[0] + h_one_one[1] * h_one_one[1]
    sq_u1 = jnp.maximum(sq_w1 - norm_h11 * (2.0 - sq_v1), 0.0)
    h_two_one = jnp.sqrt(sq_u1 + EPSILON)
    inv_two = h_two_one[None, :, None, None]
    second_basis = (image_one - scaled(h_one_one, first_vec)) / inv_two
    chosen_img = near_tiles(window_img, near_blocks, near_cols)
    chosen_two = (chosen_img - scaled(h_one_one, chosen_one)) / inv_two
    mates_img = swapped(spread(every_img), partner, width)
    mates_two = (mates_img - scaled(h_one_one, mates_one)) / inv_two
    far_img = far_inner(coef_img, weights)
    far_two = (far_img - scaled(h_one_one, far_one[:, :, None])[:, :, 0]) / h_two_one[None, :, None]
    early_columns = jnp.stack([beta, h_one_one[0], h_one_one[1], h_two_one], axis=1)
    image_two = (
        second_basis
        + near_field(chosen_two, near_blocks)
        + far_field(far_two, target_basis)
        - mates_two.reshape(second_basis.shape)
    )

    two = (
        tree_sum(
            jnp.concatenate(
                [
                    local_products([first_vec, second_basis], image_two).reshape(4, -1),
                    local_products([first_vec], second_basis)[0],
                    local_squares(image_two)[None],
                    local_squares(second_basis)[None],
                ]
            ),
            everyone,
        )
        / total
    )
    h_one_two = two[0:2]
    h_two_two = two[2:4]
    cross = two[4:6]
    sq_w2 = two[6]
    sq_v2 = two[7]
    norm_a = h_one_two[0] * h_one_two[0] + h_one_two[1] * h_one_two[1]
    norm_b = h_two_two[0] * h_two_two[0] + h_two_two[1] * h_two_two[1]
    ab_re = h_one_two[0] * h_two_two[0] + h_one_two[1] * h_two_two[1]
    ab_im = h_one_two[0] * h_two_two[1] - h_one_two[1] * h_two_two[0]
    mixed = ab_re * cross[0] - ab_im * cross[1]
    sq_u2 = sq_w2 - norm_a * (2.0 - sq_v1) - norm_b * (2.0 - sq_v2) + 2.0 * mixed
    sq_u2 = jnp.maximum(sq_u2, 0.0)
    rest_two = image_two - scaled(h_one_two, first_vec) - scaled(h_two_two, second_basis)
    h_three_two = jnp.sqrt(sq_u2 + EPSILON)
    third_basis = rest_two / h_three_two[None, :, None, None]
    hessenberg = jnp.concatenate(
        [early_columns, two[0:4].T, h_three_two[:, None]], axis=1
    )
    return (second_basis, third_basis, hessenberg)


def solution(mesh):
    return jax.shard_map(
        shards,
        mesh=mesh,
        in_specs=(
            P(None, None, "dom", "blk"),
            P("dom", "blk", None, None, None, None),
            P("dom", "blk", None),
            P("dom", "blk"),
            P("dom", None, None, "blk"),
            P("dom", None, None, "blk"),
            P("dom", "blk", None, None, None, None),
            P("dom", "blk", None),
        ),
        out_specs=(P(None, None, "dom", "blk"), P(None, None, "dom", "blk"), P()),
        check_vma=False,
    )
```

```python
import jax
import jax.numpy as jnp
from jax import lax
from jax.sharding import PartitionSpec as P

EPSILON = 1e-06


def _pow2(n):
    return n > 0 and (n & (n - 1)) == 0


def tree_sum(x, axes):
    for axis in axes:
        n = lax.axis_size(axis)
        if not _pow2(n):
            x = lax.psum(x, axis)
            continue
        k = 1
        while k < n:
            x = x + lax.ppermute(x, axis, [(i, i ^ k) for i in range(n)])
            k *= 2
    return x


def tree_collect(red, gat_blk, gat_dom, dom_first=False, halo=None):
    rounds = (("blk", gat_blk), ("dom", gat_dom))
    if dom_first:
        rounds = rounds[::-1]
    for axis, gat in rounds:
        n = lax.axis_size(axis)
        if not _pow2(n):
            red = lax.psum(red, axis)
            buf = lax.all_gather(gat, axis, axis=0)
        else:
            idx = lax.axis_index(axis)
            buf = gat[None]
            k = 1
            while k < n:
                packed = jnp.concatenate([red.reshape(-1), buf.reshape(-1)])
                if halo is not None and axis == "blk" and k == 2:
                    packed, halo = lax.optimization_barrier((packed, halo))
                    halo = neighbours(halo)
                got = lax.ppermute(packed, axis, [(i, i ^ k) for i in range(n)])
                red = red + got[: red.size].reshape(red.shape)
                other = got[red.size :].reshape(buf.shape)
                low = (idx // k) % 2 == 0
                buf = jnp.where(low, jnp.concatenate([buf, other]), jnp.concatenate([other, buf]))
                k *= 2
        if axis == "blk":
            gat_blk = buf
        else:
            gat_dom = buf
    if halo is not None:
        return red, gat_blk, gat_dom, halo
    return red, gat_blk, gat_dom


def neighbours(field):
    count = lax.axis_size("blk")
    ends = count - 1
    left = lax.ppermute(field, "blk", [(i, i + 1) for i in range(ends)])
    right = lax.ppermute(field, "blk", [(i + 1, i) for i in range(ends)])
    return jnp.concatenate([left, field, right], axis=3)


def complex_mix(products):
    return jnp.stack([products[0, 0] - products[1, 1], products[0, 1] + products[1, 0]])


def coefficients(field, source_basis):
    rounded = field.astype(jnp.bfloat16)
    coef_prod = jnp.einsum(
        "akr,pqr->apqk", source_basis[0], rounded[:, :, 0], preferred_element_type=jnp.float32
    )
    return jnp.stack([coef_prod[0, 0] + coef_prod[1, 1], coef_prod[0, 1] - coef_prod[1, 0]])


def near_tiles(window, near_blocks, near_cols):
    nrhs = window.shape[1]
    blocks_dev = near_blocks.shape[1]
    width = near_blocks.shape[4]
    tiles = window.reshape(2, nrhs, 3 * blocks_dev, width)
    return tiles.at[:, :, near_cols[0].reshape(-1)].get(mode="promise_in_bounds")


def near_field(chosen, near_blocks):
    nrhs = chosen.shape[1]
    blocks_dev = near_blocks.shape[1]
    slots = near_blocks.shape[2]
    width = near_blocks.shape[4]
    rounded = chosen.astype(jnp.bfloat16).reshape(2, nrhs, blocks_dev, slots, width)
    near_prod = jnp.einsum(
        "ikarc,pqikc->apqir", near_blocks[0], rounded, preferred_element_type=jnp.float32
    )
    return complex_mix(near_prod).reshape(2, nrhs, 1, blocks_dev * width)


def far_weights(coupling, far_ranks, rank_cap):
    row_coupling = coupling[0, 0]
    row_ranks = far_ranks[0, 0]
    levels = jnp.arange(rank_cap, dtype=jnp.int32)
    limit = row_ranks[:, None, None]
    keep = (levels[None, :, None] < limit) & (levels[None, None, :] < limit)
    return row_coupling * keep[:, None].astype(jnp.float32)


def far_inner(gathered, weights):
    inner = jnp.einsum("sakl,spql->apqk", weights, gathered, precision=lax.Precision.HIGH)
    return complex_mix(inner)


def far_field(far_coef, target_basis):
    nrhs = far_coef.shape[1]
    rows = target_basis.shape[3]
    rounded_coef = far_coef.astype(jnp.bfloat16)
    outward = jnp.einsum(
        "akr,pqk->apqr", target_basis[0], rounded_coef, preferred_element_type=jnp.float32
    )
    return complex_mix(outward).reshape(2, nrhs, 1, rows)


def swapped(every, partner, width):
    nrhs = every.shape[1]
    tiles = every.reshape(2, nrhs, -1, width)
    return tiles.at[:, :, partner[0]].get(mode="promise_in_bounds")


def local_products(vectors, image):
    stacked = []
    for basis in vectors:
        real_part = jnp.sum(basis[0] * image[0] + basis[1] * image[1], axis=(1, 2))
        imag_part = jnp.sum(basis[0] * image[1] - basis[1] * image[0], axis=(1, 2))
        stacked.append(jnp.stack([real_part, imag_part]))
    return jnp.stack(stacked)


def local_squares(field):
    return jnp.sum(field[0] * field[0] + field[1] * field[1], axis=(1, 2))


def scaled(factor, field):
    real_f = factor[0][:, None, None]
    imag_f = factor[1][:, None, None]
    return jnp.stack([real_f * field[0] - imag_f * field[1], real_f * field[1] + imag_f * field[0]])


def coef_scaled(factor, coef):
    real_f = factor[0][None, :, None]
    imag_f = factor[1][None, :, None]
    return jnp.stack(
        [real_f * coef[:, 0] - imag_f * coef[:, 1], real_f * coef[:, 1] + imag_f * coef[:, 0]],
        axis=1,
    )


def shards(
    right_side, near_blocks, near_cols, partner, source_basis, target_basis, coupling, far_ranks
):
    rows = right_side.shape[3]
    width = near_blocks.shape[4]
    total = float(rows * lax.axis_size("dom") * lax.axis_size("blk"))
    everyone = ("dom", "blk")
    weights = far_weights(coupling, far_ranks, source_basis.shape[2])

    def spread(every):
        return jnp.moveaxis(every, 0, 2)

    start_sum, coef_rhs, every_rhs, window_rhs = tree_collect(
        local_squares(right_side),
        coefficients(right_side, source_basis),
        right_side[:, :, 0],
        dom_first=True,
        halo=right_side,
    )
    beta = jnp.sqrt(start_sum / total + EPSILON)
    inv_scale = beta[None, :, None, None]
    first_vec = right_side / inv_scale
    chosen_one = near_tiles(window_rhs, near_blocks, near_cols) / inv_scale
    mates_one = swapped(spread(every_rhs), partner, width) / inv_scale
    coef_one = coef_rhs / beta[None, None, :, None]
    far_one = far_inner(coef_one, weights)
    image_one = (
        first_vec
        + near_field(chosen_one, near_blocks)
        + far_field(far_one, target_basis)
        - mates_one.reshape(first_vec.shape)
    )

    parts = jnp.concatenate(
        [
            local_products([first_vec], image_one)[0],
            local_squares(image_one)[None],
            local_squares(first_vec)[None],
        ]
    )
    one, coef_img, every_img, window_img = tree_collect(
        parts, coefficients(image_one, source_basis), image_one[:, :, 0], halo=image_one
    )
    one = one / total
    h_one_one = one[0:2]
    sq_w1 = one[2]
    sq_v1 = one[3]
    norm_h11 = h_one_one[0] * h_one_one[0] + h_one_one[1] * h_one_one[1]
    sq_u1 = jnp.maximum(sq_w1 - norm_h11 * (2.0 - sq_v1), 0.0)
    h_two_one = jnp.sqrt(sq_u1 + EPSILON)
    inv_two = h_two_one[None, :, None, None]
    second_basis = (image_one - scaled(h_one_one, first_vec)) / inv_two
    chosen_img = near_tiles(window_img, near_blocks, near_cols)
    chosen_two = (chosen_img - scaled(h_one_one, chosen_one)) / inv_two
    mates_img = swapped(spread(every_img), partner, width)
    mates_two = (mates_img - scaled(h_one_one, mates_one)) / inv_two
    far_img = far_inner(coef_img, weights)
    far_two = (far_img - scaled(h_one_one, far_one[:, :, None])[:, :, 0]) / h_two_one[None, :, None]
    early_columns = jnp.stack([beta, h_one_one[0], h_one_one[1], h_two_one], axis=1)
    image_two = (
        second_basis
        + near_field(chosen_two, near_blocks)
        + far_field(far_two, target_basis)
        - mates_two.reshape(second_basis.shape)
    )

    two = (
        tree_sum(
            jnp.concatenate(
                [
                    local_products([first_vec, second_basis], image_two).reshape(4, -1),
                    local_products([first_vec], second_basis)[0],
                    local_squares(image_two)[None],
                    local_squares(second_basis)[None],
                ]
            ),
            everyone,
        )
        / total
    )
    h_one_two = two[0:2]
    h_two_two = two[2:4]
    cross = two[4:6]
    sq_w2 = two[6]
    sq_v2 = two[7]
    norm_a = h_one_two[0] * h_one_two[0] + h_one_two[1] * h_one_two[1]
    norm_b = h_two_two[0] * h_two_two[0] + h_two_two[1] * h_two_two[1]
    ab_re = h_one_two[0] * h_two_two[0] + h_one_two[1] * h_two_two[1]
    ab_im = h_one_two[0] * h_two_two[1] - h_one_two[1] * h_two_two[0]
    mixed = ab_re * cross[0] - ab_im * cross[1]
    sq_u2 = sq_w2 - norm_a * (2.0 - sq_v1) - norm_b * (2.0 - sq_v2) + 2.0 * mixed
    sq_u2 = jnp.maximum(sq_u2, 0.0)
    rest_two = image_two - scaled(h_one_two, first_vec) - scaled(h_two_two, second_basis)
    h_three_two = jnp.sqrt(sq_u2 + EPSILON)
    third_basis = rest_two / h_three_two[None, :, None, None]
    hessenberg = jnp.concatenate(
        [early_columns, two[0:4].T, h_three_two[:, None]], axis=1
    )
    return (second_basis, third_basis, hessenberg)


def solution(mesh):
    return jax.shard_map(
        shards,
        mesh=mesh,
        in_specs=(
            P(None, None, "dom", "blk"),
            P("dom", "blk", None, None, None, None),
            P("dom", "blk", None),
            P("dom", "blk"),
            P("dom", None, None, "blk"),
            P("dom", None, None, "blk"),
            P("dom", "blk", None, None, None, None),
            P("dom", "blk", None),
        ),
        out_specs=(P(None, None, "dom", "blk"), P(None, None, "dom", "blk"), P()),
        check_vma=False,
    )
```

```python
import jax
import jax.numpy as jnp
from jax import lax
from jax.sharding import PartitionSpec as P

EPSILON = 1e-06


def _pow2(n):
    return n > 0 and (n & (n - 1)) == 0


def tree_sum(x, axes):
    for axis in axes:
        n = lax.axis_size(axis)
        if not _pow2(n):
            x = lax.psum(x, axis)
            continue
        k = 1
        while k < n:
            x = x + lax.ppermute(x, axis, [(i, i ^ k) for i in range(n)])
            k *= 2
    return x


def tree_collect(red, gat_blk, gat_dom, dom_first=False, halo=None):
    rounds = (("blk", gat_blk), ("dom", gat_dom))
    if dom_first:
        rounds = rounds[::-1]
    for axis, gat in rounds:
        n = lax.axis_size(axis)
        if not _pow2(n):
            red = lax.psum(red, axis)
            buf = lax.all_gather(gat, axis, axis=0)
        else:
            idx = lax.axis_index(axis)
            buf = gat[None]
            k = 1
            while k < n:
                packed = buf.reshape(-1)
                if red is not None:
                    packed = jnp.concatenate([red.reshape(-1), packed])
                if halo is not None and axis == "blk" and k == 2:
                    packed, halo = lax.optimization_barrier((packed, halo))
                    halo = neighbours(halo)
                got = lax.ppermute(packed, axis, [(i, i ^ k) for i in range(n)])
                skip = 0
                if red is not None:
                    red = red + got[: red.size].reshape(red.shape)
                    skip = red.size
                other = got[skip:].reshape(buf.shape)
                low = (idx // k) % 2 == 0
                buf = jnp.where(low, jnp.concatenate([buf, other]), jnp.concatenate([other, buf]))
                k *= 2
        if axis == "blk":
            gat_blk = buf
        else:
            gat_dom = buf
            if red is None:
                squares = jnp.sum(buf[:, 0] * buf[:, 0] + buf[:, 1] * buf[:, 1], axis=-1)
                red = squares[0]
                for d in range(1, squares.shape[0]):
                    red = red + squares[d]
    if halo is not None:
        return red, gat_blk, gat_dom, halo
    return red, gat_blk, gat_dom


def neighbours(field):
    count = lax.axis_size("blk")
    ends = count - 1
    left = lax.ppermute(field, "blk", [(i, i + 1) for i in range(ends)])
    right = lax.ppermute(field, "blk", [(i + 1, i) for i in range(ends)])
    return jnp.concatenate([left, field, right], axis=3)


def complex_mix(products):
    return jnp.stack([products[0, 0] - products[1, 1], products[0, 1] + products[1, 0]])


def coefficients(field, source_basis):
    rounded = field.astype(jnp.bfloat16)
    coef_prod = jnp.einsum(
        "akr,pqr->apqk", source_basis[0], rounded[:, :, 0], preferred_element_type=jnp.float32
    )
    return jnp.stack([coef_prod[0, 0] + coef_prod[1, 1], coef_prod[0, 1] - coef_prod[1, 0]])


def near_tiles(window, near_blocks, near_cols):
    nrhs = window.shape[1]
    blocks_dev = near_blocks.shape[1]
    width = near_blocks.shape[4]
    tiles = window.reshape(2, nrhs, 3 * blocks_dev, width)
    return tiles.at[:, :, near_cols[0].reshape(-1)].get(mode="promise_in_bounds")


def near_field(chosen, near_blocks):
    nrhs = chosen.shape[1]
    blocks_dev = near_blocks.shape[1]
    slots = near_blocks.shape[2]
    width = near_blocks.shape[4]
    rounded = chosen.astype(jnp.bfloat16).reshape(2, nrhs, blocks_dev, slots, width)
    near_prod = jnp.einsum(
        "ikarc,pqikc->apqir", near_blocks[0], rounded, preferred_element_type=jnp.float32
    )
    return complex_mix(near_prod).reshape(2, nrhs, 1, blocks_dev * width)


def far_weights(coupling, far_ranks, rank_cap):
    row_coupling = coupling[0, 0]
    row_ranks = far_ranks[0, 0]
    levels = jnp.arange(rank_cap, dtype=jnp.int32)
    limit = row_ranks[:, None, None]
    keep = (levels[None, :, None] < limit) & (levels[None, None, :] < limit)
    return row_coupling * keep[:, None].astype(jnp.float32)


def far_inner(gathered, weights):
    inner = jnp.einsum("sakl,spql->apqk", weights, gathered, precision=lax.Precision.HIGH)
    return complex_mix(inner)


def far_field(far_coef, target_basis):
    nrhs = far_coef.shape[1]
    rows = target_basis.shape[3]
    rounded_coef = far_coef.astype(jnp.bfloat16)
    outward = jnp.einsum(
        "akr,pqk->apqr", target_basis[0], rounded_coef, preferred_element_type=jnp.float32
    )
    return complex_mix(outward).reshape(2, nrhs, 1, rows)


def swapped(every, partner, width):
    nrhs = every.shape[1]
    tiles = every.reshape(2, nrhs, -1, width)
    return tiles.at[:, :, partner[0]].get(mode="promise_in_bounds")


def local_products(vectors, image):
    stacked = []
    for basis in vectors:
        real_part = jnp.sum(basis[0] * image[0] + basis[1] * image[1], axis=(1, 2))
        imag_part = jnp.sum(basis[0] * image[1] - basis[1] * image[0], axis=(1, 2))
        stacked.append(jnp.stack([real_part, imag_part]))
    return jnp.stack(stacked)


def local_squares(field):
    return jnp.sum(field[0] * field[0] + field[1] * field[1], axis=(1, 2))


def scaled(factor, field):
    real_f = factor[0][:, None, None]
    imag_f = factor[1][:, None, None]
    return jnp.stack([real_f * field[0] - imag_f * field[1], real_f * field[1] + imag_f * field[0]])


def coef_scaled(factor, coef):
    real_f = factor[0][None, :, None]
    imag_f = factor[1][None, :, None]
    return jnp.stack(
        [real_f * coef[:, 0] - imag_f * coef[:, 1], real_f * coef[:, 1] + imag_f * coef[:, 0]],
        axis=1,
    )


def shards(
    right_side, near_blocks, near_cols, partner, source_basis, target_basis, coupling, far_ranks
):
    rows = right_side.shape[3]
    width = near_blocks.shape[4]
    total = float(rows * lax.axis_size("dom") * lax.axis_size("blk"))
    everyone = ("dom", "blk")
    weights = far_weights(coupling, far_ranks, source_basis.shape[2])

    def spread(every):
        return jnp.moveaxis(every, 0, 2)

    start_sum, coef_rhs, every_rhs, window_rhs = tree_collect(
        None,
        coefficients(right_side, source_basis),
        right_side[:, :, 0],
        dom_first=True,
        halo=right_side,
    )
    beta = jnp.sqrt(start_sum / total + EPSILON)
    inv_scale = beta[None, :, None, None]
    first_vec = right_side / inv_scale
    chosen_one = near_tiles(window_rhs, near_blocks, near_cols) / inv_scale
    mates_one = swapped(spread(every_rhs), partner, width) / inv_scale
    coef_one = coef_rhs / beta[None, None, :, None]
    far_one = far_inner(coef_one, weights)
    image_one = (
        first_vec
        + near_field(chosen_one, near_blocks)
        + far_field(far_one, target_basis)
        - mates_one.reshape(first_vec.shape)
    )

    window_img = neighbours(image_one)
    parts = jnp.concatenate(
        [
            local_products([first_vec], image_one)[0],
            local_squares(image_one)[None],
            local_squares(first_vec)[None],
        ]
    )
    one, coef_img, every_img = tree_collect(
        parts, coefficients(image_one, source_basis), image_one[:, :, 0]
    )
    one = one / total
    h_one_one = one[0:2]
    sq_w1 = one[2]
    sq_v1 = one[3]
    norm_h11 = h_one_one[0] * h_one_one[0] + h_one_one[1] * h_one_one[1]
    sq_u1 = jnp.maximum(sq_w1 - norm_h11 * (2.0 - sq_v1), 0.0)
    h_two_one = jnp.sqrt(sq_u1 + EPSILON)
    inv_two = h_two_one[None, :, None, None]
    second_basis = (image_one - scaled(h_one_one, first_vec)) / inv_two
    chosen_img = near_tiles(window_img, near_blocks, near_cols)
    chosen_two = (chosen_img - scaled(h_one_one, chosen_one)) / inv_two
    mates_img = swapped(spread(every_img), partner, width)
    mates_two = (mates_img - scaled(h_one_one, mates_one)) / inv_two
    far_img = far_inner(coef_img, weights)
    far_two = (far_img - scaled(h_one_one, far_one[:, :, None])[:, :, 0]) / h_two_one[None, :, None]
    early_columns = jnp.stack([beta, h_one_one[0], h_one_one[1], h_two_one], axis=1)
    image_two = (
        second_basis
        + near_field(chosen_two, near_blocks)
        + far_field(far_two, target_basis)
        - mates_two.reshape(second_basis.shape)
    )

    two = (
        tree_sum(
            jnp.concatenate(
                [
                    local_products([first_vec, second_basis], image_two).reshape(4, -1),
                    local_products([first_vec], second_basis)[0],
                    local_squares(image_two)[None],
                    local_squares(second_basis)[None],
                ]
            ),
            everyone,
        )
        / total
    )
    h_one_two = two[0:2]
    h_two_two = two[2:4]
    cross = two[4:6]
    sq_w2 = two[6]
    sq_v2 = two[7]
    norm_a = h_one_two[0] * h_one_two[0] + h_one_two[1] * h_one_two[1]
    norm_b = h_two_two[0] * h_two_two[0] + h_two_two[1] * h_two_two[1]
    ab_re = h_one_two[0] * h_two_two[0] + h_one_two[1] * h_two_two[1]
    ab_im = h_one_two[0] * h_two_two[1] - h_one_two[1] * h_two_two[0]
    mixed = ab_re * cross[0] - ab_im * cross[1]
    sq_u2 = sq_w2 - norm_a * (2.0 - sq_v1) - norm_b * (2.0 - sq_v2) + 2.0 * mixed
    sq_u2 = jnp.maximum(sq_u2, 0.0)
    rest_two = image_two - scaled(h_one_two, first_vec) - scaled(h_two_two, second_basis)
    h_three_two = jnp.sqrt(sq_u2 + EPSILON)
    third_basis = rest_two / h_three_two[None, :, None, None]
    hessenberg = jnp.concatenate(
        [early_columns, two[0:4].T, h_three_two[:, None]], axis=1
    )
    return (second_basis, third_basis, hessenberg)


def solution(mesh):
    return jax.shard_map(
        shards,
        mesh=mesh,
        in_specs=(
            P(None, None, "dom", "blk"),
            P("dom", "blk", None, None, None, None),
            P("dom", "blk", None),
            P("dom", "blk"),
            P("dom", None, None, "blk"),
            P("dom", None, None, "blk"),
            P("dom", "blk", None, None, None, None),
            P("dom", "blk", None),
        ),
        out_specs=(P(None, None, "dom", "blk"), P(None, None, "dom", "blk"), P()),
        check_vma=False,
    )
```

```python
import jax
import jax.numpy as jnp
from jax import lax
from jax.sharding import PartitionSpec as P

EPSILON = 1e-06


def _pow2(n):
    return n > 0 and (n & (n - 1)) == 0


def tree_sum(x, axes):
    for axis in axes:
        n = lax.axis_size(axis)
        if not _pow2(n):
            x = lax.psum(x, axis)
            continue
        k = 1
        while k < n:
            x = x + lax.ppermute(x, axis, [(i, i ^ k) for i in range(n)])
            k *= 2
    return x


def tree_collect(red, gat_blk, gat_dom, dom_first=False, halo=None):
    rounds = (("blk", gat_blk), ("dom", gat_dom))
    if dom_first:
        rounds = rounds[::-1]
    for axis, gat in rounds:
        n = lax.axis_size(axis)
        if not _pow2(n):
            red = lax.psum(red, axis)
            buf = lax.all_gather(gat, axis, axis=0)
        else:
            idx = lax.axis_index(axis)
            buf = gat[None]
            k = 1
            while k < n:
                packed = buf.reshape(-1)
                if red is not None:
                    packed = jnp.concatenate([red.reshape(-1), packed])
                if halo is not None and axis == "blk" and k == 2:
                    packed, halo = lax.optimization_barrier((packed, halo))
                    halo = neighbours(halo)
                got = lax.ppermute(packed, axis, [(i, i ^ k) for i in range(n)])
                skip = 0
                if red is not None:
                    red = red + got[: red.size].reshape(red.shape)
                    skip = red.size
                other = got[skip:].reshape(buf.shape)
                low = (idx // k) % 2 == 0
                buf = jnp.where(low, jnp.concatenate([buf, other]), jnp.concatenate([other, buf]))
                k *= 2
        if axis == "blk":
            gat_blk = buf
        else:
            gat_dom = buf
            if red is None:
                squares = jnp.sum(buf[:, 0] * buf[:, 0] + buf[:, 1] * buf[:, 1], axis=-1)
                red = squares[0]
                for d in range(1, squares.shape[0]):
                    red = red + squares[d]
    if halo is not None:
        return red, gat_blk, gat_dom, halo
    return red, gat_blk, gat_dom


def neighbours(field):
    count = lax.axis_size("blk")
    ends = count - 1
    left = lax.ppermute(field, "blk", [(i, i + 1) for i in range(ends)])
    right = lax.ppermute(field, "blk", [(i + 1, i) for i in range(ends)])
    return jnp.concatenate([left, field, right], axis=3)


def complex_mix(products):
    return jnp.stack([products[0, 0] - products[1, 1], products[0, 1] + products[1, 0]])


def coefficients(field, source_basis):
    rounded = field.astype(jnp.bfloat16)
    coef_prod = jnp.einsum(
        "akr,pqr->apqk", source_basis[0], rounded[:, :, 0], preferred_element_type=jnp.float32
    )
    return jnp.stack([coef_prod[0, 0] + coef_prod[1, 1], coef_prod[0, 1] - coef_prod[1, 0]])


def near_tiles(window, near_blocks, near_cols):
    nrhs = window.shape[1]
    blocks_dev = near_blocks.shape[1]
    width = near_blocks.shape[4]
    tiles = window.reshape(2, nrhs, 3 * blocks_dev, width)
    return tiles.at[:, :, near_cols[0].reshape(-1)].get(mode="promise_in_bounds", wrap_negative_indices=False)


def near_field(chosen, near_blocks):
    nrhs = chosen.shape[1]
    blocks_dev = near_blocks.shape[1]
    slots = near_blocks.shape[2]
    width = near_blocks.shape[4]
    rounded = chosen.astype(jnp.bfloat16).reshape(2, nrhs, blocks_dev, slots, width)
    near_prod = jnp.einsum(
        "ikarc,pqikc->apqir", near_blocks[0], rounded, preferred_element_type=jnp.float32
    )
    return complex_mix(near_prod).reshape(2, nrhs, 1, blocks_dev * width)


def far_weights(coupling, far_ranks, rank_cap):
    row_coupling = coupling[0, 0]
    row_ranks = far_ranks[0, 0]
    levels = jnp.arange(rank_cap, dtype=jnp.int32)
    limit = row_ranks[:, None, None]
    keep = (levels[None, :, None] < limit) & (levels[None, None, :] < limit)
    return row_coupling * keep[:, None].astype(jnp.float32)


def far_inner(gathered, weights):
    inner = jnp.einsum("sakl,spql->apqk", weights, gathered, precision=lax.Precision.HIGH)
    return complex_mix(inner)


def far_field(far_coef, target_basis):
    nrhs = far_coef.shape[1]
    rows = target_basis.shape[3]
    rounded_coef = far_coef.astype(jnp.bfloat16)
    outward = jnp.einsum(
        "akr,pqk->apqr", target_basis[0], rounded_coef, preferred_element_type=jnp.float32
    )
    return complex_mix(outward).reshape(2, nrhs, 1, rows)


def swapped(every, partner, width):
    nrhs = every.shape[1]
    tiles = every.reshape(2, nrhs, -1, width)
    return tiles.at[:, :, partner[0]].get(mode="promise_in_bounds", wrap_negative_indices=False)


def local_products(vectors, image):
    stacked = []
    for basis in vectors:
        real_part = jnp.sum(basis[0] * image[0] + basis[1] * image[1], axis=(1, 2))
        imag_part = jnp.sum(basis[0] * image[1] - basis[1] * image[0], axis=(1, 2))
        stacked.append(jnp.stack([real_part, imag_part]))
    return jnp.stack(stacked)


def local_squares(field):
    return jnp.sum(field[0] * field[0] + field[1] * field[1], axis=(1, 2))


def scaled(factor, field):
    real_f = factor[0][:, None, None]
    imag_f = factor[1][:, None, None]
    return jnp.stack([real_f * field[0] - imag_f * field[1], real_f * field[1] + imag_f * field[0]])


def coef_scaled(factor, coef):
    real_f = factor[0][None, :, None]
    imag_f = factor[1][None, :, None]
    return jnp.stack(
        [real_f * coef[:, 0] - imag_f * coef[:, 1], real_f * coef[:, 1] + imag_f * coef[:, 0]],
        axis=1,
    )


def shards(
    right_side, near_blocks, near_cols, partner, source_basis, target_basis, coupling, far_ranks
):
    rows = right_side.shape[3]
    width = near_blocks.shape[4]
    total = float(rows * lax.axis_size("dom") * lax.axis_size("blk"))
    everyone = ("dom", "blk")
    weights = far_weights(coupling, far_ranks, source_basis.shape[2])

    def spread(every):
        return jnp.moveaxis(every, 0, 2)

    start_sum, coef_rhs, every_rhs, window_rhs = tree_collect(
        None,
        coefficients(right_side, source_basis),
        right_side[:, :, 0],
        dom_first=True,
        halo=right_side,
    )
    beta = jnp.sqrt(start_sum / total + EPSILON)
    inv_scale = beta[None, :, None, None]
    first_vec = right_side / inv_scale
    chosen_one = near_tiles(window_rhs, near_blocks, near_cols) / inv_scale
    mates_one = swapped(spread(every_rhs), partner, width) / inv_scale
    coef_one = coef_rhs / beta[None, None, :, None]
    far_one = far_inner(coef_one, weights)
    image_one = (
        first_vec
        + near_field(chosen_one, near_blocks)
        + far_field(far_one, target_basis)
        - mates_one.reshape(first_vec.shape)
    )

    window_img = neighbours(image_one)
    parts = jnp.concatenate(
        [
            local_products([first_vec], image_one)[0],
            local_squares(image_one)[None],
            local_squares(first_vec)[None],
        ]
    )
    one, coef_img, every_img = tree_collect(
        parts, coefficients(image_one, source_basis), image_one[:, :, 0]
    )
    one = one / total
    h_one_one = one[0:2]
    sq_w1 = one[2]
    sq_v1 = one[3]
    norm_h11 = h_one_one[0] * h_one_one[0] + h_one_one[1] * h_one_one[1]
    sq_u1 = jnp.maximum(sq_w1 - norm_h11 * (2.0 - sq_v1), 0.0)
    h_two_one = jnp.sqrt(sq_u1 + EPSILON)
    inv_two = h_two_one[None, :, None, None]
    second_basis = (image_one - scaled(h_one_one, first_vec)) / inv_two
    chosen_img = near_tiles(window_img, near_blocks, near_cols)
    chosen_two = (chosen_img - scaled(h_one_one, chosen_one)) / inv_two
    mates_img = swapped(spread(every_img), partner, width)
    mates_two = (mates_img - scaled(h_one_one, mates_one)) / inv_two
    far_img = far_inner(coef_img, weights)
    far_two = (far_img - scaled(h_one_one, far_one[:, :, None])[:, :, 0]) / h_two_one[None, :, None]
    early_columns = jnp.stack([beta, h_one_one[0], h_one_one[1], h_two_one], axis=1)
    image_two = (
        second_basis
        + near_field(chosen_two, near_blocks)
        + far_field(far_two, target_basis)
        - mates_two.reshape(second_basis.shape)
    )

    two = (
        tree_sum(
            jnp.concatenate(
                [
                    local_products([first_vec, second_basis], image_two).reshape(4, -1),
                    local_products([first_vec], second_basis)[0],
                    local_squares(image_two)[None],
                    local_squares(second_basis)[None],
                ]
            ),
            everyone,
        )
        / total
    )
    h_one_two = two[0:2]
    h_two_two = two[2:4]
    cross = two[4:6]
    sq_w2 = two[6]
    sq_v2 = two[7]
    norm_a = h_one_two[0] * h_one_two[0] + h_one_two[1] * h_one_two[1]
    norm_b = h_two_two[0] * h_two_two[0] + h_two_two[1] * h_two_two[1]
    ab_re = h_one_two[0] * h_two_two[0] + h_one_two[1] * h_two_two[1]
    ab_im = h_one_two[0] * h_two_two[1] - h_one_two[1] * h_two_two[0]
    mixed = ab_re * cross[0] - ab_im * cross[1]
    sq_u2 = sq_w2 - norm_a * (2.0 - sq_v1) - norm_b * (2.0 - sq_v2) + 2.0 * mixed
    sq_u2 = jnp.maximum(sq_u2, 0.0)
    rest_two = image_two - scaled(h_one_two, first_vec) - scaled(h_two_two, second_basis)
    h_three_two = jnp.sqrt(sq_u2 + EPSILON)
    third_basis = rest_two / h_three_two[None, :, None, None]
    hessenberg = jnp.concatenate(
        [early_columns, two[0:4].T, h_three_two[:, None]], axis=1
    )
    return (second_basis, third_basis, hessenberg)


def solution(mesh):
    return jax.shard_map(
        shards,
        mesh=mesh,
        in_specs=(
            P(None, None, "dom", "blk"),
            P("dom", "blk", None, None, None, None),
            P("dom", "blk", None),
            P("dom", "blk"),
            P("dom", None, None, "blk"),
            P("dom", None, None, "blk"),
            P("dom", "blk", None, None, None, None),
            P("dom", "blk", None),
        ),
        out_specs=(P(None, None, "dom", "blk"), P(None, None, "dom", "blk"), P()),
        check_vma=False,
    )
```

```python
import jax
import jax.numpy as jnp
from jax import lax
from jax.sharding import PartitionSpec as P

EPSILON = 1e-06


def _pow2(n):
    return n > 0 and (n & (n - 1)) == 0


def tree_sum(x, axes):
    for axis in axes:
        n = lax.axis_size(axis)
        if not _pow2(n):
            x = lax.psum(x, axis)
            continue
        k = 1
        while k < n:
            x = x + lax.ppermute(x, axis, [(i, i ^ k) for i in range(n)])
            k *= 2
    return x


def radix_sum(x, axis):
    n = lax.axis_size(axis)
    if not _pow2(n):
        return lax.psum(x, axis)
    idx = lax.axis_index(axis)
    k = 1
    while k < n:
        if 4 * k > n:
            x = x + lax.ppermute(x, axis, [(i, i ^ k) for i in range(n)])
            k *= 2
            continue
        got = [x] + [lax.ppermute(x, axis, [(i, i ^ (j * k)) for i in range(n)]) for j in (1, 2, 3)]
        digit = (idx // k) % 4
        total = None
        for m in range(4):
            member = got[0]
            for j in range(1, 4):
                member = jnp.where((digit ^ j) == m, got[j], member)
            total = member if total is None else total + member
        x = total
        k *= 4
    return x


def tree_collect(red, gat_blk, gat_dom, dom_first=False, halo=None):
    rounds = (("blk", gat_blk), ("dom", gat_dom))
    if dom_first:
        rounds = rounds[::-1]
    for axis, gat in rounds:
        n = lax.axis_size(axis)
        if not _pow2(n):
            red = lax.psum(red, axis)
            buf = lax.all_gather(gat, axis, axis=0)
        else:
            idx = lax.axis_index(axis)
            buf = gat[None]
            k = 1
            while k < n:
                packed = buf.reshape(-1)
                if red is not None:
                    packed = jnp.concatenate([red.reshape(-1), packed])
                if halo is not None and axis == "blk" and k == 2:
                    packed, halo = lax.optimization_barrier((packed, halo))
                    halo = neighbours(halo)
                got = lax.ppermute(packed, axis, [(i, i ^ k) for i in range(n)])
                skip = 0
                if red is not None:
                    red = red + got[: red.size].reshape(red.shape)
                    skip = red.size
                other = got[skip:].reshape(buf.shape)
                low = (idx // k) % 2 == 0
                buf = jnp.where(low, jnp.concatenate([buf, other]), jnp.concatenate([other, buf]))
                k *= 2
        if axis == "blk":
            gat_blk = buf
        else:
            gat_dom = buf
            if red is None:
                squares = jnp.sum(buf[:, 0] * buf[:, 0] + buf[:, 1] * buf[:, 1], axis=-1)
                red = squares[0]
                for d in range(1, squares.shape[0]):
                    red = red + squares[d]
    if halo is not None:
        return red, gat_blk, gat_dom, halo
    return red, gat_blk, gat_dom


def neighbours(field):
    count = lax.axis_size("blk")
    ends = count - 1
    left = lax.ppermute(field, "blk", [(i, i + 1) for i in range(ends)])
    right = lax.ppermute(field, "blk", [(i + 1, i) for i in range(ends)])
    return jnp.concatenate([left, field, right], axis=3)


def complex_mix(products):
    return jnp.stack([products[0, 0] - products[1, 1], products[0, 1] + products[1, 0]])


def coefficients(field, source_basis):
    rounded = field.astype(jnp.bfloat16)
    coef_prod = jnp.einsum(
        "akr,pqr->apqk", source_basis[0], rounded[:, :, 0], preferred_element_type=jnp.float32
    )
    return jnp.stack([coef_prod[0, 0] + coef_prod[1, 1], coef_prod[0, 1] - coef_prod[1, 0]])


def near_tiles(window, near_blocks, near_cols):
    nrhs = window.shape[1]
    blocks_dev = near_blocks.shape[1]
    width = near_blocks.shape[4]
    tiles = window.reshape(2, nrhs, 3 * blocks_dev, width)
    return tiles.at[:, :, near_cols[0].reshape(-1)].get(mode="promise_in_bounds", wrap_negative_indices=False)


def near_field(chosen, near_blocks):
    nrhs = chosen.shape[1]
    blocks_dev = near_blocks.shape[1]
    slots = near_blocks.shape[2]
    width = near_blocks.shape[4]
    rounded = chosen.astype(jnp.bfloat16).reshape(2, nrhs, blocks_dev, slots, width)
    near_prod = jnp.einsum(
        "ikarc,pqikc->apqir", near_blocks[0], rounded, preferred_element_type=jnp.float32
    )
    return complex_mix(near_prod).reshape(2, nrhs, 1, blocks_dev * width)


def far_weights(coupling, far_ranks, rank_cap):
    row_coupling = coupling[0, 0]
    row_ranks = far_ranks[0, 0]
    levels = jnp.arange(rank_cap, dtype=jnp.int32)
    limit = row_ranks[:, None, None]
    keep = (levels[None, :, None] < limit) & (levels[None, None, :] < limit)
    return row_coupling * keep[:, None].astype(jnp.float32)


def far_inner(gathered, weights):
    inner = jnp.einsum("sakl,spql->apqk", weights, gathered, precision=lax.Precision.HIGH)
    return complex_mix(inner)


def far_field(far_coef, target_basis):
    nrhs = far_coef.shape[1]
    rows = target_basis.shape[3]
    rounded_coef = far_coef.astype(jnp.bfloat16)
    outward = jnp.einsum(
        "akr,pqk->apqr", target_basis[0], rounded_coef, preferred_element_type=jnp.float32
    )
    return complex_mix(outward).reshape(2, nrhs, 1, rows)


def swapped(every, partner, width):
    nrhs = every.shape[1]
    tiles = every.reshape(2, nrhs, -1, width)
    return tiles.at[:, :, partner[0]].get(mode="promise_in_bounds", wrap_negative_indices=False)


def local_products(vectors, image):
    stacked = []
    for basis in vectors:
        real_part = jnp.sum(basis[0] * image[0] + basis[1] * image[1], axis=(1, 2))
        imag_part = jnp.sum(basis[0] * image[1] - basis[1] * image[0], axis=(1, 2))
        stacked.append(jnp.stack([real_part, imag_part]))
    return jnp.stack(stacked)


def local_squares(field):
    return jnp.sum(field[0] * field[0] + field[1] * field[1], axis=(1, 2))


def scaled(factor, field):
    real_f = factor[0][:, None, None]
    imag_f = factor[1][:, None, None]
    return jnp.stack([real_f * field[0] - imag_f * field[1], real_f * field[1] + imag_f * field[0]])


def coef_scaled(factor, coef):
    real_f = factor[0][None, :, None]
    imag_f = factor[1][None, :, None]
    return jnp.stack(
        [real_f * coef[:, 0] - imag_f * coef[:, 1], real_f * coef[:, 1] + imag_f * coef[:, 0]],
        axis=1,
    )


def shards(
    right_side, near_blocks, near_cols, partner, source_basis, target_basis, coupling, far_ranks
):
    rows = right_side.shape[3]
    width = near_blocks.shape[4]
    total = float(rows * lax.axis_size("dom") * lax.axis_size("blk"))
    everyone = ("dom", "blk")
    weights = far_weights(coupling, far_ranks, source_basis.shape[2])

    def spread(every):
        return jnp.moveaxis(every, 0, 2)

    start_sum, coef_rhs, every_rhs, window_rhs = tree_collect(
        None,
        coefficients(right_side, source_basis),
        right_side[:, :, 0],
        dom_first=True,
        halo=right_side,
    )
    beta = jnp.sqrt(start_sum / total + EPSILON)
    inv_scale = beta[None, :, None, None]
    first_vec = right_side / inv_scale
    chosen_one = near_tiles(window_rhs, near_blocks, near_cols) / inv_scale
    mates_one = swapped(spread(every_rhs), partner, width) / inv_scale
    coef_one = coef_rhs / beta[None, None, :, None]
    far_one = far_inner(coef_one, weights)
    image_one = (
        first_vec
        + near_field(chosen_one, near_blocks)
        + far_field(far_one, target_basis)
        - mates_one.reshape(first_vec.shape)
    )

    window_img = neighbours(image_one)
    parts = jnp.concatenate(
        [
            local_products([first_vec], image_one)[0],
            local_squares(image_one)[None],
            local_squares(first_vec)[None],
        ]
    )
    one, coef_img, every_img = tree_collect(
        parts, coefficients(image_one, source_basis), image_one[:, :, 0]
    )
    one = one / total
    h_one_one = one[0:2]
    sq_w1 = one[2]
    sq_v1 = one[3]
    norm_h11 = h_one_one[0] * h_one_one[0] + h_one_one[1] * h_one_one[1]
    sq_u1 = jnp.maximum(sq_w1 - norm_h11 * (2.0 - sq_v1), 0.0)
    h_two_one = jnp.sqrt(sq_u1 + EPSILON)
    inv_two = h_two_one[None, :, None, None]
    second_basis = (image_one - scaled(h_one_one, first_vec)) / inv_two
    chosen_img = near_tiles(window_img, near_blocks, near_cols)
    chosen_two = (chosen_img - scaled(h_one_one, chosen_one)) / inv_two
    mates_img = swapped(spread(every_img), partner, width)
    mates_two = (mates_img - scaled(h_one_one, mates_one)) / inv_two
    far_img = far_inner(coef_img, weights)
    far_two = (far_img - scaled(h_one_one, far_one[:, :, None])[:, :, 0]) / h_two_one[None, :, None]
    early_columns = jnp.stack([beta, h_one_one[0], h_one_one[1], h_two_one], axis=1)
    image_two = (
        second_basis
        + near_field(chosen_two, near_blocks)
        + far_field(far_two, target_basis)
        - mates_two.reshape(second_basis.shape)
    )

    two = (
        radix_sum(tree_sum(
            jnp.concatenate(
                [
                    local_products([first_vec, second_basis], image_two).reshape(4, -1),
                    local_products([first_vec], second_basis)[0],
                    local_squares(image_two)[None],
                    local_squares(second_basis)[None],
                ]
            ),
            ("dom",),
        ), "blk")
        / total
    )
    h_one_two = two[0:2]
    h_two_two = two[2:4]
    cross = two[4:6]
    sq_w2 = two[6]
    sq_v2 = two[7]
    norm_a = h_one_two[0] * h_one_two[0] + h_one_two[1] * h_one_two[1]
    norm_b = h_two_two[0] * h_two_two[0] + h_two_two[1] * h_two_two[1]
    ab_re = h_one_two[0] * h_two_two[0] + h_one_two[1] * h_two_two[1]
    ab_im = h_one_two[0] * h_two_two[1] - h_one_two[1] * h_two_two[0]
    mixed = ab_re * cross[0] - ab_im * cross[1]
    sq_u2 = sq_w2 - norm_a * (2.0 - sq_v1) - norm_b * (2.0 - sq_v2) + 2.0 * mixed
    sq_u2 = jnp.maximum(sq_u2, 0.0)
    rest_two = image_two - scaled(h_one_two, first_vec) - scaled(h_two_two, second_basis)
    h_three_two = jnp.sqrt(sq_u2 + EPSILON)
    third_basis = rest_two / h_three_two[None, :, None, None]
    hessenberg = jnp.concatenate(
        [early_columns, two[0:4].T, h_three_two[:, None]], axis=1
    )
    return (second_basis, third_basis, hessenberg)


def solution(mesh):
    return jax.shard_map(
        shards,
        mesh=mesh,
        in_specs=(
            P(None, None, "dom", "blk"),
            P("dom", "blk", None, None, None, None),
            P("dom", "blk", None),
            P("dom", "blk"),
            P("dom", None, None, "blk"),
            P("dom", None, None, "blk"),
            P("dom", "blk", None, None, None, None),
            P("dom", "blk", None),
        ),
        out_specs=(P(None, None, "dom", "blk"), P(None, None, "dom", "blk"), P()),
        check_vma=False,
    )
```
